32 devices in a mesh: dp: 4 (over z), ctx: 8 (over y, x, core).
Axes of the slice: x: 2, y: 2, z: 4, core: 2. Of those that a mesh axis runs over, the one named last changes fastest.
Arguments:
- queries: bfloat16 [4, 1024, 1792], P('dp', 'ctx'), may hold values from -40 to 40
- keys: bfloat16 [4, 1024, 256], P('dp', 'ctx'), may hold values from -8 to 8
- values: bfloat16 [4, 1024, 256], P('dp', 'ctx'), may hold values from -6 to 6
- spikes: int32 [4, 1024, 2], P('dp', 'ctx'), may hold values from 0 to 3
- window_lengths: int32 [2], replicated, may hold values from 128 to 256, as said below
- gain: float32 [1792], replicated, may hold values from 0.1 to 1.9
- cotangent: bfloat16 [4, 1024, 1792], P('dp', 'ctx'), may hold values from -6 to 6
Outputs:
- mixed: bfloat16 [4, 1024, 1792], P('dp', 'ctx')
- d_queries: bfloat16 [4, 1024, 1792], P('dp', 'ctx')
- keys_gradient: bfloat16 [4, 1024, 256], P('dp', 'ctx')
- values_gradient: bfloat16 [4, 1024, 256], P('dp', 'ctx')
- d_gain: float32 [1792], replicated
The draws below stay inside these ranges and needn't reach their ends.
Inputs may be any that keep to these rules, and one draw needn't show every extreme that they name: `window_lengths`: in every draw one key-value head has a look-back of exactly 256.
All inputs are finite; a program needn't handle non-finite values.
Results may differ from the reference program's by a relative error of at most 0.012.
The reference program's roundings to bfloat16 on the way count: a program that leaves them out, or rounds other values in their place, can miss the bound.
Values may be sent and summed in bfloat16 or wider, within the bound.
No kernel may reach another device: no remote copies, remote signals or barrier semaphores. Data moves between devices by JAX's collectives and lax.ppermute only.
A program may use at most 64 MiB of HBM per device.

```python
import jax
import jax.numpy as jnp
from jax import lax

QUERY_HEADS = 14
KEY_VALUE_HEADS = 2
HEAD_SIZE = 128
TOK_DEV = 128
WINDOW_REACH = 256
QUERY_PER_KV = 7
SEQUENCE_COUNT = 4
SEQUENCE_TOKENS = 1024


def draw_queries(key, part):
    own_key = jax.random.fold_in(key, 11)
    noise_seed = jax.random.fold_in(own_key, 0)
    layer_output = jnp.clip(jax.random.normal(noise_seed, (SEQUENCE_COUNT, SEQUENCE_TOKENS, KEY_VALUE_HEADS, QUERY_PER_KV, HEAD_SIZE)), -6.0, 6.0)
    return layer_output.reshape(SEQUENCE_COUNT, SEQUENCE_TOKENS, QUERY_HEADS * HEAD_SIZE).astype(jnp.bfloat16)


def draw_keys(key, part):
    noise_seed = jax.random.fold_in(key, 23)
    layer_output = jnp.clip(jax.random.normal(noise_seed, (SEQUENCE_COUNT, SEQUENCE_TOKENS, KEY_VALUE_HEADS, HEAD_SIZE)), -6.0, 6.0)
    return layer_output.reshape(SEQUENCE_COUNT, SEQUENCE_TOKENS, KEY_VALUE_HEADS * HEAD_SIZE).astype(jnp.bfloat16)


def draw_window_lengths(key, part):
    length_seed, widest_seed = jax.random.split(jax.random.fold_in(key, 202))
    length_list = jax.random.randint(length_seed, (KEY_VALUE_HEADS,), WINDOW_REACH // 2, WINDOW_REACH + 1)
    widest_window = jax.random.randint(widest_seed, (), 0, KEY_VALUE_HEADS)
    return jnp.where(jnp.arange(KEY_VALUE_HEADS) == widest_window, WINDOW_REACH, length_list).astype(jnp.int32)


def plant(result, stream_key, least, largest):
    index_at = [jax.random.randint(jax.random.fold_in(stream_key, axis), (), 0, length) for axis, length in enumerate(result.shape)]
    widest = result.shape.index(max(result.shape))
    next_to = index_at[:widest] + [(index_at[widest] + 1) % result.shape[widest]] + index_at[widest + 1:]
    return result.at[tuple(index_at)].set(least).at[tuple(next_to)].set(largest)


def raised(entries, key, source, target, blocks, factor):
    def block_of(dim):
        return (jnp.arange(entries.shape[dim]) // (entries.shape[dim] // blocks)).reshape((-1,) + (1,) * (entries.ndim - 1 - dim))

    near = jax.random.permutation(key, blocks)[block_of(target)]
    far = (block_of(target) + blocks // 2) % blocks
    return jnp.where((block_of(source) == near) | (block_of(source) == far), factor * entries, entries)


def levels(key, extent, pieces, low, high):
    def one(dim, blocks):
        steps = jax.random.uniform(jax.random.fold_in(jax.random.fold_in(key, 6), dim), (blocks,), jnp.float32, low / len(pieces), high / len(pieces))
        return jnp.repeat(jnp.exp(steps), extent[dim] // blocks).reshape((-1,) + (1,) * (len(extent) - dim - 1))

    level = one(*pieces[0])
    for cut in pieces[1:]:
        level = level * one(*cut)
    return level


def normal_values(key, extent, width, most, shards=(), held_as=jnp.bfloat16):
    loudness = levels(key, extent, shards, -0.22, 0.18) if shards else 1.0
    drawn = jax.random.normal(key, extent, jnp.float32) * width * loudness
    return jnp.minimum(jnp.maximum(drawn, -most), most).astype(held_as)


def bell_draw_with(rng, extent, spread, most, pieces, heavy, kind=jnp.bfloat16):
    values = spread * jax.random.normal(rng, extent, jnp.float32)
    if pieces:
        values = values * levels(rng, extent, pieces, -0.22, 0.18)
    return jnp.clip(raised(values, jax.random.fold_in(rng, 3), *heavy), -most, most).astype(kind)


def setup_inputs(seed: int = 0) -> dict:
    seeds = jax.random.split(jax.random.key(seed), 8)
    return {
        "queries": draw_queries(jax.random.fold_in(seeds[7], 71), 0),
        "keys": draw_keys(jax.random.fold_in(seeds[7], 71), 0),
        "values": normal_values(seeds[2], (SEQUENCE_COUNT, SEQUENCE_TOKENS, KEY_VALUE_HEADS * HEAD_SIZE), 1.0, 6.0, ((0, 4), (1, 8))),
        "spikes": plant(jax.random.randint(seeds[3], (SEQUENCE_COUNT, SEQUENCE_TOKENS, KEY_VALUE_HEADS), 0, 4), jax.random.fold_in(seeds[3], 1), 0, 3).astype(jnp.int32),
        "window_lengths": draw_window_lengths(jax.random.fold_in(seeds[7], 71), 0),
        "gain": jnp.clip(1.0 + 0.18 * jax.random.normal(seeds[5], (QUERY_HEADS * HEAD_SIZE,), jnp.float32), 0.1, 1.9),
        "cotangent": bell_draw_with(seeds[6], (SEQUENCE_COUNT, SEQUENCE_TOKENS, QUERY_HEADS * HEAD_SIZE), 1.0, 6.0, ((0, 4), (1, 8)), (1, 2, 8, 2.0)),
    }


epsilon = 1e-05
highest = lax.Precision.HIGHEST

def exact(text, left, right):
    return jnp.einsum(text, left, right, precision=highest)

def to_half(array):
    return lax.optimization_barrier(array.astype(jnp.bfloat16)).astype(jnp.float32)

def reference(queries, keys, values, spikes, window_lengths, gain, cotangent):
    token_rows = TOK_DEV
    block_list = SEQUENCE_TOKENS // token_rows
    reach = (WINDOW_REACH + token_rows - 2) // token_rows
    padding_rows = reach * token_rows
    window_rows = (reach + 1) * token_rows
    scale = HEAD_SIZE ** (-0.5)
    query_blocks = queries.astype(jnp.float32).reshape(SEQUENCE_COUNT, block_list, token_rows, KEY_VALUE_HEADS, QUERY_PER_KV, HEAD_SIZE)
    key_blocks = keys.astype(jnp.float32).reshape(SEQUENCE_COUNT, block_list, token_rows, KEY_VALUE_HEADS, HEAD_SIZE)
    value_blocks = values.astype(jnp.float32).reshape(SEQUENCE_COUNT, block_list, token_rows, KEY_VALUE_HEADS, HEAD_SIZE)
    token_counts = spikes.astype(jnp.float32).reshape(SEQUENCE_COUNT, block_list, token_rows, KEY_VALUE_HEADS, 1)
    spiked = to_half(value_blocks * token_counts)
    local_state = exact('nbrgd,nbrge->nbgde', key_blocks, spiked)
    running = jnp.cumsum(local_state, axis=1)
    prior = to_half(jnp.concatenate([jnp.zeros_like(local_state[:, :1]), running[:, :-1]], axis=1))
    row_idx = jnp.arange(token_rows)
    causal = (row_idx[:, None] >= row_idx[None, :]).astype(jnp.float32)
    lin_scores = to_half(exact('nbrghd,nbsgd->nbghrs', query_blocks, key_blocks) * causal)
    linear = exact('nbghrs,nbsge->nbrghe', lin_scores, spiked) + exact('nbrghd,nbgde->nbrghe', query_blocks, prior)
    root = jnp.sqrt(lax.optimization_barrier(jnp.mean(linear * linear, axis=-1, keepdims=True)) + epsilon)
    normed = linear / root
    head_gains = gain.reshape(KEY_VALUE_HEADS, QUERY_PER_KV, HEAD_SIZE)
    key_sequence = keys.reshape(SEQUENCE_COUNT, SEQUENCE_TOKENS, KEY_VALUE_HEADS, HEAD_SIZE)
    value_sequence = values.reshape(SEQUENCE_COUNT, SEQUENCE_TOKENS, KEY_VALUE_HEADS, HEAD_SIZE)
    keys_padded = jnp.concatenate([jnp.zeros((SEQUENCE_COUNT, padding_rows, KEY_VALUE_HEADS, HEAD_SIZE), keys.dtype), key_sequence], axis=1)
    values_padded = jnp.concatenate([jnp.zeros((SEQUENCE_COUNT, padding_rows, KEY_VALUE_HEADS, HEAD_SIZE), values.dtype), value_sequence], axis=1)
    query_rows = jnp.moveaxis(queries.reshape(SEQUENCE_COUNT, block_list, token_rows, KEY_VALUE_HEADS, QUERY_PER_KV, HEAD_SIZE), 1, 0)
    gradient_rows = jnp.moveaxis(cotangent.reshape(SEQUENCE_COUNT, block_list, token_rows, KEY_VALUE_HEADS, QUERY_PER_KV, HEAD_SIZE), 1, 0)
    key_idx = jnp.arange(window_rows)
    distance_back = row_idx[:, None] + padding_rows - key_idx[None, :]
    in_window = (distance_back[None] >= 0) & (distance_back[None] < window_lengths[:, None, None])

    def window_step(carry, inputs):
        key_accumulator, value_accumulator = carry
        block_index, query_block, grad_block = inputs
        start = block_index * token_rows
        key_window = lax.dynamic_slice_in_dim(keys_padded, start, window_rows, 1).astype(jnp.float32)
        value_window = lax.dynamic_slice_in_dim(values_padded, start, window_rows, 1).astype(jnp.float32)
        key_pos = start + key_idx - padding_rows
        visible = in_window & (key_pos >= 0)[None, None, :]
        query_wide = query_block.astype(jnp.float32)
        grad_wide = grad_block.astype(jnp.float32)
        scores = exact('nrghd,nmgd->nghrm', query_wide, key_window) * scale
        scores = jnp.where(visible[None, :, None], scores, -1e+30)
        top = lax.optimization_barrier(jnp.max(scores, axis=-1, keepdims=True))
        expo = jnp.exp(scores - top)
        probs = expo / lax.optimization_barrier(jnp.sum(expo, axis=-1, keepdims=True))
        probs_half = to_half(probs)
        window_out = exact('nghrm,nmgd->nrghd', probs_half, value_window)
        grad_probs = exact('nrghd,nmgd->nghrm', grad_wide, value_window)
        delta = jnp.transpose(lax.optimization_barrier(jnp.sum(grad_wide * window_out, axis=-1)), (0, 2, 3, 1))
        grad_scores = to_half(probs * (grad_probs - delta[..., None]) * scale)
        query_grad = exact('nghrm,nmgd->nrghd', grad_scores, key_window)
        key_grad = exact('nghrm,nrghd->nmgd', grad_scores, query_wide)
        value_grad = exact('nghrm,nrghd->nmgd', probs_half, grad_wide)
        key_accumulator = lax.dynamic_update_slice_in_dim(key_accumulator, lax.dynamic_slice_in_dim(key_accumulator, start, window_rows, 1) + key_grad, start, 1)
        value_accumulator = lax.dynamic_update_slice_in_dim(value_accumulator, lax.dynamic_slice_in_dim(value_accumulator, start, window_rows, 1) + value_grad, start, 1)
        return ((key_accumulator, value_accumulator), (window_out, query_grad))
    empty_accumulator = jnp.zeros((SEQUENCE_COUNT, SEQUENCE_TOKENS + padding_rows, KEY_VALUE_HEADS, HEAD_SIZE), jnp.float32)
    block_ids = jnp.arange(block_list, dtype=jnp.int32)
    (key_accumulator, value_accumulator), (window_steps, query_steps_grad) = lax.scan(window_step, (empty_accumulator, empty_accumulator), (block_ids, query_rows, gradient_rows))
    window_out = jnp.moveaxis(window_steps, 0, 1)
    window_dq = jnp.moveaxis(query_steps_grad, 0, 1)
    mixed = (head_gains * normed + window_out).astype(jnp.bfloat16).reshape(SEQUENCE_COUNT, SEQUENCE_TOKENS, QUERY_HEADS * HEAD_SIZE)
    gradient_blocks = cotangent.astype(jnp.float32).reshape(SEQUENCE_COUNT, block_list, token_rows, KEY_VALUE_HEADS, QUERY_PER_KV, HEAD_SIZE)
    d_gain = lax.optimization_barrier(jnp.sum(gradient_blocks * normed, axis=(0, 1, 2))).reshape(QUERY_HEADS * HEAD_SIZE) * (SEQUENCE_COUNT * SEQUENCE_TOKENS) ** (-0.5)
    scaled = gradient_blocks * head_gains
    d_linear = to_half((scaled - normed * lax.optimization_barrier(jnp.mean(scaled * normed, axis=-1, keepdims=True))) / root)
    suffix_local = exact('nbrghd,nbrghe->nbgde', query_blocks, d_linear)
    inclusive = jnp.cumsum(suffix_local[:, ::-1], axis=1)[:, ::-1]
    later = to_half(jnp.concatenate([inclusive[:, 1:], jnp.zeros_like(suffix_local[:, :1])], axis=1))
    back_scores = to_half(exact('nbrghe,nbsge->nbghrs', d_linear, spiked) * causal)
    lin_dq = exact('nbrghe,nbgde->nbrghd', d_linear, prior) + exact('nbghrs,nbsgd->nbrghd', back_scores, key_blocks)
    linear_key_gradient = exact('nbghrs,nbrghd->nbsgd', back_scores, query_blocks) + exact('nbsge,nbgde->nbsgd', spiked, later)
    d_spiked = exact('nbghrs,nbrghe->nbsge', lin_scores, d_linear) + exact('nbsgd,nbgde->nbsge', key_blocks, later)
    linear_value_gradient = d_spiked * token_counts
    d_queries = (lin_dq + window_dq).astype(jnp.bfloat16).reshape(SEQUENCE_COUNT, SEQUENCE_TOKENS, QUERY_HEADS * HEAD_SIZE)
    keys_gradient = (linear_key_gradient.reshape(SEQUENCE_COUNT, SEQUENCE_TOKENS, KEY_VALUE_HEADS, HEAD_SIZE) + key_accumulator[:, padding_rows:]).astype(jnp.bfloat16).reshape(SEQUENCE_COUNT, SEQUENCE_TOKENS, KEY_VALUE_HEADS * HEAD_SIZE)
    values_gradient = (linear_value_gradient.reshape(SEQUENCE_COUNT, SEQUENCE_TOKENS, KEY_VALUE_HEADS, HEAD_SIZE) + value_accumulator[:, padding_rows:]).astype(jnp.bfloat16).reshape(SEQUENCE_COUNT, SEQUENCE_TOKENS, KEY_VALUE_HEADS * HEAD_SIZE)
    return (mixed, d_queries, keys_gradient, values_gradient, d_gain)
```

```python
import math

import jax
import jax.numpy as jnp
from jax import lax
from jax.sharding import PartitionSpec as P

QUERY_HEADS = 14
KEY_VALUE_HEADS = 2
HEAD_SIZE = 128
WINDOW_REACH = 256


epsilon = 1e-05


def exclusive_scan(part, axis, reverse):
    count = lax.axis_size(axis)
    running = part
    total = None
    distance = 1
    while distance < count:
        if reverse:
            route = [(i + distance, i) for i in range(count - distance)]
        else:
            route = [(i, i + distance) for i in range(count - distance)]
        got = lax.ppermute(running, axis, route)
        total = got if total is None else total + got
        if distance * 2 < count:
            running = running + got
        distance *= 2
    if total is None:
        total = jnp.zeros_like(part)
    return total


def all_sum(part, axes):
    count = 1
    for axis in axes:
        count *= lax.axis_size(axis)
    step = 1
    while step < count:
        route = [(i, i ^ step) for i in range(count)]
        part = part + lax.ppermute(part, axes, route)
        step *= 2
    return part


def shifted(block, axis, distance):
    devices = range(lax.axis_size(axis))
    route = [(i - distance, i) for i in devices if i - distance in devices]
    return lax.ppermute(block, axis, route)


def per_device(queries, keys, values, spikes, window_lengths, gain, cotangent):
    batch_inputs = queries.shape[0]
    token_rows = queries.shape[1]
    group_size = QUERY_HEADS // KEY_VALUE_HEADS
    reach = (WINDOW_REACH + token_rows - 2) // token_rows
    padding_rows = reach * token_rows
    window_rows = (reach + 1) * token_rows
    scale = HEAD_SIZE ** (-0.5)
    key_value_width = KEY_VALUE_HEADS * HEAD_SIZE
    query_heads = queries.reshape(batch_inputs, token_rows, KEY_VALUE_HEADS, group_size, HEAD_SIZE)
    key_heads = keys.reshape(batch_inputs, token_rows, KEY_VALUE_HEADS, HEAD_SIZE)
    value_heads = values.reshape(batch_inputs, token_rows, KEY_VALUE_HEADS, HEAD_SIZE)
    token_counts = spikes.astype(jnp.float32)[..., None]
    spiked = (value_heads.astype(jnp.float32) * token_counts).astype(jnp.bfloat16)
    local_state = jnp.einsum(
        "nrgd,nrge->ngde", key_heads, spiked, preferred_element_type=jnp.float32
    )
    prior = exclusive_scan(local_state, "ctx", False)
    prior_half = prior.astype(jnp.bfloat16)
    packed = jnp.concatenate([keys, values], axis=2)
    earlier = []
    for distance in range(reach, 0, -1):
        earlier.append(shifted(packed, "ctx", distance))
    window_packed = jnp.concatenate(earlier + [packed], axis=1)
    key_window = window_packed[:, :, :key_value_width].reshape(
        batch_inputs, window_rows, KEY_VALUE_HEADS, HEAD_SIZE
    )
    value_window = window_packed[:, :, key_value_width:].reshape(
        batch_inputs, window_rows, KEY_VALUE_HEADS, HEAD_SIZE
    )
    row_idx = jnp.arange(token_rows)
    causal = (row_idx[:, None] >= row_idx[None, :]).astype(jnp.float32)
    key_idx = jnp.arange(window_rows)
    distance_back = row_idx[:, None] + padding_rows - key_idx[None, :]
    key_pos = lax.axis_index("ctx") * token_rows + key_idx - padding_rows
    visible = (
        (distance_back[None] >= 0)
        & (distance_back[None] < window_lengths[:, None, None])
        & (key_pos >= 0)[None, None, :]
    )
    lin_half = (
        jnp.einsum("nrghd,nsgd->nghrs", query_heads, key_heads, preferred_element_type=jnp.float32)
        * causal
    ).astype(jnp.bfloat16)
    linear = jnp.einsum("nghrs,nsge->nrghe", lin_half, spiked, preferred_element_type=jnp.float32)
    linear = linear + jnp.einsum(
        "nrghd,ngde->nrghe", query_heads, prior_half, preferred_element_type=jnp.float32
    )
    root = jnp.sqrt(jnp.mean(linear * linear, axis=-1, keepdims=True) + epsilon)
    normed = linear / root
    head_gains = gain.reshape(KEY_VALUE_HEADS, group_size, HEAD_SIZE)
    scores = (
        jnp.einsum("nrghd,nmgd->nghrm", query_heads, key_window, preferred_element_type=jnp.float32)
        * scale
    )
    scores = jnp.where(visible[None, :, None], scores, -1e30)
    top = jnp.max(scores, axis=-1, keepdims=True)
    expo = jnp.exp(scores - top)
    probs = expo / jnp.sum(expo, axis=-1, keepdims=True)
    probs_half = probs.astype(jnp.bfloat16)
    window_out = jnp.einsum(
        "nghrm,nmgd->nrghd", probs_half, value_window, preferred_element_type=jnp.float32
    )
    mixed = (
        (head_gains * normed + window_out)
        .astype(jnp.bfloat16)
        .reshape(batch_inputs, token_rows, QUERY_HEADS * HEAD_SIZE)
    )
    head_gradients = cotangent.reshape(
        batch_inputs, token_rows, KEY_VALUE_HEADS, group_size, HEAD_SIZE
    )
    grad_wide = head_gradients.astype(jnp.float32)
    total_tokens = batch_inputs * lax.axis_size("dp") * token_rows * lax.axis_size("ctx")
    gain_local = jnp.sum(grad_wide * normed, axis=(0, 1)).reshape(QUERY_HEADS * HEAD_SIZE)
    d_gain = all_sum(gain_local, ("dp", "ctx")) * (total_tokens ** (-0.5))
    scaled = grad_wide * head_gains
    d_linear = (
        (scaled - normed * jnp.mean(scaled * normed, axis=-1, keepdims=True)) / root
    ).astype(jnp.bfloat16)
    suffix_local = jnp.einsum(
        "nrghd,nrghe->ngde", query_heads, d_linear, preferred_element_type=jnp.float32
    )
    later = exclusive_scan(suffix_local, "ctx", True)
    later_half = later.astype(jnp.bfloat16)
    back_half = (
        jnp.einsum("nrghe,nsge->nghrs", d_linear, spiked, preferred_element_type=jnp.float32)
        * causal
    ).astype(jnp.bfloat16)
    lin_dq = jnp.einsum(
        "nrghe,ngde->nrghd", d_linear, prior_half, preferred_element_type=jnp.float32
    )
    lin_dq = lin_dq + jnp.einsum(
        "nghrs,nsgd->nrghd", back_half, key_heads, preferred_element_type=jnp.float32
    )
    linear_key_gradient = jnp.einsum(
        "nghrs,nrghd->nsgd", back_half, query_heads, preferred_element_type=jnp.float32
    )
    linear_key_gradient = linear_key_gradient + jnp.einsum(
        "nsge,ngde->nsgd", spiked, later_half, preferred_element_type=jnp.float32
    )
    d_spiked = jnp.einsum(
        "nghrs,nrghe->nsge", lin_half, d_linear, preferred_element_type=jnp.float32
    )
    d_spiked = d_spiked + jnp.einsum(
        "nsgd,ngde->nsge", key_heads, later_half, preferred_element_type=jnp.float32
    )
    linear_value_gradient = d_spiked * token_counts
    grad_probs = jnp.einsum(
        "nrghd,nmgd->nghrm", head_gradients, value_window, preferred_element_type=jnp.float32
    )
    delta = jnp.transpose(jnp.sum(grad_wide * window_out, axis=-1), (0, 2, 3, 1))
    grad_scores = (probs * (grad_probs - delta[..., None]) * scale).astype(jnp.bfloat16)
    window_dq = jnp.einsum(
        "nghrm,nmgd->nrghd", grad_scores, key_window, preferred_element_type=jnp.float32
    )
    key_grad_window = jnp.einsum(
        "nghrm,nrghd->nmgd", grad_scores, query_heads, preferred_element_type=jnp.float32
    ).reshape(batch_inputs, window_rows, key_value_width)
    value_grad_window = jnp.einsum(
        "nghrm,nrghd->nmgd", probs_half, head_gradients, preferred_element_type=jnp.float32
    ).reshape(batch_inputs, window_rows, key_value_width)
    received_k = jnp.zeros((batch_inputs, token_rows, key_value_width), jnp.float32)
    received_v = jnp.zeros((batch_inputs, token_rows, key_value_width), jnp.float32)
    for distance in range(1, reach + 1):
        start_row = (reach - distance) * token_rows
        sent = jnp.concatenate(
            [
                key_grad_window[:, start_row : start_row + token_rows],
                value_grad_window[:, start_row : start_row + token_rows],
            ],
            axis=2,
        )
        got = shifted(sent, "ctx", -distance)
        received_k = received_k + got[:, :, :key_value_width]
        received_v = received_v + got[:, :, key_value_width:]
    own_k = key_grad_window[:, padding_rows:]
    own_v = value_grad_window[:, padding_rows:]
    d_queries = (
        (lin_dq + window_dq)
        .astype(jnp.bfloat16)
        .reshape(batch_inputs, token_rows, QUERY_HEADS * HEAD_SIZE)
    )
    keys_gradient = (
        linear_key_gradient.reshape(batch_inputs, token_rows, key_value_width) + own_k + received_k
    ).astype(jnp.bfloat16)
    values_gradient = (
        linear_value_gradient.reshape(batch_inputs, token_rows, key_value_width)
        + own_v
        + received_v
    ).astype(jnp.bfloat16)
    return (mixed, d_queries, keys_gradient, values_gradient, d_gain)


def solution(mesh):
    placed = (
        P("dp", "ctx", None),
        P("dp", "ctx", None),
        P("dp", "ctx", None),
        P("dp", "ctx", None),
        P(),
        P(),
        P("dp", "ctx", None),
    )
    return jax.shard_map(
        per_device,
        mesh=mesh,
        in_specs=placed,
        out_specs=(
            P("dp", "ctx", None),
            P("dp", "ctx", None),
            P("dp", "ctx", None),
            P("dp", "ctx", None),
            P(),
        ),
        check_vma=False,
    )
```

```python
import math

import jax
import jax.numpy as jnp
from jax import lax
from jax.sharding import PartitionSpec as P

QUERY_HEADS = 14
KEY_VALUE_HEADS = 2
HEAD_SIZE = 128
WINDOW_REACH = 256


epsilon = 1e-05


def gathered_before(gathered, axis, reverse):
    count = lax.axis_size(axis)
    place = lax.axis_index(axis)
    slots = jnp.arange(count).reshape((count,) + (1,) * (gathered.ndim - 1))
    chosen = slots > place if reverse else slots < place
    return jnp.sum(jnp.where(chosen, gathered, 0.0), axis=0)


def all_sum(part, axes):
    count = 1
    for axis in axes:
        count *= lax.axis_size(axis)
    step = 1
    while step < count:
        route = [(i, i ^ step) for i in range(count)]
        part = part + lax.ppermute(part, axes, route)
        step *= 2
    return part


def shifted(block, axis, distance):
    devices = range(lax.axis_size(axis))
    route = [(i - distance, i) for i in devices if i - distance in devices]
    return lax.ppermute(block, axis, route)


def per_device(queries, keys, values, spikes, window_lengths, gain, cotangent):
    batch_inputs = queries.shape[0]
    token_rows = queries.shape[1]
    group_size = QUERY_HEADS // KEY_VALUE_HEADS
    reach = (WINDOW_REACH + token_rows - 2) // token_rows
    padding_rows = reach * token_rows
    window_rows = (reach + 1) * token_rows
    scale = HEAD_SIZE ** (-0.5)
    key_value_width = KEY_VALUE_HEADS * HEAD_SIZE
    query_heads = queries.reshape(batch_inputs, token_rows, KEY_VALUE_HEADS, group_size, HEAD_SIZE)
    key_heads = keys.reshape(batch_inputs, token_rows, KEY_VALUE_HEADS, HEAD_SIZE)
    value_heads = values.reshape(batch_inputs, token_rows, KEY_VALUE_HEADS, HEAD_SIZE)
    token_counts = spikes.astype(jnp.float32)[..., None]
    spiked = (value_heads.astype(jnp.float32) * token_counts).astype(jnp.bfloat16)
    local_state = jnp.einsum(
        "nrgd,nrge->ngde", key_heads, spiked, preferred_element_type=jnp.float32
    )
    prior = gathered_before(lax.all_gather(local_state, "ctx"), "ctx", False)
    prior_half = prior.astype(jnp.bfloat16)
    packed = jnp.concatenate([keys, values], axis=2)
    earlier = []
    for distance in range(reach, 0, -1):
        earlier.append(shifted(packed, "ctx", distance))
    window_packed = jnp.concatenate(earlier + [packed], axis=1)
    key_window = window_packed[:, :, :key_value_width].reshape(
        batch_inputs, window_rows, KEY_VALUE_HEADS, HEAD_SIZE
    )
    value_window = window_packed[:, :, key_value_width:].reshape(
        batch_inputs, window_rows, KEY_VALUE_HEADS, HEAD_SIZE
    )
    row_idx = jnp.arange(token_rows)
    causal = (row_idx[:, None] >= row_idx[None, :]).astype(jnp.float32)
    key_idx = jnp.arange(window_rows)
    distance_back = row_idx[:, None] + padding_rows - key_idx[None, :]
    key_pos = lax.axis_index("ctx") * token_rows + key_idx - padding_rows
    visible = (
        (distance_back[None] >= 0)
        & (distance_back[None] < window_lengths[:, None, None])
        & (key_pos >= 0)[None, None, :]
    )
    lin_half = (
        jnp.einsum("nrghd,nsgd->nghrs", query_heads, key_heads, preferred_element_type=jnp.float32)
        * causal
    ).astype(jnp.bfloat16)
    linear = jnp.einsum("nghrs,nsge->nrghe", lin_half, spiked, preferred_element_type=jnp.float32)
    linear = linear + jnp.einsum(
        "nrghd,ngde->nrghe", query_heads, prior_half, preferred_element_type=jnp.float32
    )
    root = jnp.sqrt(jnp.mean(linear * linear, axis=-1, keepdims=True) + epsilon)
    normed = linear / root
    head_gains = gain.reshape(KEY_VALUE_HEADS, group_size, HEAD_SIZE)
    scores = (
        jnp.einsum("nrghd,nmgd->nghrm", query_heads, key_window, preferred_element_type=jnp.float32)
        * scale
    )
    scores = jnp.where(visible[None, :, None], scores, -1e30)
    top = jnp.max(scores, axis=-1, keepdims=True)
    expo = jnp.exp(scores - top)
    probs = expo / jnp.sum(expo, axis=-1, keepdims=True)
    probs_half = probs.astype(jnp.bfloat16)
    window_out = jnp.einsum(
        "nghrm,nmgd->nrghd", probs_half, value_window, preferred_element_type=jnp.float32
    )
    mixed = (
        (head_gains * normed + window_out)
        .astype(jnp.bfloat16)
        .reshape(batch_inputs, token_rows, QUERY_HEADS * HEAD_SIZE)
    )
    head_gradients = cotangent.reshape(
        batch_inputs, token_rows, KEY_VALUE_HEADS, group_size, HEAD_SIZE
    )
    grad_wide = head_gradients.astype(jnp.float32)
    total_tokens = batch_inputs * lax.axis_size("dp") * token_rows * lax.axis_size("ctx")
    gain_local = jnp.sum(grad_wide * normed, axis=(0, 1)).reshape(QUERY_HEADS * HEAD_SIZE)
    scaled = grad_wide * head_gains
    d_linear = (
        (scaled - normed * jnp.mean(scaled * normed, axis=-1, keepdims=True)) / root
    ).astype(jnp.bfloat16)
    suffix_local = jnp.einsum(
        "nrghd,nrghe->ngde", query_heads, d_linear, preferred_element_type=jnp.float32
    )
    state_rows = KEY_VALUE_HEADS * HEAD_SIZE
    gain_rows = QUERY_HEADS * HEAD_SIZE // HEAD_SIZE
    pad_rows = (-(state_rows + gain_rows)) % 8
    riding = jnp.concatenate(
        [
            suffix_local.reshape(state_rows, HEAD_SIZE),
            gain_local.reshape(gain_rows, HEAD_SIZE),
            jnp.zeros((pad_rows, HEAD_SIZE), jnp.float32),
        ],
        axis=0,
    )
    riding_all = lax.all_gather(riding, "ctx")
    later = gathered_before(riding_all[:, :state_rows], "ctx", True).reshape(suffix_local.shape)
    gain_ctx = jnp.sum(riding_all[:, state_rows : state_rows + gain_rows], axis=0)
    d_gain = all_sum(gain_ctx.reshape(QUERY_HEADS * HEAD_SIZE), ("dp",)) * (total_tokens ** (-0.5))
    later_half = later.astype(jnp.bfloat16)
    back_half = (
        jnp.einsum("nrghe,nsge->nghrs", d_linear, spiked, preferred_element_type=jnp.float32)
        * causal
    ).astype(jnp.bfloat16)
    lin_dq = jnp.einsum(
        "nrghe,ngde->nrghd", d_linear, prior_half, preferred_element_type=jnp.float32
    )
    lin_dq = lin_dq + jnp.einsum(
        "nghrs,nsgd->nrghd", back_half, key_heads, preferred_element_type=jnp.float32
    )
    linear_key_gradient = jnp.einsum(
        "nghrs,nrghd->nsgd", back_half, query_heads, preferred_element_type=jnp.float32
    )
    linear_key_gradient = linear_key_gradient + jnp.einsum(
        "nsge,ngde->nsgd", spiked, later_half, preferred_element_type=jnp.float32
    )
    d_spiked = jnp.einsum(
        "nghrs,nrghe->nsge", lin_half, d_linear, preferred_element_type=jnp.float32
    )
    d_spiked = d_spiked + jnp.einsum(
        "nsgd,ngde->nsge", key_heads, later_half, preferred_element_type=jnp.float32
    )
    linear_value_gradient = d_spiked * token_counts
    grad_probs = jnp.einsum(
        "nrghd,nmgd->nghrm", head_gradients, value_window, preferred_element_type=jnp.float32
    )
    delta = jnp.transpose(jnp.sum(grad_wide * window_out, axis=-1), (0, 2, 3, 1))
    grad_scores = (probs * (grad_probs - delta[..., None]) * scale).astype(jnp.bfloat16)
    window_dq = jnp.einsum(
        "nghrm,nmgd->nrghd", grad_scores, key_window, preferred_element_type=jnp.float32
    )
    key_grad_window = jnp.einsum(
        "nghrm,nrghd->nmgd", grad_scores, query_heads, preferred_element_type=jnp.float32
    ).reshape(batch_inputs, window_rows, key_value_width)
    value_grad_window = jnp.einsum(
        "nghrm,nrghd->nmgd", probs_half, head_gradients, preferred_element_type=jnp.float32
    ).reshape(batch_inputs, window_rows, key_value_width)
    received_k = jnp.zeros((batch_inputs, token_rows, key_value_width), jnp.float32)
    received_v = jnp.zeros((batch_inputs, token_rows, key_value_width), jnp.float32)
    for distance in range(1, reach + 1):
        start_row = (reach - distance) * token_rows
        sent = jnp.concatenate(
            [
                key_grad_window[:, start_row : start_row + token_rows],
                value_grad_window[:, start_row : start_row + token_rows],
            ],
            axis=2,
        )
        got = shifted(sent, "ctx", -distance)
        received_k = received_k + got[:, :, :key_value_width]
        received_v = received_v + got[:, :, key_value_width:]
    own_k = key_grad_window[:, padding_rows:]
    own_v = value_grad_window[:, padding_rows:]
    d_queries = (
        (lin_dq + window_dq)
        .astype(jnp.bfloat16)
        .reshape(batch_inputs, token_rows, QUERY_HEADS * HEAD_SIZE)
    )
    keys_gradient = (
        linear_key_gradient.reshape(batch_inputs, token_rows, key_value_width) + own_k + received_k
    ).astype(jnp.bfloat16)
    values_gradient = (
        linear_value_gradient.reshape(batch_inputs, token_rows, key_value_width)
        + own_v
        + received_v
    ).astype(jnp.bfloat16)
    return (mixed, d_queries, keys_gradient, values_gradient, d_gain)


def solution(mesh):
    placed = (
        P("dp", "ctx", None),
        P("dp", "ctx", None),
        P("dp", "ctx", None),
        P("dp", "ctx", None),
        P(),
        P(),
        P("dp", "ctx", None),
    )
    return jax.shard_map(
        per_device,
        mesh=mesh,
        in_specs=placed,
        out_specs=(
            P("dp", "ctx", None),
            P("dp", "ctx", None),
            P("dp", "ctx", None),
            P("dp", "ctx", None),
            P(),
        ),
        check_vma=False,
    )
```

```python
import jax
import jax.numpy as jnp
from jax import lax
from jax.experimental import pallas as pl
from jax.experimental.pallas import tpu as pltpu
from jax.sharding import PartitionSpec as P

QUERY_HEADS = 14
KEY_VALUE_HEADS = 2
HEAD_SIZE = 128
WINDOW_REACH = 256


epsilon = 1e-05


def exclusive_scan(part, axis, reverse):
    count = lax.axis_size(axis)
    running = part
    total = None
    distance = 1
    while distance < count:
        if reverse:
            route = [(i + distance, i) for i in range(count - distance)]
        else:
            route = [(i, i + distance) for i in range(count - distance)]
        got = lax.ppermute(running, axis, route)
        total = got if total is None else total + got
        if distance * 2 < count:
            running = running + got
        distance *= 2
    if total is None:
        total = jnp.zeros_like(part)
    return total


def all_sum(part, axes):
    count = 1
    for axis in axes:
        count *= lax.axis_size(axis)
    step = 1
    while step < count:
        route = [(i, i ^ step) for i in range(count)]
        part = part + lax.ppermute(part, axes, route)
        step *= 2
    return part


def shifted(block, axis, distance):
    devices = range(lax.axis_size(axis))
    route = [(i - distance, i) for i in devices if i - distance in devices]
    return lax.ppermute(block, axis, route)


def window_kernel(info_ref, q_ref, c_ref, k_ref, v_ref, wout_ref, wdq_ref, dk_ref, dv_ref):
    group_size = QUERY_HEADS // KEY_VALUE_HEADS
    token_rows = q_ref.shape[0]
    window_rows = k_ref.shape[0]
    padding_rows = window_rows - token_rows
    scale = HEAD_SIZE ** (-0.5)
    row = lax.broadcasted_iota(jnp.int32, (token_rows, window_rows), 0)
    col = lax.broadcasted_iota(jnp.int32, (token_rows, window_rows), 1)
    back = row + padding_rows - col
    seen = (back >= 0) & (col + info_ref[2] >= 0)
    for g in range(KEY_VALUE_HEADS):
        visible = seen & (back < info_ref[g])
        lanes = slice(g * HEAD_SIZE, (g + 1) * HEAD_SIZE)
        kg = k_ref[:, lanes]
        vg = v_ref[:, lanes]
        dk = jnp.zeros((window_rows, HEAD_SIZE), jnp.float32)
        dv = jnp.zeros((window_rows, HEAD_SIZE), jnp.float32)
        for h in range(group_size):
            cols = slice((g * group_size + h) * HEAD_SIZE, (g * group_size + h + 1) * HEAD_SIZE)
            qh = q_ref[:, cols]
            ch = c_ref[:, cols]
            s = lax.dot_general(qh, kg, (((1,), (1,)), ((), ())), preferred_element_type=jnp.float32) * scale
            s = jnp.where(visible, s, -1e30)
            top = jnp.max(s, axis=-1, keepdims=True)
            e = jnp.exp(s - top)
            p = e / jnp.sum(e, axis=-1, keepdims=True)
            ph = p.astype(jnp.bfloat16)
            wout = jnp.dot(ph, vg, preferred_element_type=jnp.float32)
            wout_ref[:, cols] = wout
            gp = lax.dot_general(ch, vg, (((1,), (1,)), ((), ())), preferred_element_type=jnp.float32)
            delta = jnp.sum(ch.astype(jnp.float32) * wout, axis=-1, keepdims=True)
            ds = (p * (gp - delta) * scale).astype(jnp.bfloat16)
            wdq_ref[:, cols] = jnp.dot(ds, kg, preferred_element_type=jnp.float32)
            dk = dk + lax.dot_general(ds, qh, (((0,), (0,)), ((), ())), preferred_element_type=jnp.float32)
            dv = dv + lax.dot_general(ph, ch, (((0,), (0,)), ((), ())), preferred_element_type=jnp.float32)
        dk_ref[:, lanes] = dk
        dv_ref[:, lanes] = dv


def linear_kernel(q_ref, c_ref, k_ref, s_ref, prior_ref, gain_ref, wout_ref, wdq_ref,
                  mixed_ref, dq_ref, suffix_ref, gsum_ref, ldk_ref, dsp_ref):
    group_size = QUERY_HEADS // KEY_VALUE_HEADS
    token_rows = q_ref.shape[0]
    row = lax.broadcasted_iota(jnp.int32, (token_rows, token_rows), 0)
    col = lax.broadcasted_iota(jnp.int32, (token_rows, token_rows), 1)
    causal = row >= col
    for g in range(KEY_VALUE_HEADS):
        lanes = slice(g * HEAD_SIZE, (g + 1) * HEAD_SIZE)
        kg = k_ref[:, lanes]
        sg = s_ref[:, lanes]
        pg = prior_ref[g]
        suffix = jnp.zeros((HEAD_SIZE, HEAD_SIZE), jnp.float32)
        ldk = jnp.zeros((token_rows, HEAD_SIZE), jnp.float32)
        dsp = jnp.zeros((token_rows, HEAD_SIZE), jnp.float32)
        for h in range(group_size):
            cols = slice((g * group_size + h) * HEAD_SIZE, (g * group_size + h + 1) * HEAD_SIZE)
            qh = q_ref[:, cols]
            ch = c_ref[:, cols].astype(jnp.float32)
            gh = gain_ref[:, cols]
            lh = jnp.where(
                causal,
                lax.dot_general(qh, kg, (((1,), (1,)), ((), ())), preferred_element_type=jnp.float32),
                0.0,
            ).astype(jnp.bfloat16)
            lin = jnp.dot(lh, sg, preferred_element_type=jnp.float32) + jnp.dot(
                qh, pg, preferred_element_type=jnp.float32
            )
            root = jnp.sqrt(jnp.mean(lin * lin, axis=-1, keepdims=True) + epsilon)
            normed = lin / root
            mixed_ref[:, cols] = (gh * normed + wout_ref[:, cols]).astype(mixed_ref.dtype)
            gsum_ref[:, cols] = jnp.sum(ch * normed, axis=0, keepdims=True)
            scaled = ch * gh
            dl = ((scaled - normed * jnp.mean(scaled * normed, axis=-1, keepdims=True)) / root).astype(
                jnp.bfloat16
            )
            suffix = suffix + lax.dot_general(qh, dl, (((0,), (0,)), ((), ())), preferred_element_type=jnp.float32)
            bh = jnp.where(
                causal,
                lax.dot_general(dl, sg, (((1,), (1,)), ((), ())), preferred_element_type=jnp.float32),
                0.0,
            ).astype(jnp.bfloat16)
            ldq = lax.dot_general(dl, pg, (((1,), (1,)), ((), ())), preferred_element_type=jnp.float32)
            ldq = ldq + jnp.dot(bh, kg, preferred_element_type=jnp.float32)
            dq_ref[:, cols] = (ldq + wdq_ref[:, cols]).astype(dq_ref.dtype)
            ldk = ldk + lax.dot_general(bh, qh, (((0,), (0,)), ((), ())), preferred_element_type=jnp.float32)
            dsp = dsp + lax.dot_general(lh, dl, (((0,), (0,)), ((), ())), preferred_element_type=jnp.float32)
        suffix_ref[g] = suffix
        ldk_ref[:, lanes] = ldk
        dsp_ref[:, lanes] = dsp


def in_vmem(count):
    return [pl.BlockSpec(memory_space=pltpu.VMEM)] * count


def per_device(queries, keys, values, spikes, window_lengths, gain, cotangent):
    token_rows = queries.shape[1]
    width = QUERY_HEADS * HEAD_SIZE
    reach = (WINDOW_REACH + token_rows - 2) // token_rows
    padding_rows = reach * token_rows
    window_rows = (reach + 1) * token_rows
    key_value_width = KEY_VALUE_HEADS * HEAD_SIZE
    q = queries[0]
    c = cotangent[0]
    k = keys[0]
    v = values[0]
    counts = jnp.repeat(spikes[0].astype(jnp.float32), HEAD_SIZE, axis=1)
    spiked = (v.astype(jnp.float32) * counts).astype(jnp.bfloat16)
    local_state = jnp.stack(
        [
            lax.dot_general(
                k[:, g * HEAD_SIZE : (g + 1) * HEAD_SIZE],
                spiked[:, g * HEAD_SIZE : (g + 1) * HEAD_SIZE],
                (((0,), (0,)), ((), ())),
                preferred_element_type=jnp.float32,
            )
            for g in range(KEY_VALUE_HEADS)
        ]
    )
    prior_half = exclusive_scan(local_state, "ctx", False).astype(jnp.bfloat16)
    packed = jnp.concatenate([k, v], axis=1)
    earlier = []
    for distance in range(reach, 0, -1):
        earlier.append(shifted(packed, "ctx", distance))
    window_packed = jnp.concatenate(earlier + [packed], axis=0)
    info = jnp.concatenate(
        [window_lengths.astype(jnp.int32), (lax.axis_index("ctx") * token_rows - padding_rows).reshape(1)]
    ).astype(jnp.int32)
    wout, wdq, dk_win, dv_win = pl.pallas_call(
        window_kernel,
        out_shape=(
            jax.ShapeDtypeStruct((token_rows, width), jnp.float32),
            jax.ShapeDtypeStruct((token_rows, width), jnp.float32),
            jax.ShapeDtypeStruct((window_rows, key_value_width), jnp.float32),
            jax.ShapeDtypeStruct((window_rows, key_value_width), jnp.float32),
        ),
        in_specs=[pl.BlockSpec(memory_space=pltpu.SMEM)] + in_vmem(4),
        out_specs=tuple(in_vmem(4)),
    )(info, q, c, window_packed[:, :key_value_width], window_packed[:, key_value_width:])
    mixed, d_queries, suffix_local, gain_local, ldk, dsp = pl.pallas_call(
        linear_kernel,
        out_shape=(
            jax.ShapeDtypeStruct((token_rows, width), jnp.bfloat16),
            jax.ShapeDtypeStruct((token_rows, width), jnp.bfloat16),
            jax.ShapeDtypeStruct((KEY_VALUE_HEADS, HEAD_SIZE, HEAD_SIZE), jnp.float32),
            jax.ShapeDtypeStruct((1, width), jnp.float32),
            jax.ShapeDtypeStruct((token_rows, key_value_width), jnp.float32),
            jax.ShapeDtypeStruct((token_rows, key_value_width), jnp.float32),
        ),
        in_specs=in_vmem(8),
        out_specs=tuple(in_vmem(6)),
    )(q, c, k, spiked, prior_half, gain.reshape(1, width), wout, wdq)
    total_tokens = queries.shape[0] * lax.axis_size("dp") * token_rows * lax.axis_size("ctx")
    d_gain = all_sum(gain_local.reshape(width), ("dp", "ctx")) * (total_tokens ** (-0.5))
    later_half = exclusive_scan(suffix_local, "ctx", True).astype(jnp.bfloat16)
    ldk_parts = []
    dsp_parts = []
    for g in range(KEY_VALUE_HEADS):
        lanes = slice(g * HEAD_SIZE, (g + 1) * HEAD_SIZE)
        ldk_parts.append(
            ldk[:, lanes]
            + lax.dot_general(
                spiked[:, lanes], later_half[g], (((1,), (1,)), ((), ())), preferred_element_type=jnp.float32
            )
        )
        dsp_parts.append(
            dsp[:, lanes] + jnp.dot(k[:, lanes], later_half[g], preferred_element_type=jnp.float32)
        )
    linear_key_gradient = jnp.concatenate(ldk_parts, axis=1)
    linear_value_gradient = jnp.concatenate(dsp_parts, axis=1) * counts
    received = jnp.zeros((token_rows, 2 * key_value_width), jnp.float32)
    for distance in range(1, reach + 1):
        start_row = (reach - distance) * token_rows
        sent = jnp.concatenate(
            [
                dk_win[start_row : start_row + token_rows],
                dv_win[start_row : start_row + token_rows],
            ],
            axis=1,
        )
        received = received + shifted(sent, "ctx", -distance)
    keys_gradient = (
        linear_key_gradient + dk_win[padding_rows:] + received[:, :key_value_width]
    ).astype(jnp.bfloat16)
    values_gradient = (
        linear_value_gradient + dv_win[padding_rows:] + received[:, key_value_width:]
    ).astype(jnp.bfloat16)
    return (
        mixed[None],
        d_queries[None],
        keys_gradient[None],
        values_gradient[None],
        d_gain,
    )


def solution(mesh):
    placed = (
        P("dp", "ctx", None),
        P("dp", "ctx", None),
        P("dp", "ctx", None),
        P("dp", "ctx", None),
        P(),
        P(),
        P("dp", "ctx", None),
    )
    return jax.shard_map(
        per_device,
        mesh=mesh,
        in_specs=placed,
        out_specs=(
            P("dp", "ctx", None),
            P("dp", "ctx", None),
            P("dp", "ctx", None),
            P("dp", "ctx", None),
            P(),
        ),
        check_vma=False,
    )
```

```python
import jax
import jax.numpy as jnp
from jax import lax
from jax.experimental import pallas as pl
from jax.experimental.pallas import tpu as pltpu
from jax.sharding import PartitionSpec as P

QUERY_HEADS = 14
KEY_VALUE_HEADS = 2
HEAD_SIZE = 128
WINDOW_REACH = 256


epsilon = 1e-05


def exclusive_scan(part, axis, reverse, riders):
    count = lax.axis_size(axis)
    width = part.shape[1]
    running = part
    total = jnp.zeros_like(part)
    received = {}
    distance = 1
    while distance < count:
        if reverse:
            route = [(i + distance, i) for i in range(count - distance)]
        else:
            route = [(i, i + distance) for i in range(count - distance)]
        payload = running
        if distance in riders:
            payload = jnp.concatenate([running, riders[distance]], axis=1)
        got = lax.ppermute(payload, axis, route)
        if distance in riders:
            received[distance] = got[:, width:]
            got = got[:, :width]
        total = total + got
        if distance * 2 < count:
            running = running + got
        distance *= 2
    for distance, rider in riders.items():
        if distance not in received:
            received[distance] = shifted(rider, axis, -distance if reverse else distance)
    return total, received


def all_sum(part, axes):
    count = 1
    for axis in axes:
        count *= lax.axis_size(axis)
    step = 1
    while step < count:
        route = [(i, i ^ step) for i in range(count)]
        part = part + lax.ppermute(part, axes, route)
        step *= 2
    return part


def shifted(block, axis, distance):
    devices = range(lax.axis_size(axis))
    route = [(i - distance, i) for i in devices if i - distance in devices]
    return lax.ppermute(block, axis, route)


def window_kernel(info_ref, q_ref, c_ref, k_ref, v_ref, wout_ref, wdq_ref, dk_ref, dv_ref):
    group_size = QUERY_HEADS // KEY_VALUE_HEADS
    token_rows = q_ref.shape[0]
    window_rows = k_ref.shape[0]
    padding_rows = window_rows - token_rows
    scale = HEAD_SIZE ** (-0.5)
    row = lax.broadcasted_iota(jnp.int32, (token_rows, window_rows), 0)
    col = lax.broadcasted_iota(jnp.int32, (token_rows, window_rows), 1)
    back = row + padding_rows - col
    seen = (back >= 0) & (col + info_ref[2] >= 0)
    for g in range(KEY_VALUE_HEADS):
        visible = seen & (back < info_ref[g])
        lanes = slice(g * HEAD_SIZE, (g + 1) * HEAD_SIZE)
        kg = k_ref[:, lanes]
        vg = v_ref[:, lanes]
        dk = jnp.zeros((window_rows, HEAD_SIZE), jnp.float32)
        dv = jnp.zeros((window_rows, HEAD_SIZE), jnp.float32)
        for h in range(group_size):
            cols = slice((g * group_size + h) * HEAD_SIZE, (g * group_size + h + 1) * HEAD_SIZE)
            qh = q_ref[:, cols]
            ch = c_ref[:, cols]
            s = lax.dot_general(qh, kg, (((1,), (1,)), ((), ())), preferred_element_type=jnp.float32) * scale
            s = jnp.where(visible, s, -1e30)
            top = jnp.max(s, axis=-1, keepdims=True)
            e = jnp.exp(s - top)
            p = e / jnp.sum(e, axis=-1, keepdims=True)
            ph = p.astype(jnp.bfloat16)
            wout = jnp.dot(ph, vg, preferred_element_type=jnp.float32)
            wout_ref[:, cols] = wout
            gp = lax.dot_general(ch, vg, (((1,), (1,)), ((), ())), preferred_element_type=jnp.float32)
            delta = jnp.sum(ch.astype(jnp.float32) * wout, axis=-1, keepdims=True)
            ds = (p * (gp - delta) * scale).astype(jnp.bfloat16)
            wdq_ref[:, cols] = jnp.dot(ds, kg, preferred_element_type=jnp.float32)
            dk = dk + lax.dot_general(ds, qh, (((0,), (0,)), ((), ())), preferred_element_type=jnp.float32)
            dv = dv + lax.dot_general(ph, ch, (((0,), (0,)), ((), ())), preferred_element_type=jnp.float32)
        dk_ref[:, lanes] = dk
        dv_ref[:, lanes] = dv


def linear_kernel(q_ref, c_ref, k_ref, s_ref, prior_ref, gain_ref, wout_ref, wdq_ref,
                  mixed_ref, dq_ref, suffix_ref, gsum_ref, ldk_ref, dsp_ref):
    group_size = QUERY_HEADS // KEY_VALUE_HEADS
    token_rows = q_ref.shape[0]
    row = lax.broadcasted_iota(jnp.int32, (token_rows, token_rows), 0)
    col = lax.broadcasted_iota(jnp.int32, (token_rows, token_rows), 1)
    causal = row >= col
    for g in range(KEY_VALUE_HEADS):
        lanes = slice(g * HEAD_SIZE, (g + 1) * HEAD_SIZE)
        kg = k_ref[:, lanes]
        sg = s_ref[:, lanes]
        pg = prior_ref[:, lanes]
        suffix = jnp.zeros((HEAD_SIZE, HEAD_SIZE), jnp.float32)
        ldk = jnp.zeros((token_rows, HEAD_SIZE), jnp.float32)
        dsp = jnp.zeros((token_rows, HEAD_SIZE), jnp.float32)
        for h in range(group_size):
            cols = slice((g * group_size + h) * HEAD_SIZE, (g * group_size + h + 1) * HEAD_SIZE)
            qh = q_ref[:, cols]
            ch = c_ref[:, cols].astype(jnp.float32)
            gh = gain_ref[:, cols]
            lh = jnp.where(
                causal,
                lax.dot_general(qh, kg, (((1,), (1,)), ((), ())), preferred_element_type=jnp.float32),
                0.0,
            ).astype(jnp.bfloat16)
            lin = jnp.dot(lh, sg, preferred_element_type=jnp.float32) + jnp.dot(
                qh, pg, preferred_element_type=jnp.float32
            )
            root = jnp.sqrt(jnp.mean(lin * lin, axis=-1, keepdims=True) + epsilon)
            normed = lin / root
            mixed_ref[:, cols] = (gh * normed + wout_ref[:, cols]).astype(mixed_ref.dtype)
            gsum_ref[:, cols] = jnp.sum(ch * normed, axis=0, keepdims=True)
            scaled = ch * gh
            dl = ((scaled - normed * jnp.mean(scaled * normed, axis=-1, keepdims=True)) / root).astype(
                jnp.bfloat16
            )
            suffix = suffix + lax.dot_general(qh, dl, (((0,), (0,)), ((), ())), preferred_element_type=jnp.float32)
            bh = jnp.where(
                causal,
                lax.dot_general(dl, sg, (((1,), (1,)), ((), ())), preferred_element_type=jnp.float32),
                0.0,
            ).astype(jnp.bfloat16)
            ldq = lax.dot_general(dl, pg, (((1,), (1,)), ((), ())), preferred_element_type=jnp.float32)
            ldq = ldq + jnp.dot(bh, kg, preferred_element_type=jnp.float32)
            dq_ref[:, cols] = (ldq + wdq_ref[:, cols]).astype(dq_ref.dtype)
            ldk = ldk + lax.dot_general(bh, qh, (((0,), (0,)), ((), ())), preferred_element_type=jnp.float32)
            dsp = dsp + lax.dot_general(lh, dl, (((0,), (0,)), ((), ())), preferred_element_type=jnp.float32)
        suffix_ref[:, lanes] = suffix
        ldk_ref[:, lanes] = ldk
        dsp_ref[:, lanes] = dsp


def in_vmem(count):
    return [pl.BlockSpec(memory_space=pltpu.VMEM)] * count


def per_device(queries, keys, values, spikes, window_lengths, gain, cotangent):
    token_rows = queries.shape[1]
    width = QUERY_HEADS * HEAD_SIZE
    reach = (WINDOW_REACH + token_rows - 2) // token_rows
    padding_rows = reach * token_rows
    window_rows = (reach + 1) * token_rows
    key_value_width = KEY_VALUE_HEADS * HEAD_SIZE
    q = queries[0]
    c = cotangent[0]
    k = keys[0]
    v = values[0]
    counts = jnp.repeat(spikes[0].astype(jnp.float32), HEAD_SIZE, axis=1)
    spiked = (v.astype(jnp.float32) * counts).astype(jnp.bfloat16)
    local_state = jnp.concatenate(
        [
            lax.dot_general(
                k[:, g * HEAD_SIZE : (g + 1) * HEAD_SIZE],
                spiked[:, g * HEAD_SIZE : (g + 1) * HEAD_SIZE],
                (((0,), (0,)), ((), ())),
                preferred_element_type=jnp.float32,
            )
            for g in range(KEY_VALUE_HEADS)
        ],
        axis=1,
    )
    packed = jnp.concatenate([k, v], axis=1).astype(jnp.float32)
    prior, halo = exclusive_scan(
        local_state, "ctx", False, {distance: packed for distance in range(1, reach + 1)}
    )
    prior_half = prior.astype(jnp.bfloat16)
    window_packed = jnp.concatenate(
        [halo[distance] for distance in range(reach, 0, -1)] + [packed], axis=0
    ).astype(jnp.bfloat16)
    info = jnp.concatenate(
        [window_lengths.astype(jnp.int32), (lax.axis_index("ctx") * token_rows - padding_rows).reshape(1)]
    ).astype(jnp.int32)
    wout, wdq, dk_win, dv_win = pl.pallas_call(
        window_kernel,
        out_shape=(
            jax.ShapeDtypeStruct((token_rows, width), jnp.float32),
            jax.ShapeDtypeStruct((token_rows, width), jnp.float32),
            jax.ShapeDtypeStruct((window_rows, key_value_width), jnp.float32),
            jax.ShapeDtypeStruct((window_rows, key_value_width), jnp.float32),
        ),
        in_specs=[pl.BlockSpec(memory_space=pltpu.SMEM)] + in_vmem(4),
        out_specs=tuple(in_vmem(4)),
    )(info, q, c, window_packed[:, :key_value_width], window_packed[:, key_value_width:])
    mixed, d_queries, suffix_local, gain_local, ldk, dsp = pl.pallas_call(
        linear_kernel,
        out_shape=(
            jax.ShapeDtypeStruct((token_rows, width), jnp.bfloat16),
            jax.ShapeDtypeStruct((token_rows, width), jnp.bfloat16),
            jax.ShapeDtypeStruct((HEAD_SIZE, key_value_width), jnp.float32),
            jax.ShapeDtypeStruct((1, width), jnp.float32),
            jax.ShapeDtypeStruct((token_rows, key_value_width), jnp.float32),
            jax.ShapeDtypeStruct((token_rows, key_value_width), jnp.float32),
        ),
        in_specs=in_vmem(8),
        out_specs=tuple(in_vmem(6)),
    )(q, c, k, spiked, prior_half, gain.reshape(1, width), wout, wdq)
    total_tokens = queries.shape[0] * lax.axis_size("dp") * token_rows * lax.axis_size("ctx")
    gain_rows = width // HEAD_SIZE
    gain_block = jnp.concatenate(
        [
            gain_local.reshape(gain_rows, HEAD_SIZE),
            jnp.zeros((key_value_width - gain_rows, HEAD_SIZE), jnp.float32),
        ],
        axis=0,
    )
    gains = lax.all_gather(gain_block, "ctx")[:, :gain_rows]
    d_gain = all_sum(jnp.sum(gains, axis=0).reshape(width), ("dp",)) * (total_tokens ** (-0.5))
    sent = {}
    for distance in range(1, reach + 1):
        start_row = (reach - distance) * token_rows
        sent[distance] = jnp.concatenate(
            [
                dk_win[start_row : start_row + token_rows],
                dv_win[start_row : start_row + token_rows],
            ],
            axis=1,
        )
    later, back = exclusive_scan(suffix_local, "ctx", True, sent)
    later_half = later.astype(jnp.bfloat16)
    ldk_parts = []
    dsp_parts = []
    for g in range(KEY_VALUE_HEADS):
        lanes = slice(g * HEAD_SIZE, (g + 1) * HEAD_SIZE)
        ldk_parts.append(
            ldk[:, lanes]
            + lax.dot_general(
                spiked[:, lanes], later_half[:, lanes], (((1,), (1,)), ((), ())), preferred_element_type=jnp.float32
            )
        )
        dsp_parts.append(
            dsp[:, lanes] + jnp.dot(k[:, lanes], later_half[:, lanes], preferred_element_type=jnp.float32)
        )
    linear_key_gradient = jnp.concatenate(ldk_parts, axis=1)
    linear_value_gradient = jnp.concatenate(dsp_parts, axis=1) * counts
    received = back[1]
    for distance in range(2, reach + 1):
        received = received + back[distance]
    keys_gradient = (
        linear_key_gradient + dk_win[padding_rows:] + received[:, :key_value_width]
    ).astype(jnp.bfloat16)
    values_gradient = (
        linear_value_gradient + dv_win[padding_rows:] + received[:, key_value_width:]
    ).astype(jnp.bfloat16)
    return (
        mixed[None],
        d_queries[None],
        keys_gradient[None],
        values_gradient[None],
        d_gain,
    )


def solution(mesh):
    placed = (
        P("dp", "ctx", None),
        P("dp", "ctx", None),
        P("dp", "ctx", None),
        P("dp", "ctx", None),
        P(),
        P(),
        P("dp", "ctx", None),
    )
    return jax.shard_map(
        per_device,
        mesh=mesh,
        in_specs=placed,
        out_specs=(
            P("dp", "ctx", None),
            P("dp", "ctx", None),
            P("dp", "ctx", None),
            P("dp", "ctx", None),
            P(),
        ),
        check_vma=False,
    )
```

```python
import jax
import jax.numpy as jnp
from jax import lax
from jax.experimental import pallas as pl
from jax.experimental.pallas import tpu as pltpu
from jax.sharding import PartitionSpec as P

QUERY_HEADS = 14
KEY_VALUE_HEADS = 2
HEAD_SIZE = 128
WINDOW_REACH = 256


epsilon = 1e-05


def exclusive_scan(part, axis, reverse):
    count = lax.axis_size(axis)
    running = part
    total = None
    distance = 1
    while distance < count:
        if reverse:
            route = [(i + distance, i) for i in range(count - distance)]
        else:
            route = [(i, i + distance) for i in range(count - distance)]
        got = lax.ppermute(running, axis, route)
        total = got if total is None else total + got
        if distance * 2 < count:
            running = running + got
        distance *= 2
    if total is None:
        total = jnp.zeros_like(part)
    return total


def butterfly_scan(part, axis, reverse):
    count = lax.axis_size(axis)
    place = lax.axis_index(axis)
    group = part
    before = jnp.zeros_like(part)
    step = 1
    while step < count:
        got = lax.ppermute(group, axis, [(i, i ^ step) for i in range(count)])
        partner = jnp.bitwise_xor(place, step)
        take = partner > place if reverse else partner < place
        before = before + jnp.where(take, got, 0.0)
        group = group + got
        step *= 2
    return before, group


def all_sum(part, axes):
    count = 1
    for axis in axes:
        count *= lax.axis_size(axis)
    step = 1
    while step < count:
        route = [(i, i ^ step) for i in range(count)]
        part = part + lax.ppermute(part, axes, route)
        step *= 2
    return part


def shifted(block, axis, distance):
    devices = range(lax.axis_size(axis))
    route = [(i - distance, i) for i in devices if i - distance in devices]
    return lax.ppermute(block, axis, route)


def window_kernel(info_ref, q_ref, c_ref, k_ref, v_ref, wout_ref, wdq_ref, dk_ref, dv_ref):
    group_size = QUERY_HEADS // KEY_VALUE_HEADS
    token_rows = q_ref.shape[0]
    window_rows = k_ref.shape[0]
    padding_rows = window_rows - token_rows
    scale = HEAD_SIZE ** (-0.5)
    row = lax.broadcasted_iota(jnp.int32, (token_rows, window_rows), 0)
    col = lax.broadcasted_iota(jnp.int32, (token_rows, window_rows), 1)
    back = row + padding_rows - col
    seen = (back >= 0) & (col + info_ref[2] >= 0)
    for g in range(KEY_VALUE_HEADS):
        visible = seen & (back < info_ref[g])
        lanes = slice(g * HEAD_SIZE, (g + 1) * HEAD_SIZE)
        kg = k_ref[:, lanes]
        vg = v_ref[:, lanes]
        dk = jnp.zeros((window_rows, HEAD_SIZE), jnp.float32)
        dv = jnp.zeros((window_rows, HEAD_SIZE), jnp.float32)
        for h in range(group_size):
            cols = slice((g * group_size + h) * HEAD_SIZE, (g * group_size + h + 1) * HEAD_SIZE)
            qh = q_ref[:, cols]
            ch = c_ref[:, cols]
            s = lax.dot_general(qh, kg, (((1,), (1,)), ((), ())), preferred_element_type=jnp.float32) * scale
            s = jnp.where(visible, s, -1e30)
            top = jnp.max(s, axis=-1, keepdims=True)
            e = jnp.exp(s - top)
            p = e / jnp.sum(e, axis=-1, keepdims=True)
            ph = p.astype(jnp.bfloat16)
            wout = jnp.dot(ph, vg, preferred_element_type=jnp.float32)
            wout_ref[:, cols] = wout
            gp = lax.dot_general(ch, vg, (((1,), (1,)), ((), ())), preferred_element_type=jnp.float32)
            delta = jnp.sum(ch.astype(jnp.float32) * wout, axis=-1, keepdims=True)
            ds = (p * (gp - delta) * scale).astype(jnp.bfloat16)
            wdq_ref[:, cols] = jnp.dot(ds, kg, preferred_element_type=jnp.float32)
            dk = dk + lax.dot_general(ds, qh, (((0,), (0,)), ((), ())), preferred_element_type=jnp.float32)
            dv = dv + lax.dot_general(ph, ch, (((0,), (0,)), ((), ())), preferred_element_type=jnp.float32)
        dk_ref[:, lanes] = dk
        dv_ref[:, lanes] = dv


def linear_kernel(q_ref, c_ref, k_ref, s_ref, prior_ref, gain_ref, wout_ref, wdq_ref,
                  mixed_ref, dq_ref, suffix_ref, gsum_ref, ldk_ref, dsp_ref):
    group_size = QUERY_HEADS // KEY_VALUE_HEADS
    token_rows = q_ref.shape[0]
    row = lax.broadcasted_iota(jnp.int32, (token_rows, token_rows), 0)
    col = lax.broadcasted_iota(jnp.int32, (token_rows, token_rows), 1)
    causal = row >= col
    for g in range(KEY_VALUE_HEADS):
        lanes = slice(g * HEAD_SIZE, (g + 1) * HEAD_SIZE)
        kg = k_ref[:, lanes]
        sg = s_ref[:, lanes]
        pg = prior_ref[g]
        suffix = jnp.zeros((HEAD_SIZE, HEAD_SIZE), jnp.float32)
        ldk = jnp.zeros((token_rows, HEAD_SIZE), jnp.float32)
        dsp = jnp.zeros((token_rows, HEAD_SIZE), jnp.float32)
        for h in range(group_size):
            cols = slice((g * group_size + h) * HEAD_SIZE, (g * group_size + h + 1) * HEAD_SIZE)
            qh = q_ref[:, cols]
            ch = c_ref[:, cols].astype(jnp.float32)
            gh = gain_ref[:, cols]
            lh = jnp.where(
                causal,
                lax.dot_general(qh, kg, (((1,), (1,)), ((), ())), preferred_element_type=jnp.float32),
                0.0,
            ).astype(jnp.bfloat16)
            lin = jnp.dot(lh, sg, preferred_element_type=jnp.float32) + jnp.dot(
                qh, pg, preferred_element_type=jnp.float32
            )
            root = jnp.sqrt(jnp.mean(lin * lin, axis=-1, keepdims=True) + epsilon)
            normed = lin / root
            mixed_ref[:, cols] = (gh * normed + wout_ref[:, cols]).astype(mixed_ref.dtype)
            gsum_ref[:, cols] = jnp.sum(ch * normed, axis=0, keepdims=True)
            scaled = ch * gh
            dl = ((scaled - normed * jnp.mean(scaled * normed, axis=-1, keepdims=True)) / root).astype(
                jnp.bfloat16
            )
            suffix = suffix + lax.dot_general(qh, dl, (((0,), (0,)), ((), ())), preferred_element_type=jnp.float32)
            bh = jnp.where(
                causal,
                lax.dot_general(dl, sg, (((1,), (1,)), ((), ())), preferred_element_type=jnp.float32),
                0.0,
            ).astype(jnp.bfloat16)
            ldq = lax.dot_general(dl, pg, (((1,), (1,)), ((), ())), preferred_element_type=jnp.float32)
            ldq = ldq + jnp.dot(bh, kg, preferred_element_type=jnp.float32)
            dq_ref[:, cols] = (ldq + wdq_ref[:, cols]).astype(dq_ref.dtype)
            ldk = ldk + lax.dot_general(bh, qh, (((0,), (0,)), ((), ())), preferred_element_type=jnp.float32)
            dsp = dsp + lax.dot_general(lh, dl, (((0,), (0,)), ((), ())), preferred_element_type=jnp.float32)
        suffix_ref[g] = suffix
        ldk_ref[:, lanes] = ldk
        dsp_ref[:, lanes] = dsp


def in_vmem(count):
    return [pl.BlockSpec(memory_space=pltpu.VMEM)] * count


def per_device(queries, keys, values, spikes, window_lengths, gain, cotangent):
    token_rows = queries.shape[1]
    width = QUERY_HEADS * HEAD_SIZE
    reach = (WINDOW_REACH + token_rows - 2) // token_rows
    padding_rows = reach * token_rows
    window_rows = (reach + 1) * token_rows
    key_value_width = KEY_VALUE_HEADS * HEAD_SIZE
    q = queries[0]
    c = cotangent[0]
    k = keys[0]
    v = values[0]
    counts = jnp.repeat(spikes[0].astype(jnp.float32), HEAD_SIZE, axis=1)
    spiked = (v.astype(jnp.float32) * counts).astype(jnp.bfloat16)
    local_state = jnp.stack(
        [
            lax.dot_general(
                k[:, g * HEAD_SIZE : (g + 1) * HEAD_SIZE],
                spiked[:, g * HEAD_SIZE : (g + 1) * HEAD_SIZE],
                (((0,), (0,)), ((), ())),
                preferred_element_type=jnp.float32,
            )
            for g in range(KEY_VALUE_HEADS)
        ]
    )
    prior_half = exclusive_scan(local_state, "ctx", False).astype(jnp.bfloat16)
    packed = jnp.concatenate([k, v], axis=1)
    earlier = []
    for distance in range(reach, 0, -1):
        earlier.append(shifted(packed, "ctx", distance))
    window_packed = jnp.concatenate(earlier + [packed], axis=0)
    info = jnp.concatenate(
        [window_lengths.astype(jnp.int32), (lax.axis_index("ctx") * token_rows - padding_rows).reshape(1)]
    ).astype(jnp.int32)
    wout, wdq, dk_win, dv_win = pl.pallas_call(
        window_kernel,
        out_shape=(
            jax.ShapeDtypeStruct((token_rows, width), jnp.float32),
            jax.ShapeDtypeStruct((token_rows, width), jnp.float32),
            jax.ShapeDtypeStruct((window_rows, key_value_width), jnp.float32),
            jax.ShapeDtypeStruct((window_rows, key_value_width), jnp.float32),
        ),
        in_specs=[pl.BlockSpec(memory_space=pltpu.SMEM)] + in_vmem(4),
        out_specs=tuple(in_vmem(4)),
    )(info, q, c, window_packed[:, :key_value_width], window_packed[:, key_value_width:])
    mixed, d_queries, suffix_local, gain_local, ldk, dsp = pl.pallas_call(
        linear_kernel,
        out_shape=(
            jax.ShapeDtypeStruct((token_rows, width), jnp.bfloat16),
            jax.ShapeDtypeStruct((token_rows, width), jnp.bfloat16),
            jax.ShapeDtypeStruct((KEY_VALUE_HEADS, HEAD_SIZE, HEAD_SIZE), jnp.float32),
            jax.ShapeDtypeStruct((1, width), jnp.float32),
            jax.ShapeDtypeStruct((token_rows, key_value_width), jnp.float32),
            jax.ShapeDtypeStruct((token_rows, key_value_width), jnp.float32),
        ),
        in_specs=in_vmem(8),
        out_specs=tuple(in_vmem(6)),
    )(q, c, k, spiked, prior_half, gain.reshape(1, width), wout, wdq)
    total_tokens = queries.shape[0] * lax.axis_size("dp") * token_rows * lax.axis_size("ctx")
    state_rows = KEY_VALUE_HEADS * HEAD_SIZE
    gain_rows = width // HEAD_SIZE
    pad_rows = (-(state_rows + gain_rows)) % 8
    riding = jnp.concatenate(
        [
            suffix_local.reshape(state_rows, HEAD_SIZE),
            gain_local.reshape(gain_rows, HEAD_SIZE),
            jnp.zeros((pad_rows, HEAD_SIZE), jnp.float32),
        ],
        axis=0,
    )
    later_rows, total_rows = butterfly_scan(riding, "ctx", True)
    later_half = later_rows[:state_rows].reshape(suffix_local.shape).astype(jnp.bfloat16)
    gain_ctx = total_rows[state_rows : state_rows + gain_rows].reshape(width)
    d_gain = all_sum(gain_ctx, ("dp",)) * (total_tokens ** (-0.5))
    ldk_parts = []
    dsp_parts = []
    for g in range(KEY_VALUE_HEADS):
        lanes = slice(g * HEAD_SIZE, (g + 1) * HEAD_SIZE)
        ldk_parts.append(
            ldk[:, lanes]
            + lax.dot_general(
                spiked[:, lanes], later_half[g], (((1,), (1,)), ((), ())), preferred_element_type=jnp.float32
            )
        )
        dsp_parts.append(
            dsp[:, lanes] + jnp.dot(k[:, lanes], later_half[g], preferred_element_type=jnp.float32)
        )
    linear_key_gradient = jnp.concatenate(ldk_parts, axis=1)
    linear_value_gradient = jnp.concatenate(dsp_parts, axis=1) * counts
    received = jnp.zeros((token_rows, 2 * key_value_width), jnp.float32)
    for distance in range(1, reach + 1):
        start_row = (reach - distance) * token_rows
        sent = jnp.concatenate(
            [
                dk_win[start_row : start_row + token_rows],
                dv_win[start_row : start_row + token_rows],
            ],
            axis=1,
        )
        received = received + shifted(sent, "ctx", -distance)
    keys_gradient = (
        linear_key_gradient + dk_win[padding_rows:] + received[:, :key_value_width]
    ).astype(jnp.bfloat16)
    values_gradient = (
        linear_value_gradient + dv_win[padding_rows:] + received[:, key_value_width:]
    ).astype(jnp.bfloat16)
    return (
        mixed[None],
        d_queries[None],
        keys_gradient[None],
        values_gradient[None],
        d_gain,
    )


def solution(mesh):
    placed = (
        P("dp", "ctx", None),
        P("dp", "ctx", None),
        P("dp", "ctx", None),
        P("dp", "ctx", None),
        P(),
        P(),
        P("dp", "ctx", None),
    )
    return jax.shard_map(
        per_device,
        mesh=mesh,
        in_specs=placed,
        out_specs=(
            P("dp", "ctx", None),
            P("dp", "ctx", None),
            P("dp", "ctx", None),
            P("dp", "ctx", None),
            P(),
        ),
        check_vma=False,
    )
```

```python
import jax
import jax.numpy as jnp
from jax import lax
from jax.experimental import pallas as pl
from jax.experimental.pallas import tpu as pltpu
from jax.sharding import PartitionSpec as P

QUERY_HEADS = 14
KEY_VALUE_HEADS = 2
HEAD_SIZE = 128
WINDOW_REACH = 256


epsilon = 1e-05


def exclusive_scan(part, axis, reverse):
    count = lax.axis_size(axis)
    running = part
    total = None
    distance = 1
    while distance < count:
        if reverse:
            route = [(i + distance, i) for i in range(count - distance)]
        else:
            route = [(i, i + distance) for i in range(count - distance)]
        got = lax.ppermute(running, axis, route)
        total = got if total is None else total + got
        if distance * 2 < count:
            running = running + got
        distance *= 2
    if total is None:
        total = jnp.zeros_like(part)
    return total


def butterfly_scan(part, axis, reverse):
    count = lax.axis_size(axis)
    place = lax.axis_index(axis)
    group = part
    before = jnp.zeros_like(part)
    step = 1
    while step < count:
        got = lax.ppermute(group, axis, [(i, i ^ step) for i in range(count)])
        partner = jnp.bitwise_xor(place, step)
        take = partner > place if reverse else partner < place
        before = before + jnp.where(take, got, 0.0)
        group = group + got
        step *= 2
    return before, group


def all_sum(part, axes):
    count = 1
    for axis in axes:
        count *= lax.axis_size(axis)
    step = 1
    while step < count:
        route = [(i, i ^ step) for i in range(count)]
        part = part + lax.ppermute(part, axes, route)
        step *= 2
    return part


def shifted(block, axis, distance):
    devices = range(lax.axis_size(axis))
    route = [(i - distance, i) for i in devices if i - distance in devices]
    return lax.ppermute(block, axis, route)


def window_kernel(info_ref, q_ref, c_ref, k_ref, v_ref, wout_ref, wdq_ref, dk_ref, dv_ref):
    group_size = QUERY_HEADS // KEY_VALUE_HEADS
    token_rows = q_ref.shape[0]
    window_rows = k_ref.shape[0]
    padding_rows = window_rows - token_rows
    scale = HEAD_SIZE ** (-0.5)
    row = lax.broadcasted_iota(jnp.int32, (token_rows, window_rows), 0)
    col = lax.broadcasted_iota(jnp.int32, (token_rows, window_rows), 1)
    back = row + padding_rows - col
    seen = (back >= 0) & (col + info_ref[2] >= 0)
    for g in range(KEY_VALUE_HEADS):
        visible = seen & (back < info_ref[g])
        lanes = slice(g * HEAD_SIZE, (g + 1) * HEAD_SIZE)
        kg = k_ref[:, lanes]
        vg = v_ref[:, lanes]
        dk = jnp.zeros((window_rows, HEAD_SIZE), jnp.float32)
        dv = jnp.zeros((window_rows, HEAD_SIZE), jnp.float32)
        for h in range(group_size):
            cols = slice((g * group_size + h) * HEAD_SIZE, (g * group_size + h + 1) * HEAD_SIZE)
            qh = q_ref[:, cols]
            ch = c_ref[:, cols]
            s = lax.dot_general(qh, kg, (((1,), (1,)), ((), ())), preferred_element_type=jnp.float32) * scale
            s = jnp.where(visible, s, -1e30)
            top = jnp.max(s, axis=-1, keepdims=True)
            e = jnp.exp(s - top)
            p = e / jnp.sum(e, axis=-1, keepdims=True)
            ph = p.astype(jnp.bfloat16)
            wout = jnp.dot(ph, vg, preferred_element_type=jnp.float32)
            wout_ref[:, cols] = wout
            gp = lax.dot_general(ch, vg, (((1,), (1,)), ((), ())), preferred_element_type=jnp.float32)
            delta = jnp.sum(ch.astype(jnp.float32) * wout, axis=-1, keepdims=True)
            ds = (p * (gp - delta) * scale).astype(jnp.bfloat16)
            wdq_ref[:, cols] = jnp.dot(ds, kg, preferred_element_type=jnp.float32)
            dk = dk + lax.dot_general(ds, qh, (((0,), (0,)), ((), ())), preferred_element_type=jnp.float32)
            dv = dv + lax.dot_general(ph, ch, (((0,), (0,)), ((), ())), preferred_element_type=jnp.float32)
        dk_ref[:, lanes] = dk
        dv_ref[:, lanes] = dv


def linear_kernel(q_ref, c_ref, k_ref, s_ref, prior_ref, gain_ref, wout_ref, wdq_ref,
                  mixed_ref, dq_ref, suffix_ref, gsum_ref, ldk_ref, dsp_ref):
    group_size = QUERY_HEADS // KEY_VALUE_HEADS
    token_rows = q_ref.shape[0]
    row = lax.broadcasted_iota(jnp.int32, (token_rows, token_rows), 0)
    col = lax.broadcasted_iota(jnp.int32, (token_rows, token_rows), 1)
    causal = row >= col
    for g in range(KEY_VALUE_HEADS):
        lanes = slice(g * HEAD_SIZE, (g + 1) * HEAD_SIZE)
        kg = k_ref[:, lanes]
        sg = s_ref[:, lanes]
        pg = prior_ref[g]
        suffix = jnp.zeros((HEAD_SIZE, HEAD_SIZE), jnp.float32)
        ldk = jnp.zeros((token_rows, HEAD_SIZE), jnp.float32)
        dsp = jnp.zeros((token_rows, HEAD_SIZE), jnp.float32)
        for h in range(group_size):
            cols = slice((g * group_size + h) * HEAD_SIZE, (g * group_size + h + 1) * HEAD_SIZE)
            qh = q_ref[:, cols]
            ch = c_ref[:, cols].astype(jnp.float32)
            gh = gain_ref[:, cols]
            lh = jnp.where(
                causal,
                lax.dot_general(qh, kg, (((1,), (1,)), ((), ())), preferred_element_type=jnp.float32),
                0.0,
            ).astype(jnp.bfloat16)
            lin = jnp.dot(lh, sg, preferred_element_type=jnp.float32) + jnp.dot(
                qh, pg, preferred_element_type=jnp.float32
            )
            root = jnp.sqrt(jnp.mean(lin * lin, axis=-1, keepdims=True) + epsilon)
            normed = lin / root
            mixed_ref[:, cols] = (gh * normed + wout_ref[:, cols]).astype(mixed_ref.dtype)
            gsum_ref[:, cols] = jnp.sum(ch * normed, axis=0, keepdims=True)
            scaled = ch * gh
            dl = ((scaled - normed * jnp.mean(scaled * normed, axis=-1, keepdims=True)) / root).astype(
                jnp.bfloat16
            )
            suffix = suffix + lax.dot_general(qh, dl, (((0,), (0,)), ((), ())), preferred_element_type=jnp.float32)
            bh = jnp.where(
                causal,
                lax.dot_general(dl, sg, (((1,), (1,)), ((), ())), preferred_element_type=jnp.float32),
                0.0,
            ).astype(jnp.bfloat16)
            ldq = lax.dot_general(dl, pg, (((1,), (1,)), ((), ())), preferred_element_type=jnp.float32)
            ldq = ldq + jnp.dot(bh, kg, preferred_element_type=jnp.float32)
            dq_ref[:, cols] = (ldq + wdq_ref[:, cols]).astype(dq_ref.dtype)
            ldk = ldk + lax.dot_general(bh, qh, (((0,), (0,)), ((), ())), preferred_element_type=jnp.float32)
            dsp = dsp + lax.dot_general(lh, dl, (((0,), (0,)), ((), ())), preferred_element_type=jnp.float32)
        suffix_ref[g] = suffix
        ldk_ref[:, lanes] = ldk
        dsp_ref[:, lanes] = dsp


def in_vmem(count):
    return [pl.BlockSpec(memory_space=pltpu.VMEM)] * count


def per_device(queries, keys, values, spikes, window_lengths, gain, cotangent):
    token_rows = queries.shape[1]
    width = QUERY_HEADS * HEAD_SIZE
    reach = (WINDOW_REACH + token_rows - 2) // token_rows
    padding_rows = reach * token_rows
    window_rows = (reach + 1) * token_rows
    key_value_width = KEY_VALUE_HEADS * HEAD_SIZE
    q = queries[0]
    c = cotangent[0]
    k = keys[0]
    v = values[0]
    counts = jnp.repeat(spikes[0].astype(jnp.float32), HEAD_SIZE, axis=1)
    spiked = (v.astype(jnp.float32) * counts).astype(jnp.bfloat16)
    local_state = jnp.stack(
        [
            lax.dot_general(
                k[:, g * HEAD_SIZE : (g + 1) * HEAD_SIZE],
                spiked[:, g * HEAD_SIZE : (g + 1) * HEAD_SIZE],
                (((0,), (0,)), ((), ())),
                preferred_element_type=jnp.float32,
            )
            for g in range(KEY_VALUE_HEADS)
        ]
    )
    prior_half = exclusive_scan(local_state, "ctx", False).astype(jnp.bfloat16)
    packed = jnp.concatenate([k, v], axis=1)
    earlier = []
    for distance in range(reach, 0, -1):
        earlier.append(shifted(packed, "ctx", distance))
    window_packed = jnp.concatenate(earlier + [packed], axis=0)
    info = jnp.concatenate(
        [window_lengths.astype(jnp.int32), (lax.axis_index("ctx") * token_rows - padding_rows).reshape(1)]
    ).astype(jnp.int32)
    wout, wdq, dk_win, dv_win = pl.pallas_call(
        window_kernel,
        out_shape=(
            jax.ShapeDtypeStruct((token_rows, width), jnp.float32),
            jax.ShapeDtypeStruct((token_rows, width), jnp.float32),
            jax.ShapeDtypeStruct((window_rows, key_value_width), jnp.float32),
            jax.ShapeDtypeStruct((window_rows, key_value_width), jnp.float32),
        ),
        in_specs=[pl.BlockSpec(memory_space=pltpu.SMEM)] + in_vmem(4),
        out_specs=tuple(in_vmem(4)),
        cost_estimate=pl.CostEstimate(
            flops=12 * QUERY_HEADS * token_rows * window_rows * HEAD_SIZE,
            transcendentals=QUERY_HEADS * token_rows * window_rows,
            bytes_accessed=2 * token_rows * width * (2 + 4) + 2 * window_rows * key_value_width * (2 + 4),
        ),
    )(info, q, c, window_packed[:, :key_value_width], window_packed[:, key_value_width:])
    mixed, d_queries, suffix_local, gain_local, ldk, dsp = pl.pallas_call(
        linear_kernel,
        out_shape=(
            jax.ShapeDtypeStruct((token_rows, width), jnp.bfloat16),
            jax.ShapeDtypeStruct((token_rows, width), jnp.bfloat16),
            jax.ShapeDtypeStruct((KEY_VALUE_HEADS, HEAD_SIZE, HEAD_SIZE), jnp.float32),
            jax.ShapeDtypeStruct((1, width), jnp.float32),
            jax.ShapeDtypeStruct((token_rows, key_value_width), jnp.float32),
            jax.ShapeDtypeStruct((token_rows, key_value_width), jnp.float32),
        ),
        in_specs=in_vmem(8),
        out_specs=tuple(in_vmem(6)),
        cost_estimate=pl.CostEstimate(
            flops=20 * QUERY_HEADS * token_rows * token_rows * HEAD_SIZE,
            transcendentals=QUERY_HEADS * token_rows,
            bytes_accessed=token_rows * width * (2 + 2 + 4 + 4 + 2 + 2) + 6 * token_rows * key_value_width * 4,
        ),
    )(q, c, k, spiked, prior_half, gain.reshape(1, width), wout, wdq)
    total_tokens = queries.shape[0] * lax.axis_size("dp") * token_rows * lax.axis_size("ctx")
    state_rows = KEY_VALUE_HEADS * HEAD_SIZE
    gain_rows = width // HEAD_SIZE
    pad_rows = (-(state_rows + gain_rows)) % 8
    riding = jnp.concatenate(
        [
            suffix_local.reshape(state_rows, HEAD_SIZE),
            gain_local.reshape(gain_rows, HEAD_SIZE),
            jnp.zeros((pad_rows, HEAD_SIZE), jnp.float32),
        ],
        axis=0,
    )
    later_rows, total_rows = butterfly_scan(riding, "ctx", True)
    later_half = later_rows[:state_rows].reshape(suffix_local.shape).astype(jnp.bfloat16)
    gain_ctx = total_rows[state_rows : state_rows + gain_rows].reshape(width)
    d_gain = all_sum(gain_ctx, ("dp",)) * (total_tokens ** (-0.5))
    ldk_parts = []
    dsp_parts = []
    for g in range(KEY_VALUE_HEADS):
        lanes = slice(g * HEAD_SIZE, (g + 1) * HEAD_SIZE)
        ldk_parts.append(
            ldk[:, lanes]
            + lax.dot_general(
                spiked[:, lanes], later_half[g], (((1,), (1,)), ((), ())), preferred_element_type=jnp.float32
            )
        )
        dsp_parts.append(
            dsp[:, lanes] + jnp.dot(k[:, lanes], later_half[g], preferred_element_type=jnp.float32)
        )
    linear_key_gradient = jnp.concatenate(ldk_parts, axis=1)
    linear_value_gradient = jnp.concatenate(dsp_parts, axis=1) * counts
    received = jnp.zeros((token_rows, 2 * key_value_width), jnp.float32)
    for distance in range(1, reach + 1):
        start_row = (reach - distance) * token_rows
        sent = jnp.concatenate(
            [
                dk_win[start_row : start_row + token_rows],
                dv_win[start_row : start_row + token_rows],
            ],
            axis=1,
        )
        received = received + shifted(sent.astype(jnp.bfloat16), "ctx", -distance).astype(jnp.float32)
    keys_gradient = (
        linear_key_gradient + dk_win[padding_rows:] + received[:, :key_value_width]
    ).astype(jnp.bfloat16)
    values_gradient = (
        linear_value_gradient + dv_win[padding_rows:] + received[:, key_value_width:]
    ).astype(jnp.bfloat16)
    return (
        mixed[None],
        d_queries[None],
        keys_gradient[None],
        values_gradient[None],
        d_gain,
    )


def solution(mesh):
    placed = (
        P("dp", "ctx", None),
        P("dp", "ctx", None),
        P("dp", "ctx", None),
        P("dp", "ctx", None),
        P(),
        P(),
        P("dp", "ctx", None),
    )
    return jax.shard_map(
        per_device,
        mesh=mesh,
        in_specs=placed,
        out_specs=(
            P("dp", "ctx", None),
            P("dp", "ctx", None),
            P("dp", "ctx", None),
            P("dp", "ctx", None),
            P(),
        ),
        check_vma=False,
    )
```

```python
import jax
import jax.numpy as jnp
from jax import lax
from jax.experimental import pallas as pl
from jax.experimental.pallas import tpu as pltpu
from jax.sharding import PartitionSpec as P

QUERY_HEADS = 14
KEY_VALUE_HEADS = 2
HEAD_SIZE = 128
WINDOW_REACH = 256


epsilon = 1e-05


def exclusive_scan(part, axis, reverse):
    count = lax.axis_size(axis)
    running = part
    total = None
    distance = 1
    while distance < count:
        if reverse:
            route = [(i + distance, i) for i in range(count - distance)]
        else:
            route = [(i, i + distance) for i in range(count - distance)]
        got = lax.ppermute(running, axis, route)
        total = got if total is None else total + got
        if distance * 2 < count:
            running = running + got
        distance *= 2
    if total is None:
        total = jnp.zeros_like(part)
    return total


def butterfly_scan(part, axis, reverse):
    count = lax.axis_size(axis)
    place = lax.axis_index(axis)
    group = part
    before = jnp.zeros_like(part)
    step = 1
    while step < count:
        got = lax.ppermute(group, axis, [(i, i ^ step) for i in range(count)])
        partner = jnp.bitwise_xor(place, step)
        take = partner > place if reverse else partner < place
        before = before + jnp.where(take, got, 0.0)
        group = group + got
        step *= 2
    return before, group


def all_sum(part, axes):
    count = 1
    for axis in axes:
        count *= lax.axis_size(axis)
    step = 1
    while step < count:
        route = [(i, i ^ step) for i in range(count)]
        part = part + lax.ppermute(part, axes, route)
        step *= 2
    return part


def shifted(block, axis, distance):
    devices = range(lax.axis_size(axis))
    route = [(i - distance, i) for i in devices if i - distance in devices]
    return lax.ppermute(block, axis, route)


def window_kernel(info_ref, q_ref, c_ref, k_ref, v_ref, wout_ref, wdq_ref, dk_ref, dv_ref):
    group_size = QUERY_HEADS // KEY_VALUE_HEADS
    token_rows = q_ref.shape[0]
    window_rows = k_ref.shape[0]
    padding_rows = window_rows - token_rows
    scale = HEAD_SIZE ** (-0.5)
    row = lax.broadcasted_iota(jnp.int32, (token_rows, window_rows), 0)
    col = lax.broadcasted_iota(jnp.int32, (token_rows, window_rows), 1)
    back = row + padding_rows - col
    seen = (back >= 0) & (col + info_ref[2] >= 0)
    for g in range(KEY_VALUE_HEADS):
        visible = seen & (back < info_ref[g])
        lanes = slice(g * HEAD_SIZE, (g + 1) * HEAD_SIZE)
        kg = k_ref[:, lanes]
        vg = v_ref[:, lanes]
        dk = jnp.zeros((window_rows, HEAD_SIZE), jnp.float32)
        dv = jnp.zeros((window_rows, HEAD_SIZE), jnp.float32)
        for h in range(group_size):
            cols = slice((g * group_size + h) * HEAD_SIZE, (g * group_size + h + 1) * HEAD_SIZE)
            qh = q_ref[:, cols]
            ch = c_ref[:, cols]
            s = lax.dot_general(qh, kg, (((1,), (1,)), ((), ())), preferred_element_type=jnp.float32) * scale
            s = jnp.where(visible, s, -1e30)
            top = jnp.max(s, axis=-1, keepdims=True)
            e = jnp.exp(s - top)
            p = e * (1.0 / jnp.sum(e, axis=-1, keepdims=True))
            ph = p.astype(jnp.bfloat16)
            wout = jnp.dot(ph, vg, preferred_element_type=jnp.float32)
            wout_ref[:, cols] = wout
            gp = lax.dot_general(ch, vg, (((1,), (1,)), ((), ())), preferred_element_type=jnp.float32)
            delta = jnp.sum(ch.astype(jnp.float32) * wout, axis=-1, keepdims=True)
            ds = (p * (gp - delta) * scale).astype(jnp.bfloat16)
            wdq_ref[:, cols] = jnp.dot(ds, kg, preferred_element_type=jnp.float32)
            dk = dk + lax.dot_general(ds, qh, (((0,), (0,)), ((), ())), preferred_element_type=jnp.float32)
            dv = dv + lax.dot_general(ph, ch, (((0,), (0,)), ((), ())), preferred_element_type=jnp.float32)
        dk_ref[:, lanes] = dk
        dv_ref[:, lanes] = dv


def linear_kernel(q_ref, c_ref, k_ref, s_ref, prior_ref, gain_ref, wout_ref, wdq_ref,
                  mixed_ref, dq_ref, suffix_ref, gsum_ref, ldk_ref, dsp_ref):
    group_size = QUERY_HEADS // KEY_VALUE_HEADS
    token_rows = q_ref.shape[0]
    row = lax.broadcasted_iota(jnp.int32, (token_rows, token_rows), 0)
    col = lax.broadcasted_iota(jnp.int32, (token_rows, token_rows), 1)
    causal = row >= col
    for g in range(KEY_VALUE_HEADS):
        lanes = slice(g * HEAD_SIZE, (g + 1) * HEAD_SIZE)
        kg = k_ref[:, lanes]
        sg = s_ref[:, lanes]
        pg = prior_ref[g]
        suffix = jnp.zeros((HEAD_SIZE, HEAD_SIZE), jnp.float32)
        ldk = jnp.zeros((token_rows, HEAD_SIZE), jnp.float32)
        dsp = jnp.zeros((token_rows, HEAD_SIZE), jnp.float32)
        for h in range(group_size):
            cols = slice((g * group_size + h) * HEAD_SIZE, (g * group_size + h + 1) * HEAD_SIZE)
            qh = q_ref[:, cols]
            ch = c_ref[:, cols].astype(jnp.float32)
            gh = gain_ref[:, cols]
            lh = jnp.where(
                causal,
                lax.dot_general(qh, kg, (((1,), (1,)), ((), ())), preferred_element_type=jnp.float32),
                0.0,
            ).astype(jnp.bfloat16)
            lin = jnp.dot(lh, sg, preferred_element_type=jnp.float32) + jnp.dot(
                qh, pg, preferred_element_type=jnp.float32
            )
            inverse_root = 1.0 / jnp.sqrt(jnp.mean(lin * lin, axis=-1, keepdims=True) + epsilon)
            normed = lin * inverse_root
            mixed_ref[:, cols] = (gh * normed + wout_ref[:, cols]).astype(mixed_ref.dtype)
            gsum_ref[:, cols] = jnp.sum(ch * normed, axis=0, keepdims=True)
            scaled = ch * gh
            dl = ((scaled - normed * jnp.mean(scaled * normed, axis=-1, keepdims=True)) * inverse_root).astype(
                jnp.bfloat16
            )
            suffix = suffix + lax.dot_general(qh, dl, (((0,), (0,)), ((), ())), preferred_element_type=jnp.float32)
            bh = jnp.where(
                causal,
                lax.dot_general(dl, sg, (((1,), (1,)), ((), ())), preferred_element_type=jnp.float32),
                0.0,
            ).astype(jnp.bfloat16)
            ldq = lax.dot_general(dl, pg, (((1,), (1,)), ((), ())), preferred_element_type=jnp.float32)
            ldq = ldq + jnp.dot(bh, kg, preferred_element_type=jnp.float32)
            dq_ref[:, cols] = (ldq + wdq_ref[:, cols]).astype(dq_ref.dtype)
            ldk = ldk + lax.dot_general(bh, qh, (((0,), (0,)), ((), ())), preferred_element_type=jnp.float32)
            dsp = dsp + lax.dot_general(lh, dl, (((0,), (0,)), ((), ())), preferred_element_type=jnp.float32)
        suffix_ref[g] = suffix
        ldk_ref[:, lanes] = ldk
        dsp_ref[:, lanes] = dsp


def in_vmem(count):
    return [pl.BlockSpec(memory_space=pltpu.VMEM)] * count


def per_device(queries, keys, values, spikes, window_lengths, gain, cotangent):
    token_rows = queries.shape[1]
    width = QUERY_HEADS * HEAD_SIZE
    reach = (WINDOW_REACH + token_rows - 2) // token_rows
    padding_rows = reach * token_rows
    window_rows = (reach + 1) * token_rows
    key_value_width = KEY_VALUE_HEADS * HEAD_SIZE
    q = queries[0]
    c = cotangent[0]
    k = keys[0]
    v = values[0]
    counts = jnp.repeat(spikes[0].astype(jnp.float32), HEAD_SIZE, axis=1)
    spiked = (v.astype(jnp.float32) * counts).astype(jnp.bfloat16)
    local_state = jnp.stack(
        [
            lax.dot_general(
                k[:, g * HEAD_SIZE : (g + 1) * HEAD_SIZE],
                spiked[:, g * HEAD_SIZE : (g + 1) * HEAD_SIZE],
                (((0,), (0,)), ((), ())),
                preferred_element_type=jnp.float32,
            )
            for g in range(KEY_VALUE_HEADS)
        ]
    )
    prior_half = exclusive_scan(local_state, "ctx", False).astype(jnp.bfloat16)
    packed = jnp.concatenate([k, v], axis=1)
    earlier = []
    for distance in range(reach, 0, -1):
        earlier.append(shifted(packed, "ctx", distance))
    window_packed = jnp.concatenate(earlier + [packed], axis=0)
    info = jnp.concatenate(
        [window_lengths.astype(jnp.int32), (lax.axis_index("ctx") * token_rows - padding_rows).reshape(1)]
    ).astype(jnp.int32)
    wout, wdq, dk_win, dv_win = pl.pallas_call(
        window_kernel,
        out_shape=(
            jax.ShapeDtypeStruct((token_rows, width), jnp.float32),
            jax.ShapeDtypeStruct((token_rows, width), jnp.float32),
            jax.ShapeDtypeStruct((window_rows, key_value_width), jnp.float32),
            jax.ShapeDtypeStruct((window_rows, key_value_width), jnp.float32),
        ),
        in_specs=[pl.BlockSpec(memory_space=pltpu.SMEM)] + in_vmem(4),
        out_specs=tuple(in_vmem(4)),
        cost_estimate=pl.CostEstimate(
            flops=12 * QUERY_HEADS * token_rows * window_rows * HEAD_SIZE,
            transcendentals=QUERY_HEADS * token_rows * window_rows,
            bytes_accessed=2 * token_rows * width * (2 + 4) + 2 * window_rows * key_value_width * (2 + 4),
        ),
    )(info, q, c, window_packed[:, :key_value_width], window_packed[:, key_value_width:])
    mixed, d_queries, suffix_local, gain_local, ldk, dsp = pl.pallas_call(
        linear_kernel,
        out_shape=(
            jax.ShapeDtypeStruct((token_rows, width), jnp.bfloat16),
            jax.ShapeDtypeStruct((token_rows, width), jnp.bfloat16),
            jax.ShapeDtypeStruct((KEY_VALUE_HEADS, HEAD_SIZE, HEAD_SIZE), jnp.float32),
            jax.ShapeDtypeStruct((1, width), jnp.float32),
            jax.ShapeDtypeStruct((token_rows, key_value_width), jnp.float32),
            jax.ShapeDtypeStruct((token_rows, key_value_width), jnp.float32),
        ),
        in_specs=in_vmem(8),
        out_specs=tuple(in_vmem(6)),
        cost_estimate=pl.CostEstimate(
            flops=20 * QUERY_HEADS * token_rows * token_rows * HEAD_SIZE,
            transcendentals=QUERY_HEADS * token_rows,
            bytes_accessed=token_rows * width * (2 + 2 + 4 + 4 + 2 + 2) + 6 * token_rows * key_value_width * 4,
        ),
    )(q, c, k, spiked, prior_half, gain.reshape(1, width), wout, wdq)
    total_tokens = queries.shape[0] * lax.axis_size("dp") * token_rows * lax.axis_size("ctx")
    state_rows = KEY_VALUE_HEADS * HEAD_SIZE
    gain_rows = width // HEAD_SIZE
    pad_rows = (-(state_rows + gain_rows)) % 8
    riding = jnp.concatenate(
        [
            suffix_local.reshape(state_rows, HEAD_SIZE),
            gain_local.reshape(gain_rows, HEAD_SIZE),
            jnp.zeros((pad_rows, HEAD_SIZE), jnp.float32),
        ],
        axis=0,
    )
    later_rows, total_rows = butterfly_scan(riding, "ctx", True)
    later_half = later_rows[:state_rows].reshape(suffix_local.shape).astype(jnp.bfloat16)
    gain_ctx = total_rows[state_rows : state_rows + gain_rows].reshape(width)
    d_gain = all_sum(gain_ctx, ("dp",)) * (total_tokens ** (-0.5))
    ldk_parts = []
    dsp_parts = []
    for g in range(KEY_VALUE_HEADS):
        lanes = slice(g * HEAD_SIZE, (g + 1) * HEAD_SIZE)
        ldk_parts.append(
            ldk[:, lanes]
            + lax.dot_general(
                spiked[:, lanes], later_half[g], (((1,), (1,)), ((), ())), preferred_element_type=jnp.float32
            )
        )
        dsp_parts.append(
            dsp[:, lanes] + jnp.dot(k[:, lanes], later_half[g], preferred_element_type=jnp.float32)
        )
    linear_key_gradient = jnp.concatenate(ldk_parts, axis=1)
    linear_value_gradient = jnp.concatenate(dsp_parts, axis=1) * counts
    received = jnp.zeros((token_rows, 2 * key_value_width), jnp.float32)
    for distance in range(1, reach + 1):
        start_row = (reach - distance) * token_rows
        sent = jnp.concatenate(
            [
                dk_win[start_row : start_row + token_rows],
                dv_win[start_row : start_row + token_rows],
            ],
            axis=1,
        )
        received = received + shifted(sent.astype(jnp.bfloat16), "ctx", -distance).astype(jnp.float32)
    keys_gradient = (
        linear_key_gradient + dk_win[padding_rows:] + received[:, :key_value_width]
    ).astype(jnp.bfloat16)
    values_gradient = (
        linear_value_gradient + dv_win[padding_rows:] + received[:, key_value_width:]
    ).astype(jnp.bfloat16)
    return (
        mixed[None],
        d_queries[None],
        keys_gradient[None],
        values_gradient[None],
        d_gain,
    )


def solution(mesh):
    placed = (
        P("dp", "ctx", None),
        P("dp", "ctx", None),
        P("dp", "ctx", None),
        P("dp", "ctx", None),
        P(),
        P(),
        P("dp", "ctx", None),
    )
    return jax.shard_map(
        per_device,
        mesh=mesh,
        in_specs=placed,
        out_specs=(
            P("dp", "ctx", None),
            P("dp", "ctx", None),
            P("dp", "ctx", None),
            P("dp", "ctx", None),
            P(),
        ),
        check_vma=False,
    )
```

```python
import jax
import jax.numpy as jnp
from jax import lax
from jax.experimental import pallas as pl
from jax.experimental.pallas import tpu as pltpu
from jax.sharding import PartitionSpec as P

QUERY_HEADS = 14
KEY_VALUE_HEADS = 2
HEAD_SIZE = 128
WINDOW_REACH = 256


epsilon = 1e-05


def exclusive_scan(part, axis, reverse):
    count = lax.axis_size(axis)
    running = part
    total = None
    distance = 1
    while distance < count:
        if reverse:
            route = [(i + distance, i) for i in range(count - distance)]
        else:
            route = [(i, i + distance) for i in range(count - distance)]
        got = lax.ppermute(running, axis, route)
        total = got if total is None else total + got
        if distance * 2 < count:
            running = running + got
        distance *= 2
    if total is None:
        total = jnp.zeros_like(part)
    return total


def butterfly_scan(part, axis, reverse):
    count = lax.axis_size(axis)
    place = lax.axis_index(axis)
    group = part
    before = jnp.zeros_like(part)
    step = 1
    while step < count:
        got = lax.ppermute(group, axis, [(i, i ^ step) for i in range(count)])
        partner = jnp.bitwise_xor(place, step)
        take = partner > place if reverse else partner < place
        before = before + jnp.where(take, got, 0.0)
        group = group + got
        step *= 2
    return before, group


def spread_scan(near, own, axis):
    count = lax.axis_size(axis)
    total = near
    running = own
    stride = 3
    while stride < count:
        parts = []
        for distance in (stride, 2 * stride):
            if distance < count:
                parts.append(shifted(running, axis, distance))
        for got in parts:
            total = total + got
        if 3 * stride < count:
            for got in parts:
                running = running + got
        stride *= 3
    return total


def all_sum(part, axes):
    count = 1
    for axis in axes:
        count *= lax.axis_size(axis)
    step = 1
    while step < count:
        route = [(i, i ^ step) for i in range(count)]
        part = part + lax.ppermute(part, axes, route)
        step *= 2
    return part


def shifted(block, axis, distance):
    devices = range(lax.axis_size(axis))
    route = [(i - distance, i) for i in devices if i - distance in devices]
    return lax.ppermute(block, axis, route)


def window_kernel(info_ref, q_ref, c_ref, k_ref, v_ref, wout_ref, wdq_ref, dk_ref, dv_ref):
    group_size = QUERY_HEADS // KEY_VALUE_HEADS
    token_rows = q_ref.shape[0]
    window_rows = k_ref.shape[0]
    padding_rows = window_rows - token_rows
    scale = HEAD_SIZE ** (-0.5)
    row = lax.broadcasted_iota(jnp.int32, (token_rows, window_rows), 0)
    col = lax.broadcasted_iota(jnp.int32, (token_rows, window_rows), 1)
    back = row + padding_rows - col
    seen = (back >= 0) & (col + info_ref[2] >= 0)
    for g in range(KEY_VALUE_HEADS):
        visible = seen & (back < info_ref[g])
        lanes = slice(g * HEAD_SIZE, (g + 1) * HEAD_SIZE)
        kg = k_ref[:, lanes]
        vg = v_ref[:, lanes]
        dk = jnp.zeros((window_rows, HEAD_SIZE), jnp.float32)
        dv = jnp.zeros((window_rows, HEAD_SIZE), jnp.float32)
        for h in range(group_size):
            cols = slice((g * group_size + h) * HEAD_SIZE, (g * group_size + h + 1) * HEAD_SIZE)
            qh = q_ref[:, cols]
            ch = c_ref[:, cols]
            s = lax.dot_general(qh, kg, (((1,), (1,)), ((), ())), preferred_element_type=jnp.float32) * scale
            s = jnp.where(visible, s, -1e30)
            top = jnp.max(s, axis=-1, keepdims=True)
            e = jnp.exp(s - top)
            p = e * (1.0 / jnp.sum(e, axis=-1, keepdims=True))
            ph = p.astype(jnp.bfloat16)
            wout = jnp.dot(ph, vg, preferred_element_type=jnp.float32)
            wout_ref[:, cols] = wout
            gp = lax.dot_general(ch, vg, (((1,), (1,)), ((), ())), preferred_element_type=jnp.float32)
            delta = jnp.sum(ch.astype(jnp.float32) * wout, axis=-1, keepdims=True)
            ds = (p * (gp - delta) * scale).astype(jnp.bfloat16)
            wdq_ref[:, cols] = jnp.dot(ds, kg, preferred_element_type=jnp.float32)
            dk = dk + lax.dot_general(ds, qh, (((0,), (0,)), ((), ())), preferred_element_type=jnp.float32)
            dv = dv + lax.dot_general(ph, ch, (((0,), (0,)), ((), ())), preferred_element_type=jnp.float32)
        dk_ref[:, lanes] = dk
        dv_ref[:, lanes] = dv


def linear_kernel(q_ref, c_ref, k_ref, s_ref, prior_ref, gain_ref, wout_ref, wdq_ref,
                  mixed_ref, dq_ref, suffix_ref, gsum_ref, ldk_ref, dsp_ref):
    group_size = QUERY_HEADS // KEY_VALUE_HEADS
    token_rows = q_ref.shape[0]
    row = lax.broadcasted_iota(jnp.int32, (token_rows, token_rows), 0)
    col = lax.broadcasted_iota(jnp.int32, (token_rows, token_rows), 1)
    causal = row >= col
    for g in range(KEY_VALUE_HEADS):
        lanes = slice(g * HEAD_SIZE, (g + 1) * HEAD_SIZE)
        kg = k_ref[:, lanes]
        sg = s_ref[:, lanes]
        pg = prior_ref[g]
        suffix = jnp.zeros((HEAD_SIZE, HEAD_SIZE), jnp.float32)
        ldk = jnp.zeros((token_rows, HEAD_SIZE), jnp.float32)
        dsp = jnp.zeros((token_rows, HEAD_SIZE), jnp.float32)
        for h in range(group_size):
            cols = slice((g * group_size + h) * HEAD_SIZE, (g * group_size + h + 1) * HEAD_SIZE)
            qh = q_ref[:, cols]
            ch = c_ref[:, cols].astype(jnp.float32)
            gh = gain_ref[:, cols]
            lh = jnp.where(
                causal,
                lax.dot_general(qh, kg, (((1,), (1,)), ((), ())), preferred_element_type=jnp.float32),
                0.0,
            ).astype(jnp.bfloat16)
            lin = jnp.dot(lh, sg, preferred_element_type=jnp.float32) + jnp.dot(
                qh, pg, preferred_element_type=jnp.float32
            )
            inverse_root = 1.0 / jnp.sqrt(jnp.mean(lin * lin, axis=-1, keepdims=True) + epsilon)
            normed = lin * inverse_root
            mixed_ref[:, cols] = (gh * normed + wout_ref[:, cols]).astype(mixed_ref.dtype)
            gsum_ref[:, cols] = jnp.sum(ch * normed, axis=0, keepdims=True)
            scaled = ch * gh
            dl = ((scaled - normed * jnp.mean(scaled * normed, axis=-1, keepdims=True)) * inverse_root).astype(
                jnp.bfloat16
            )
            suffix = suffix + lax.dot_general(qh, dl, (((0,), (0,)), ((), ())), preferred_element_type=jnp.float32)
            bh = jnp.where(
                causal,
                lax.dot_general(dl, sg, (((1,), (1,)), ((), ())), preferred_element_type=jnp.float32),
                0.0,
            ).astype(jnp.bfloat16)
            ldq = lax.dot_general(dl, pg, (((1,), (1,)), ((), ())), preferred_element_type=jnp.float32)
            ldq = ldq + jnp.dot(bh, kg, preferred_element_type=jnp.float32)
            dq_ref[:, cols] = (ldq + wdq_ref[:, cols]).astype(dq_ref.dtype)
            ldk = ldk + lax.dot_general(bh, qh, (((0,), (0,)), ((), ())), preferred_element_type=jnp.float32)
            dsp = dsp + lax.dot_general(lh, dl, (((0,), (0,)), ((), ())), preferred_element_type=jnp.float32)
        suffix_ref[g] = suffix
        ldk_ref[:, lanes] = ldk
        dsp_ref[:, lanes] = dsp


def in_vmem(count):
    return [pl.BlockSpec(memory_space=pltpu.VMEM)] * count


def per_device(queries, keys, values, spikes, window_lengths, gain, cotangent):
    token_rows = queries.shape[1]
    width = QUERY_HEADS * HEAD_SIZE
    reach = (WINDOW_REACH + token_rows - 2) // token_rows
    padding_rows = reach * token_rows
    window_rows = (reach + 1) * token_rows
    key_value_width = KEY_VALUE_HEADS * HEAD_SIZE
    q = queries[0]
    c = cotangent[0]
    k = keys[0]
    v = values[0]
    counts = jnp.repeat(spikes[0].astype(jnp.float32), HEAD_SIZE, axis=1)
    spiked = (v.astype(jnp.float32) * counts).astype(jnp.bfloat16)
    def state_of(block_keys, block_spiked):
        return jnp.stack(
            [
                lax.dot_general(
                    block_keys[:, g * HEAD_SIZE : (g + 1) * HEAD_SIZE],
                    block_spiked[:, g * HEAD_SIZE : (g + 1) * HEAD_SIZE],
                    (((0,), (0,)), ((), ())),
                    preferred_element_type=jnp.float32,
                )
                for g in range(KEY_VALUE_HEADS)
            ]
        )

    count_lanes = HEAD_SIZE
    spike_block = jnp.concatenate(
        [
            spikes[0].astype(jnp.bfloat16),
            jnp.zeros((token_rows, count_lanes - KEY_VALUE_HEADS), jnp.bfloat16),
        ],
        axis=1,
    )
    packed = jnp.concatenate([k, v, spike_block], axis=1)
    earlier = []
    for distance in range(reach, 0, -1):
        earlier.append(shifted(packed, "ctx", distance))
    near = jnp.zeros((KEY_VALUE_HEADS, HEAD_SIZE, HEAD_SIZE), jnp.float32)
    for piece in earlier:
        piece_counts = jnp.repeat(
            piece[:, 2 * key_value_width : 2 * key_value_width + KEY_VALUE_HEADS].astype(jnp.float32),
            HEAD_SIZE,
            axis=1,
        )
        piece_spiked = (
            piece[:, key_value_width : 2 * key_value_width].astype(jnp.float32) * piece_counts
        ).astype(jnp.bfloat16)
        near = near + state_of(piece[:, :key_value_width], piece_spiked)
    own_and_near = near + state_of(k, spiked)
    prior_half = spread_scan(near, own_and_near, "ctx").astype(jnp.bfloat16)
    window_packed = jnp.concatenate(
        [piece[:, : 2 * key_value_width] for piece in earlier] + [jnp.concatenate([k, v], axis=1)], axis=0
    )
    info = jnp.concatenate(
        [window_lengths.astype(jnp.int32), (lax.axis_index("ctx") * token_rows - padding_rows).reshape(1)]
    ).astype(jnp.int32)
    wout, wdq, dk_win, dv_win = pl.pallas_call(
        window_kernel,
        out_shape=(
            jax.ShapeDtypeStruct((token_rows, width), jnp.float32),
            jax.ShapeDtypeStruct((token_rows, width), jnp.float32),
            jax.ShapeDtypeStruct((window_rows, key_value_width), jnp.float32),
            jax.ShapeDtypeStruct((window_rows, key_value_width), jnp.float32),
        ),
        in_specs=[pl.BlockSpec(memory_space=pltpu.SMEM)] + in_vmem(4),
        out_specs=tuple(in_vmem(4)),
        cost_estimate=pl.CostEstimate(
            flops=12 * QUERY_HEADS * token_rows * window_rows * HEAD_SIZE,
            transcendentals=QUERY_HEADS * token_rows * window_rows,
            bytes_accessed=2 * token_rows * width * (2 + 4) + 2 * window_rows * key_value_width * (2 + 4),
        ),
    )(info, q, c, window_packed[:, :key_value_width], window_packed[:, key_value_width:])
    mixed, d_queries, suffix_local, gain_local, ldk, dsp = pl.pallas_call(
        linear_kernel,
        out_shape=(
            jax.ShapeDtypeStruct((token_rows, width), jnp.bfloat16),
            jax.ShapeDtypeStruct((token_rows, width), jnp.bfloat16),
            jax.ShapeDtypeStruct((KEY_VALUE_HEADS, HEAD_SIZE, HEAD_SIZE), jnp.float32),
            jax.ShapeDtypeStruct((1, width), jnp.float32),
            jax.ShapeDtypeStruct((token_rows, key_value_width), jnp.float32),
            jax.ShapeDtypeStruct((token_rows, key_value_width), jnp.float32),
        ),
        in_specs=in_vmem(8),
        out_specs=tuple(in_vmem(6)),
        cost_estimate=pl.CostEstimate(
            flops=20 * QUERY_HEADS * token_rows * token_rows * HEAD_SIZE,
            transcendentals=QUERY_HEADS * token_rows,
            bytes_accessed=token_rows * width * (2 + 2 + 4 + 4 + 2 + 2) + 6 * token_rows * key_value_width * 4,
        ),
    )(q, c, k, spiked, prior_half, gain.reshape(1, width), wout, wdq)
    total_tokens = queries.shape[0] * lax.axis_size("dp") * token_rows * lax.axis_size("ctx")
    state_rows = KEY_VALUE_HEADS * HEAD_SIZE
    gain_rows = width // HEAD_SIZE
    pad_rows = (-(state_rows + gain_rows)) % 8
    riding = jnp.concatenate(
        [
            suffix_local.reshape(state_rows, HEAD_SIZE),
            gain_local.reshape(gain_rows, HEAD_SIZE),
            jnp.zeros((pad_rows, HEAD_SIZE), jnp.float32),
        ],
        axis=0,
    )
    later_rows, total_rows = butterfly_scan(riding, "ctx", True)
    later_half = later_rows[:state_rows].reshape(suffix_local.shape).astype(jnp.bfloat16)
    gain_ctx = total_rows[state_rows : state_rows + gain_rows].reshape(width)
    d_gain = all_sum(gain_ctx, ("dp",)) * (total_tokens ** (-0.5))
    ldk_parts = []
    dsp_parts = []
    for g in range(KEY_VALUE_HEADS):
        lanes = slice(g * HEAD_SIZE, (g + 1) * HEAD_SIZE)
        ldk_parts.append(
            ldk[:, lanes]
            + lax.dot_general(
                spiked[:, lanes], later_half[g], (((1,), (1,)), ((), ())), preferred_element_type=jnp.float32
            )
        )
        dsp_parts.append(
            dsp[:, lanes] + jnp.dot(k[:, lanes], later_half[g], preferred_element_type=jnp.float32)
        )
    linear_key_gradient = jnp.concatenate(ldk_parts, axis=1)
    linear_value_gradient = jnp.concatenate(dsp_parts, axis=1) * counts
    received = jnp.zeros((token_rows, 2 * key_value_width), jnp.float32)
    for distance in range(1, reach + 1):
        start_row = (reach - distance) * token_rows
        sent = jnp.concatenate(
            [
                dk_win[start_row : start_row + token_rows],
                dv_win[start_row : start_row + token_rows],
            ],
            axis=1,
        )
        received = received + shifted(sent.astype(jnp.bfloat16), "ctx", -distance).astype(jnp.float32)
    keys_gradient = (
        linear_key_gradient + dk_win[padding_rows:] + received[:, :key_value_width]
    ).astype(jnp.bfloat16)
    values_gradient = (
        linear_value_gradient + dv_win[padding_rows:] + received[:, key_value_width:]
    ).astype(jnp.bfloat16)
    return (
        mixed[None],
        d_queries[None],
        keys_gradient[None],
        values_gradient[None],
        d_gain,
    )


def solution(mesh):
    placed = (
        P("dp", "ctx", None),
        P("dp", "ctx", None),
        P("dp", "ctx", None),
        P("dp", "ctx", None),
        P(),
        P(),
        P("dp", "ctx", None),
    )
    return jax.shard_map(
        per_device,
        mesh=mesh,
        in_specs=placed,
        out_specs=(
            P("dp", "ctx", None),
            P("dp", "ctx", None),
            P("dp", "ctx", None),
            P("dp", "ctx", None),
            P(),
        ),
        check_vma=False,
    )
```

```python
import functools

import jax
import jax.numpy as jnp
from jax import lax
from jax.experimental import pallas as pl
from jax.experimental.pallas import tpu as pltpu
from jax.sharding import PartitionSpec as P

QUERY_HEADS = 14
KEY_VALUE_HEADS = 2
HEAD_SIZE = 128
WINDOW_REACH = 256


epsilon = 1e-05


def exclusive_scan(part, axis, reverse):
    count = lax.axis_size(axis)
    running = part
    total = None
    distance = 1
    while distance < count:
        if reverse:
            route = [(i + distance, i) for i in range(count - distance)]
        else:
            route = [(i, i + distance) for i in range(count - distance)]
        got = lax.ppermute(running, axis, route)
        total = got if total is None else total + got
        if distance * 2 < count:
            running = running + got
        distance *= 2
    if total is None:
        total = jnp.zeros_like(part)
    return total


def butterfly_scan(part, axis, reverse):
    count = lax.axis_size(axis)
    place = lax.axis_index(axis)
    group = part
    before = jnp.zeros_like(part)
    first = None
    step = 1
    while step < count:
        got = lax.ppermute(group, axis, [(i, i ^ step) for i in range(count)])
        if first is None:
            first = got
        partner = jnp.bitwise_xor(place, step)
        take = partner > place if reverse else partner < place
        before = before + jnp.where(take, got, 0.0)
        group = group + got
        step *= 2
    return before, group, first


def spread_scan(near, own, axis):
    count = lax.axis_size(axis)
    total = near
    running = own
    stride = 3
    while stride < count:
        parts = []
        for distance in (stride, 2 * stride):
            if distance < count:
                parts.append(shifted(running, axis, distance))
        for got in parts:
            total = total + got
        if 3 * stride < count:
            for got in parts:
                running = running + got
        stride *= 3
    return total


def all_sum(part, axes):
    count = 1
    for axis in axes:
        count *= lax.axis_size(axis)
    step = 1
    while step < count:
        route = [(i, i ^ step) for i in range(count)]
        part = part + lax.ppermute(part, axes, route)
        step *= 2
    return part


def shifted(block, axis, distance):
    devices = range(lax.axis_size(axis))
    route = [(i - distance, i) for i in devices if i - distance in devices]
    return lax.ppermute(block, axis, route)


def window_kernel(group, info_ref, q_ref, c_ref, k_ref, v_ref, wout_ref, wdq_ref, dk_ref, dv_ref):
    group_size = QUERY_HEADS // KEY_VALUE_HEADS
    token_rows = q_ref.shape[0]
    window_rows = k_ref.shape[0]
    padding_rows = window_rows - token_rows
    scale = HEAD_SIZE ** (-0.5)
    row = lax.broadcasted_iota(jnp.int32, (token_rows, window_rows), 0)
    col = lax.broadcasted_iota(jnp.int32, (token_rows, window_rows), 1)
    back = row + padding_rows - col
    visible = (back >= 0) & (col + info_ref[KEY_VALUE_HEADS] >= 0) & (back < info_ref[group])
    lanes = slice(group * HEAD_SIZE, (group + 1) * HEAD_SIZE)
    kg = k_ref[:, lanes]
    vg = v_ref[:, lanes]
    dk = jnp.zeros((window_rows, HEAD_SIZE), jnp.float32)
    dv = jnp.zeros((window_rows, HEAD_SIZE), jnp.float32)
    for h in range(group_size):
        head = group * group_size + h
        cols = slice(head * HEAD_SIZE, (head + 1) * HEAD_SIZE)
        here = slice(h * HEAD_SIZE, (h + 1) * HEAD_SIZE)
        qh = q_ref[:, cols]
        ch = c_ref[:, cols]
        s = lax.dot_general(qh, kg, (((1,), (1,)), ((), ())), preferred_element_type=jnp.float32) * scale
        s = jnp.where(visible, s, -1e30)
        top = jnp.max(s, axis=-1, keepdims=True)
        e = jnp.exp(s - top)
        p = e * (1.0 / jnp.sum(e, axis=-1, keepdims=True))
        ph = p.astype(jnp.bfloat16)
        wout = jnp.dot(ph, vg, preferred_element_type=jnp.float32)
        wout_ref[:, here] = wout
        gp = lax.dot_general(ch, vg, (((1,), (1,)), ((), ())), preferred_element_type=jnp.float32)
        delta = jnp.sum(ch.astype(jnp.float32) * wout, axis=-1, keepdims=True)
        ds = (p * (gp - delta) * scale).astype(jnp.bfloat16)
        wdq_ref[:, here] = jnp.dot(ds, kg, preferred_element_type=jnp.float32)
        dk = dk + lax.dot_general(ds, qh, (((0,), (0,)), ((), ())), preferred_element_type=jnp.float32)
        dv = dv + lax.dot_general(ph, ch, (((0,), (0,)), ((), ())), preferred_element_type=jnp.float32)
    dk_ref[...] = dk
    dv_ref[...] = dv


def window_call(group, info, q, c, key_window, value_window):
    token_rows = q.shape[0]
    window_rows = key_window.shape[0]
    half = QUERY_HEADS * HEAD_SIZE // KEY_VALUE_HEADS
    return pl.pallas_call(
        functools.partial(window_kernel, group),
        out_shape=(
            jax.ShapeDtypeStruct((token_rows, half), jnp.float32),
            jax.ShapeDtypeStruct((token_rows, half), jnp.float32),
            jax.ShapeDtypeStruct((window_rows, HEAD_SIZE), jnp.float32),
            jax.ShapeDtypeStruct((window_rows, HEAD_SIZE), jnp.float32),
        ),
        in_specs=[pl.BlockSpec(memory_space=pltpu.SMEM)] + in_vmem(4),
        out_specs=tuple(in_vmem(4)),
        cost_estimate=pl.CostEstimate(
            flops=12 * (QUERY_HEADS // KEY_VALUE_HEADS) * token_rows * window_rows * HEAD_SIZE,
            transcendentals=(QUERY_HEADS // KEY_VALUE_HEADS) * token_rows * window_rows,
            bytes_accessed=token_rows * half * (2 + 2 + 4 + 4) + 2 * window_rows * HEAD_SIZE * (2 + 4),
        ),
    )(info, q, c, key_window, value_window)


def linear_kernel(q_ref, c_ref, k_ref, s_ref, prior_ref, gain_ref,
                  gn_ref, ldq_ref, suffix_ref, gsum_ref, ldk_ref, dsp_ref):
    group_size = QUERY_HEADS // KEY_VALUE_HEADS
    token_rows = q_ref.shape[0]
    row = lax.broadcasted_iota(jnp.int32, (token_rows, token_rows), 0)
    col = lax.broadcasted_iota(jnp.int32, (token_rows, token_rows), 1)
    causal = row >= col
    for g in range(KEY_VALUE_HEADS):
        lanes = slice(g * HEAD_SIZE, (g + 1) * HEAD_SIZE)
        kg = k_ref[:, lanes]
        sg = s_ref[:, lanes]
        pg = prior_ref[g]
        suffix = jnp.zeros((HEAD_SIZE, HEAD_SIZE), jnp.float32)
        ldk = jnp.zeros((token_rows, HEAD_SIZE), jnp.float32)
        dsp = jnp.zeros((token_rows, HEAD_SIZE), jnp.float32)
        for h in range(group_size):
            cols = slice((g * group_size + h) * HEAD_SIZE, (g * group_size + h + 1) * HEAD_SIZE)
            qh = q_ref[:, cols]
            ch = c_ref[:, cols].astype(jnp.float32)
            gh = gain_ref[:, cols]
            lh = jnp.where(
                causal,
                lax.dot_general(qh, kg, (((1,), (1,)), ((), ())), preferred_element_type=jnp.float32),
                0.0,
            ).astype(jnp.bfloat16)
            lin = jnp.dot(lh, sg, preferred_element_type=jnp.float32) + jnp.dot(
                qh, pg, preferred_element_type=jnp.float32
            )
            inverse_root = 1.0 / jnp.sqrt(jnp.mean(lin * lin, axis=-1, keepdims=True) + epsilon)
            normed = lin * inverse_root
            gn_ref[:, cols] = gh * normed
            gsum_ref[:, cols] = jnp.sum(ch * normed, axis=0, keepdims=True)
            scaled = ch * gh
            dl = ((scaled - normed * jnp.mean(scaled * normed, axis=-1, keepdims=True)) * inverse_root).astype(
                jnp.bfloat16
            )
            suffix = suffix + lax.dot_general(qh, dl, (((0,), (0,)), ((), ())), preferred_element_type=jnp.float32)
            bh = jnp.where(
                causal,
                lax.dot_general(dl, sg, (((1,), (1,)), ((), ())), preferred_element_type=jnp.float32),
                0.0,
            ).astype(jnp.bfloat16)
            ldq = lax.dot_general(dl, pg, (((1,), (1,)), ((), ())), preferred_element_type=jnp.float32)
            ldq = ldq + jnp.dot(bh, kg, preferred_element_type=jnp.float32)
            ldq_ref[:, cols] = ldq
            ldk = ldk + lax.dot_general(bh, qh, (((0,), (0,)), ((), ())), preferred_element_type=jnp.float32)
            dsp = dsp + lax.dot_general(lh, dl, (((0,), (0,)), ((), ())), preferred_element_type=jnp.float32)
        suffix_ref[g] = suffix
        ldk_ref[:, lanes] = ldk
        dsp_ref[:, lanes] = dsp


def in_vmem(count):
    return [pl.BlockSpec(memory_space=pltpu.VMEM)] * count


def per_device(queries, keys, values, spikes, window_lengths, gain, cotangent):
    token_rows = queries.shape[1]
    width = QUERY_HEADS * HEAD_SIZE
    reach = (WINDOW_REACH + token_rows - 2) // token_rows
    padding_rows = reach * token_rows
    window_rows = (reach + 1) * token_rows
    key_value_width = KEY_VALUE_HEADS * HEAD_SIZE
    q = queries[0]
    c = cotangent[0]
    k = keys[0]
    v = values[0]
    counts = jnp.repeat(spikes[0].astype(jnp.float32), HEAD_SIZE, axis=1)
    spiked = (v.astype(jnp.float32) * counts).astype(jnp.bfloat16)
    def state_of(block_keys, block_spiked):
        return jnp.stack(
            [
                lax.dot_general(
                    block_keys[:, g * HEAD_SIZE : (g + 1) * HEAD_SIZE],
                    block_spiked[:, g * HEAD_SIZE : (g + 1) * HEAD_SIZE],
                    (((0,), (0,)), ((), ())),
                    preferred_element_type=jnp.float32,
                )
                for g in range(KEY_VALUE_HEADS)
            ]
        )

    count_lanes = HEAD_SIZE
    spike_block = jnp.concatenate(
        [
            spikes[0].astype(jnp.bfloat16),
            jnp.zeros((token_rows, count_lanes - KEY_VALUE_HEADS), jnp.bfloat16),
        ],
        axis=1,
    )
    packed = jnp.concatenate([k, v, spike_block], axis=1)
    earlier = []
    for distance in range(reach, 0, -1):
        earlier.append(shifted(packed, "ctx", distance))
    near = jnp.zeros((KEY_VALUE_HEADS, HEAD_SIZE, HEAD_SIZE), jnp.float32)
    for piece in earlier:
        piece_counts = jnp.repeat(
            piece[:, 2 * key_value_width : 2 * key_value_width + KEY_VALUE_HEADS].astype(jnp.float32),
            HEAD_SIZE,
            axis=1,
        )
        piece_spiked = (
            piece[:, key_value_width : 2 * key_value_width].astype(jnp.float32) * piece_counts
        ).astype(jnp.bfloat16)
        near = near + state_of(piece[:, :key_value_width], piece_spiked)
    own_and_near = near + state_of(k, spiked)
    prior_half = spread_scan(near, own_and_near, "ctx").astype(jnp.bfloat16)
    window_packed = jnp.concatenate(
        [piece[:, : 2 * key_value_width] for piece in earlier] + [jnp.concatenate([k, v], axis=1)], axis=0
    )
    info = jnp.concatenate(
        [window_lengths.astype(jnp.int32), (lax.axis_index("ctx") * token_rows - padding_rows).reshape(1)]
    ).astype(jnp.int32)
    key_window = window_packed[:, :key_value_width]
    value_window = window_packed[:, key_value_width:]
    first_piece = window_call(0, info, q, c, key_window, value_window)
    gn, ldq, suffix_local, gain_local, ldk, dsp = pl.pallas_call(
        linear_kernel,
        out_shape=(
            jax.ShapeDtypeStruct((token_rows, width), jnp.float32),
            jax.ShapeDtypeStruct((token_rows, width), jnp.float32),
            jax.ShapeDtypeStruct((KEY_VALUE_HEADS, HEAD_SIZE, HEAD_SIZE), jnp.float32),
            jax.ShapeDtypeStruct((1, width), jnp.float32),
            jax.ShapeDtypeStruct((token_rows, key_value_width), jnp.float32),
            jax.ShapeDtypeStruct((token_rows, key_value_width), jnp.float32),
        ),
        in_specs=in_vmem(6),
        out_specs=tuple(in_vmem(6)),
        cost_estimate=pl.CostEstimate(
            flops=20 * QUERY_HEADS * token_rows * token_rows * HEAD_SIZE,
            transcendentals=QUERY_HEADS * token_rows,
            bytes_accessed=token_rows * width * (2 + 2 + 4 + 4) + 6 * token_rows * key_value_width * 4,
        ),
    )(q, c, k, spiked, prior_half, gain.reshape(1, width))
    total_tokens = queries.shape[0] * lax.axis_size("dp") * token_rows * lax.axis_size("ctx")
    state_rows = KEY_VALUE_HEADS * HEAD_SIZE
    gain_rows = width // HEAD_SIZE
    pad_rows = (-(state_rows + gain_rows)) % 8
    riding = jnp.concatenate(
        [
            suffix_local.reshape(state_rows, HEAD_SIZE),
            gain_local.reshape(gain_rows, HEAD_SIZE),
            jnp.zeros((pad_rows, HEAD_SIZE), jnp.float32),
        ],
        axis=0,
    )
    later_rows, total_rows, first_round = butterfly_scan(riding, "ctx", True)
    late_q, _ = lax.optimization_barrier((q, first_round))
    second_piece = window_call(1, info, late_q, c, key_window, value_window)
    pieces = (first_piece, second_piece)
    window_out = jnp.concatenate([piece[0] for piece in pieces], axis=1)
    window_dq = jnp.concatenate([piece[1] for piece in pieces], axis=1)
    dk_win = jnp.concatenate([piece[2] for piece in pieces], axis=1)
    dv_win = jnp.concatenate([piece[3] for piece in pieces], axis=1)
    mixed = (gn + window_out).astype(jnp.bfloat16)
    d_queries = (ldq + window_dq).astype(jnp.bfloat16)
    later_half = later_rows[:state_rows].reshape(suffix_local.shape).astype(jnp.bfloat16)
    gain_ctx = total_rows[state_rows : state_rows + gain_rows].reshape(width)
    d_gain = all_sum(gain_ctx, ("dp",)) * (total_tokens ** (-0.5))
    ldk_parts = []
    dsp_parts = []
    for g in range(KEY_VALUE_HEADS):
        lanes = slice(g * HEAD_SIZE, (g + 1) * HEAD_SIZE)
        ldk_parts.append(
            ldk[:, lanes]
            + lax.dot_general(
                spiked[:, lanes], later_half[g], (((1,), (1,)), ((), ())), preferred_element_type=jnp.float32
            )
        )
        dsp_parts.append(
            dsp[:, lanes] + jnp.dot(k[:, lanes], later_half[g], preferred_element_type=jnp.float32)
        )
    linear_key_gradient = jnp.concatenate(ldk_parts, axis=1)
    linear_value_gradient = jnp.concatenate(dsp_parts, axis=1) * counts
    received = jnp.zeros((token_rows, 2 * key_value_width), jnp.float32)
    for distance in range(1, reach + 1):
        start_row = (reach - distance) * token_rows
        sent = jnp.concatenate(
            [
                dk_win[start_row : start_row + token_rows],
                dv_win[start_row : start_row + token_rows],
            ],
            axis=1,
        )
        received = received + shifted(sent.astype(jnp.bfloat16), "ctx", -distance).astype(jnp.float32)
    keys_gradient = (
        linear_key_gradient + dk_win[padding_rows:] + received[:, :key_value_width]
    ).astype(jnp.bfloat16)
    values_gradient = (
        linear_value_gradient + dv_win[padding_rows:] + received[:, key_value_width:]
    ).astype(jnp.bfloat16)
    return (
        mixed[None],
        d_queries[None],
        keys_gradient[None],
        values_gradient[None],
        d_gain,
    )


def solution(mesh):
    placed = (
        P("dp", "ctx", None),
        P("dp", "ctx", None),
        P("dp", "ctx", None),
        P("dp", "ctx", None),
        P(),
        P(),
        P("dp", "ctx", None),
    )
    return jax.shard_map(
        per_device,
        mesh=mesh,
        in_specs=placed,
        out_specs=(
            P("dp", "ctx", None),
            P("dp", "ctx", None),
            P("dp", "ctx", None),
            P("dp", "ctx", None),
            P(),
        ),
        check_vma=False,
    )
```

```python
import jax
import jax.numpy as jnp
from jax import lax
from jax.experimental import pallas as pl
from jax.experimental.pallas import tpu as pltpu
from jax.sharding import PartitionSpec as P

QUERY_HEADS = 14
KEY_VALUE_HEADS = 2
HEAD_SIZE = 128
WINDOW_REACH = 256


epsilon = 1e-05


def exclusive_scan(part, axis, reverse):
    count = lax.axis_size(axis)
    running = part
    total = None
    distance = 1
    while distance < count:
        if reverse:
            route = [(i + distance, i) for i in range(count - distance)]
        else:
            route = [(i, i + distance) for i in range(count - distance)]
        got = lax.ppermute(running, axis, route)
        total = got if total is None else total + got
        if distance * 2 < count:
            running = running + got
        distance *= 2
    if total is None:
        total = jnp.zeros_like(part)
    return total


def butterfly_scan(part, axis, reverse):
    count = lax.axis_size(axis)
    place = lax.axis_index(axis)
    group = part
    before = jnp.zeros_like(part)
    step = 1
    while step < count:
        mine = group.astype(jnp.bfloat16)
        got = lax.ppermute(mine, axis, [(i, i ^ step) for i in range(count)]).astype(jnp.float32)
        partner = jnp.bitwise_xor(place, step)
        take = partner > place if reverse else partner < place
        before = before + jnp.where(take, got, 0.0)
        group = mine.astype(jnp.float32) + got
        step *= 2
    return before, group


def spread_scan(near, own, axis):
    count = lax.axis_size(axis)
    total = near
    running = own
    stride = 3
    while stride < count:
        parts = []
        for distance in (stride, 2 * stride):
            if distance < count:
                parts.append(shifted(running, axis, distance))
        for got in parts:
            total = total + got
        if 3 * stride < count:
            for got in parts:
                running = running + got
        stride *= 3
    return total


def all_sum(part, axes):
    count = 1
    for axis in axes:
        count *= lax.axis_size(axis)
    step = 1
    while step < count:
        route = [(i, i ^ step) for i in range(count)]
        part = part + lax.ppermute(part, axes, route)
        step *= 2
    return part


def shifted(block, axis, distance):
    devices = range(lax.axis_size(axis))
    route = [(i - distance, i) for i in devices if i - distance in devices]
    return lax.ppermute(block, axis, route)


def window_kernel(info_ref, q_ref, c_ref, k_ref, v_ref, wout_ref, wdq_ref, dk_ref, dv_ref):
    group_size = QUERY_HEADS // KEY_VALUE_HEADS
    token_rows = q_ref.shape[0]
    window_rows = k_ref.shape[0]
    padding_rows = window_rows - token_rows
    scale = HEAD_SIZE ** (-0.5)
    row = lax.broadcasted_iota(jnp.int32, (token_rows, window_rows), 0)
    col = lax.broadcasted_iota(jnp.int32, (token_rows, window_rows), 1)
    back = row + padding_rows - col
    seen = (back >= 0) & (col + info_ref[2] >= 0)
    for g in range(KEY_VALUE_HEADS):
        visible = seen & (back < info_ref[g])
        lanes = slice(g * HEAD_SIZE, (g + 1) * HEAD_SIZE)
        kg = k_ref[:, lanes]
        vg = v_ref[:, lanes]
        dk = jnp.zeros((window_rows, HEAD_SIZE), jnp.float32)
        dv = jnp.zeros((window_rows, HEAD_SIZE), jnp.float32)
        for h in range(group_size):
            cols = slice((g * group_size + h) * HEAD_SIZE, (g * group_size + h + 1) * HEAD_SIZE)
            qh = q_ref[:, cols]
            ch = c_ref[:, cols]
            s = lax.dot_general(qh, kg, (((1,), (1,)), ((), ())), preferred_element_type=jnp.float32) * scale
            s = jnp.where(visible, s, -1e30)
            top = jnp.max(s, axis=-1, keepdims=True)
            e = jnp.exp(s - top)
            p = e * (1.0 / jnp.sum(e, axis=-1, keepdims=True))
            ph = p.astype(jnp.bfloat16)
            wout = jnp.dot(ph, vg, preferred_element_type=jnp.float32)
            wout_ref[:, cols] = wout
            gp = lax.dot_general(ch, vg, (((1,), (1,)), ((), ())), preferred_element_type=jnp.float32)
            delta = jnp.sum(ch.astype(jnp.float32) * wout, axis=-1, keepdims=True)
            ds = (p * (gp - delta) * scale).astype(jnp.bfloat16)
            wdq_ref[:, cols] = jnp.dot(ds, kg, preferred_element_type=jnp.float32)
            dk = dk + lax.dot_general(ds, qh, (((0,), (0,)), ((), ())), preferred_element_type=jnp.float32)
            dv = dv + lax.dot_general(ph, ch, (((0,), (0,)), ((), ())), preferred_element_type=jnp.float32)
        dk_ref[:, lanes] = dk
        dv_ref[:, lanes] = dv


def linear_kernel(q_ref, c_ref, k_ref, s_ref, prior_ref, gain_ref, wout_ref, wdq_ref,
                  mixed_ref, dq_ref, suffix_ref, gsum_ref, ldk_ref, dsp_ref):
    group_size = QUERY_HEADS // KEY_VALUE_HEADS
    token_rows = q_ref.shape[0]
    row = lax.broadcasted_iota(jnp.int32, (token_rows, token_rows), 0)
    col = lax.broadcasted_iota(jnp.int32, (token_rows, token_rows), 1)
    causal = row >= col
    for g in range(KEY_VALUE_HEADS):
        lanes = slice(g * HEAD_SIZE, (g + 1) * HEAD_SIZE)
        kg = k_ref[:, lanes]
        sg = s_ref[:, lanes]
        pg = prior_ref[g]
        suffix = jnp.zeros((HEAD_SIZE, HEAD_SIZE), jnp.float32)
        ldk = jnp.zeros((token_rows, HEAD_SIZE), jnp.float32)
        dsp = jnp.zeros((token_rows, HEAD_SIZE), jnp.float32)
        for h in range(group_size):
            cols = slice((g * group_size + h) * HEAD_SIZE, (g * group_size + h + 1) * HEAD_SIZE)
            qh = q_ref[:, cols]
            ch = c_ref[:, cols].astype(jnp.float32)
            gh = gain_ref[:, cols]
            lh = jnp.where(
                causal,
                lax.dot_general(qh, kg, (((1,), (1,)), ((), ())), preferred_element_type=jnp.float32),
                0.0,
            ).astype(jnp.bfloat16)
            lin = jnp.dot(lh, sg, preferred_element_type=jnp.float32) + jnp.dot(
                qh, pg, preferred_element_type=jnp.float32
            )
            inverse_root = 1.0 / jnp.sqrt(jnp.mean(lin * lin, axis=-1, keepdims=True) + epsilon)
            normed = lin * inverse_root
            mixed_ref[:, cols] = (gh * normed + wout_ref[:, cols]).astype(mixed_ref.dtype)
            gsum_ref[:, cols] = jnp.sum(ch * normed, axis=0, keepdims=True)
            scaled = ch * gh
            dl = ((scaled - normed * jnp.mean(scaled * normed, axis=-1, keepdims=True)) * inverse_root).astype(
                jnp.bfloat16
            )
            suffix = suffix + lax.dot_general(qh, dl, (((0,), (0,)), ((), ())), preferred_element_type=jnp.float32)
            bh = jnp.where(
                causal,
                lax.dot_general(dl, sg, (((1,), (1,)), ((), ())), preferred_element_type=jnp.float32),
                0.0,
            ).astype(jnp.bfloat16)
            ldq = lax.dot_general(dl, pg, (((1,), (1,)), ((), ())), preferred_element_type=jnp.float32)
            ldq = ldq + jnp.dot(bh, kg, preferred_element_type=jnp.float32)
            dq_ref[:, cols] = (ldq + wdq_ref[:, cols]).astype(dq_ref.dtype)
            ldk = ldk + lax.dot_general(bh, qh, (((0,), (0,)), ((), ())), preferred_element_type=jnp.float32)
            dsp = dsp + lax.dot_general(lh, dl, (((0,), (0,)), ((), ())), preferred_element_type=jnp.float32)
        suffix_ref[g] = suffix
        ldk_ref[:, lanes] = ldk
        dsp_ref[:, lanes] = dsp


def in_vmem(count):
    return [pl.BlockSpec(memory_space=pltpu.VMEM)] * count


def per_device(queries, keys, values, spikes, window_lengths, gain, cotangent):
    token_rows = queries.shape[1]
    width = QUERY_HEADS * HEAD_SIZE
    reach = (WINDOW_REACH + token_rows - 2) // token_rows
    padding_rows = reach * token_rows
    window_rows = (reach + 1) * token_rows
    key_value_width = KEY_VALUE_HEADS * HEAD_SIZE
    q = queries[0]
    c = cotangent[0]
    k = keys[0]
    v = values[0]
    counts = jnp.repeat(spikes[0].astype(jnp.float32), HEAD_SIZE, axis=1)
    spiked = (v.astype(jnp.float32) * counts).astype(jnp.bfloat16)
    def state_of(block_keys, block_spiked):
        return jnp.stack(
            [
                lax.dot_general(
                    block_keys[:, g * HEAD_SIZE : (g + 1) * HEAD_SIZE],
                    block_spiked[:, g * HEAD_SIZE : (g + 1) * HEAD_SIZE],
                    (((0,), (0,)), ((), ())),
                    preferred_element_type=jnp.float32,
                )
                for g in range(KEY_VALUE_HEADS)
            ]
        )

    count_lanes = HEAD_SIZE
    spike_block = jnp.concatenate(
        [
            spikes[0].astype(jnp.bfloat16),
            jnp.zeros((token_rows, count_lanes - KEY_VALUE_HEADS), jnp.bfloat16),
        ],
        axis=1,
    )
    packed = jnp.concatenate([k, v, spike_block], axis=1)
    earlier = []
    for distance in range(reach, 0, -1):
        earlier.append(shifted(packed, "ctx", distance))
    near = jnp.zeros((KEY_VALUE_HEADS, HEAD_SIZE, HEAD_SIZE), jnp.float32)
    for piece in earlier:
        piece_counts = jnp.repeat(
            piece[:, 2 * key_value_width : 2 * key_value_width + KEY_VALUE_HEADS].astype(jnp.float32),
            HEAD_SIZE,
            axis=1,
        )
        piece_spiked = (
            piece[:, key_value_width : 2 * key_value_width].astype(jnp.float32) * piece_counts
        ).astype(jnp.bfloat16)
        near = near + state_of(piece[:, :key_value_width], piece_spiked)
    own_and_near = near + state_of(k, spiked)
    prior_half = spread_scan(near, own_and_near, "ctx").astype(jnp.bfloat16)
    window_packed = jnp.concatenate(
        [piece[:, : 2 * key_value_width] for piece in earlier] + [jnp.concatenate([k, v], axis=1)], axis=0
    )
    info = jnp.concatenate(
        [window_lengths.astype(jnp.int32), (lax.axis_index("ctx") * token_rows - padding_rows).reshape(1)]
    ).astype(jnp.int32)
    wout, wdq, dk_win, dv_win = pl.pallas_call(
        window_kernel,
        out_shape=(
            jax.ShapeDtypeStruct((token_rows, width), jnp.float32),
            jax.ShapeDtypeStruct((token_rows, width), jnp.float32),
            jax.ShapeDtypeStruct((window_rows, key_value_width), jnp.float32),
            jax.ShapeDtypeStruct((window_rows, key_value_width), jnp.float32),
        ),
        in_specs=[pl.BlockSpec(memory_space=pltpu.SMEM)] + in_vmem(4),
        out_specs=tuple(in_vmem(4)),
        cost_estimate=pl.CostEstimate(
            flops=12 * QUERY_HEADS * token_rows * window_rows * HEAD_SIZE,
            transcendentals=QUERY_HEADS * token_rows * window_rows,
            bytes_accessed=2 * token_rows * width * (2 + 4) + 2 * window_rows * key_value_width * (2 + 4),
        ),
    )(info, q, c, window_packed[:, :key_value_width], window_packed[:, key_value_width:])
    mixed, d_queries, suffix_local, gain_local, ldk, dsp = pl.pallas_call(
        linear_kernel,
        out_shape=(
            jax.ShapeDtypeStruct((token_rows, width), jnp.bfloat16),
            jax.ShapeDtypeStruct((token_rows, width), jnp.bfloat16),
            jax.ShapeDtypeStruct((KEY_VALUE_HEADS, HEAD_SIZE, HEAD_SIZE), jnp.float32),
            jax.ShapeDtypeStruct((1, width), jnp.float32),
            jax.ShapeDtypeStruct((token_rows, key_value_width), jnp.float32),
            jax.ShapeDtypeStruct((token_rows, key_value_width), jnp.float32),
        ),
        in_specs=in_vmem(8),
        out_specs=tuple(in_vmem(6)),
        cost_estimate=pl.CostEstimate(
            flops=20 * QUERY_HEADS * token_rows * token_rows * HEAD_SIZE,
            transcendentals=QUERY_HEADS * token_rows,
            bytes_accessed=token_rows * width * (2 + 2 + 4 + 4 + 2 + 2) + 6 * token_rows * key_value_width * 4,
        ),
    )(q, c, k, spiked, prior_half, gain.reshape(1, width), wout, wdq)
    total_tokens = queries.shape[0] * lax.axis_size("dp") * token_rows * lax.axis_size("ctx")
    state_rows = KEY_VALUE_HEADS * HEAD_SIZE
    gain_rows = width // HEAD_SIZE
    pad_rows = (-(state_rows + gain_rows)) % 8
    riding = jnp.concatenate(
        [
            suffix_local.reshape(state_rows, HEAD_SIZE),
            gain_local.reshape(gain_rows, HEAD_SIZE),
            jnp.zeros((pad_rows, HEAD_SIZE), jnp.float32),
        ],
        axis=0,
    )
    later_rows, total_rows = butterfly_scan(riding, "ctx", True)
    later_half = later_rows[:state_rows].reshape(suffix_local.shape).astype(jnp.bfloat16)
    gain_ctx = total_rows[state_rows : state_rows + gain_rows].reshape(width)
    d_gain = all_sum(gain_ctx, ("dp",)) * (total_tokens ** (-0.5))
    ldk_parts = []
    dsp_parts = []
    for g in range(KEY_VALUE_HEADS):
        lanes = slice(g * HEAD_SIZE, (g + 1) * HEAD_SIZE)
        ldk_parts.append(
            ldk[:, lanes]
            + lax.dot_general(
                spiked[:, lanes], later_half[g], (((1,), (1,)), ((), ())), preferred_element_type=jnp.float32
            )
        )
        dsp_parts.append(
            dsp[:, lanes] + jnp.dot(k[:, lanes], later_half[g], preferred_element_type=jnp.float32)
        )
    linear_key_gradient = jnp.concatenate(ldk_parts, axis=1)
    linear_value_gradient = jnp.concatenate(dsp_parts, axis=1) * counts
    received = jnp.zeros((token_rows, 2 * key_value_width), jnp.float32)
    for distance in range(1, reach + 1):
        start_row = (reach - distance) * token_rows
        sent = jnp.concatenate(
            [
                dk_win[start_row : start_row + token_rows],
                dv_win[start_row : start_row + token_rows],
            ],
            axis=1,
        )
        received = received + shifted(sent.astype(jnp.bfloat16), "ctx", -distance).astype(jnp.float32)
    keys_gradient = (
        linear_key_gradient + dk_win[padding_rows:] + received[:, :key_value_width]
    ).astype(jnp.bfloat16)
    values_gradient = (
        linear_value_gradient + dv_win[padding_rows:] + received[:, key_value_width:]
    ).astype(jnp.bfloat16)
    return (
        mixed[None],
        d_queries[None],
        keys_gradient[None],
        values_gradient[None],
        d_gain,
    )


def solution(mesh):
    placed = (
        P("dp", "ctx", None),
        P("dp", "ctx", None),
        P("dp", "ctx", None),
        P("dp", "ctx", None),
        P(),
        P(),
        P("dp", "ctx", None),
    )
    return jax.shard_map(
        per_device,
        mesh=mesh,
        in_specs=placed,
        out_specs=(
            P("dp", "ctx", None),
            P("dp", "ctx", None),
            P("dp", "ctx", None),
            P("dp", "ctx", None),
            P(),
        ),
        check_vma=False,
    )
```

```python
import jax
import jax.numpy as jnp
from jax import lax
from jax.experimental import pallas as pl
from jax.experimental.pallas import tpu as pltpu
from jax.sharding import PartitionSpec as P

QUERY_HEADS = 14
KEY_VALUE_HEADS = 2
HEAD_SIZE = 128
WINDOW_REACH = 256


epsilon = 1e-05


def exclusive_scan(part, axis, reverse):
    count = lax.axis_size(axis)
    running = part
    total = None
    distance = 1
    while distance < count:
        if reverse:
            route = [(i + distance, i) for i in range(count - distance)]
        else:
            route = [(i, i + distance) for i in range(count - distance)]
        got = lax.ppermute(running, axis, route)
        total = got if total is None else total + got
        if distance * 2 < count:
            running = running + got
        distance *= 2
    if total is None:
        total = jnp.zeros_like(part)
    return total


def butterfly_scan(part, axis, reverse):
    count = lax.axis_size(axis)
    place = lax.axis_index(axis)
    group = part
    before = jnp.zeros_like(part)
    step = 1
    while step < count:
        mine = group.astype(jnp.bfloat16)
        got = lax.ppermute(mine, axis, [(i, i ^ step) for i in range(count)]).astype(jnp.float32)
        partner = jnp.bitwise_xor(place, step)
        take = partner > place if reverse else partner < place
        before = before + jnp.where(take, got, 0.0)
        group = mine.astype(jnp.float32) + got
        step *= 2
    return before, group


def spread_scan(near, own, axis):
    count = lax.axis_size(axis)
    total = near
    running = own
    stride = 3
    while stride < count:
        parts = []
        for distance in (stride, 2 * stride):
            if distance < count:
                parts.append(shifted(running, axis, distance))
        for got in parts:
            total = total + got
        if 3 * stride < count:
            for got in parts:
                running = running + got
        stride *= 3
    return total


def all_sum(part, axis):
    count = lax.axis_size(axis)
    place = lax.axis_index(axis)
    span = 1
    while span < count:
        width = min(4, count // span)
        members = [part] + [
            lax.ppermute(part, axis, [(i, i ^ (m * span)) for i in range(count)]) for m in range(1, width)
        ]
        stacked = jnp.stack(members)
        digit = (place // span) % width
        total = None
        for j in range(width):
            value = lax.dynamic_index_in_dim(stacked, jnp.bitwise_xor(digit, j), 0, False)
            total = value if total is None else total + value
        part = total
        span *= width
    return part


def shifted(block, axis, distance):
    devices = range(lax.axis_size(axis))
    route = [(i - distance, i) for i in devices if i - distance in devices]
    return lax.ppermute(block, axis, route)


def window_kernel(info_ref, q_ref, c_ref, k_ref, v_ref, wout_ref, wdq_ref, dk_ref, dv_ref):
    group_size = QUERY_HEADS // KEY_VALUE_HEADS
    token_rows = q_ref.shape[0]
    window_rows = k_ref.shape[0]
    padding_rows = window_rows - token_rows
    scale = HEAD_SIZE ** (-0.5)
    row = lax.broadcasted_iota(jnp.int32, (token_rows, window_rows), 0)
    col = lax.broadcasted_iota(jnp.int32, (token_rows, window_rows), 1)
    back = row + padding_rows - col
    seen = (back >= 0) & (col + info_ref[2] >= 0)
    for g in range(KEY_VALUE_HEADS):
        visible = seen & (back < info_ref[g])
        lanes = slice(g * HEAD_SIZE, (g + 1) * HEAD_SIZE)
        kg = k_ref[:, lanes]
        vg = v_ref[:, lanes]
        dk = jnp.zeros((window_rows, HEAD_SIZE), jnp.float32)
        dv = jnp.zeros((window_rows, HEAD_SIZE), jnp.float32)
        for h in range(group_size):
            cols = slice((g * group_size + h) * HEAD_SIZE, (g * group_size + h + 1) * HEAD_SIZE)
            qh = q_ref[:, cols]
            ch = c_ref[:, cols]
            s = lax.dot_general(qh, kg, (((1,), (1,)), ((), ())), preferred_element_type=jnp.float32) * scale
            s = jnp.where(visible, s, -1e30)
            top = jnp.max(s, axis=-1, keepdims=True)
            e = jnp.exp(s - top)
            p = e * (1.0 / jnp.sum(e, axis=-1, keepdims=True))
            ph = p.astype(jnp.bfloat16)
            wout = jnp.dot(ph, vg, preferred_element_type=jnp.float32)
            wout_ref[:, cols] = wout
            gp = lax.dot_general(ch, vg, (((1,), (1,)), ((), ())), preferred_element_type=jnp.float32)
            delta = jnp.sum(ch.astype(jnp.float32) * wout, axis=-1, keepdims=True)
            ds = (p * (gp - delta) * scale).astype(jnp.bfloat16)
            wdq_ref[:, cols] = jnp.dot(ds, kg, preferred_element_type=jnp.float32)
            dk = dk + lax.dot_general(ds, qh, (((0,), (0,)), ((), ())), preferred_element_type=jnp.float32)
            dv = dv + lax.dot_general(ph, ch, (((0,), (0,)), ((), ())), preferred_element_type=jnp.float32)
        dk_ref[:, lanes] = dk
        dv_ref[:, lanes] = dv


def linear_kernel(q_ref, c_ref, k_ref, s_ref, prior_ref, gain_ref, wout_ref, wdq_ref,
                  mixed_ref, dq_ref, suffix_ref, gsum_ref, ldk_ref, dsp_ref):
    group_size = QUERY_HEADS // KEY_VALUE_HEADS
    token_rows = q_ref.shape[0]
    row = lax.broadcasted_iota(jnp.int32, (token_rows, token_rows), 0)
    col = lax.broadcasted_iota(jnp.int32, (token_rows, token_rows), 1)
    causal = row >= col
    for g in range(KEY_VALUE_HEADS):
        lanes = slice(g * HEAD_SIZE, (g + 1) * HEAD_SIZE)
        kg = k_ref[:, lanes]
        sg = s_ref[:, lanes]
        pg = prior_ref[g]
        suffix = jnp.zeros((HEAD_SIZE, HEAD_SIZE), jnp.float32)
        ldk = jnp.zeros((token_rows, HEAD_SIZE), jnp.float32)
        dsp = jnp.zeros((token_rows, HEAD_SIZE), jnp.float32)
        for h in range(group_size):
            cols = slice((g * group_size + h) * HEAD_SIZE, (g * group_size + h + 1) * HEAD_SIZE)
            qh = q_ref[:, cols]
            ch = c_ref[:, cols].astype(jnp.float32)
            gh = gain_ref[:, cols]
            lh = jnp.where(
                causal,
                lax.dot_general(qh, kg, (((1,), (1,)), ((), ())), preferred_element_type=jnp.float32),
                0.0,
            ).astype(jnp.bfloat16)
            lin = jnp.dot(lh, sg, preferred_element_type=jnp.float32) + jnp.dot(
                qh, pg, preferred_element_type=jnp.float32
            )
            inverse_root = 1.0 / jnp.sqrt(jnp.mean(lin * lin, axis=-1, keepdims=True) + epsilon)
            normed = lin * inverse_root
            mixed_ref[:, cols] = (gh * normed + wout_ref[:, cols]).astype(mixed_ref.dtype)
            gsum_ref[:, cols] = jnp.sum(ch * normed, axis=0, keepdims=True)
            scaled = ch * gh
            dl = ((scaled - normed * jnp.mean(scaled * normed, axis=-1, keepdims=True)) * inverse_root).astype(
                jnp.bfloat16
            )
            suffix = suffix + lax.dot_general(qh, dl, (((0,), (0,)), ((), ())), preferred_element_type=jnp.float32)
            bh = jnp.where(
                causal,
                lax.dot_general(dl, sg, (((1,), (1,)), ((), ())), preferred_element_type=jnp.float32),
                0.0,
            ).astype(jnp.bfloat16)
            ldq = lax.dot_general(dl, pg, (((1,), (1,)), ((), ())), preferred_element_type=jnp.float32)
            ldq = ldq + jnp.dot(bh, kg, preferred_element_type=jnp.float32)
            dq_ref[:, cols] = (ldq + wdq_ref[:, cols]).astype(dq_ref.dtype)
            ldk = ldk + lax.dot_general(bh, qh, (((0,), (0,)), ((), ())), preferred_element_type=jnp.float32)
            dsp = dsp + lax.dot_general(lh, dl, (((0,), (0,)), ((), ())), preferred_element_type=jnp.float32)
        suffix_ref[g] = suffix
        ldk_ref[:, lanes] = ldk
        dsp_ref[:, lanes] = dsp


def in_vmem(count):
    return [pl.BlockSpec(memory_space=pltpu.VMEM)] * count


def per_device(queries, keys, values, spikes, window_lengths, gain, cotangent):
    token_rows = queries.shape[1]
    width = QUERY_HEADS * HEAD_SIZE
    reach = (WINDOW_REACH + token_rows - 2) // token_rows
    padding_rows = reach * token_rows
    window_rows = (reach + 1) * token_rows
    key_value_width = KEY_VALUE_HEADS * HEAD_SIZE
    q = queries[0]
    c = cotangent[0]
    k = keys[0]
    v = values[0]
    counts = jnp.repeat(spikes[0].astype(jnp.float32), HEAD_SIZE, axis=1)
    spiked = (v.astype(jnp.float32) * counts).astype(jnp.bfloat16)
    def state_of(block_keys, block_spiked):
        return jnp.stack(
            [
                lax.dot_general(
                    block_keys[:, g * HEAD_SIZE : (g + 1) * HEAD_SIZE],
                    block_spiked[:, g * HEAD_SIZE : (g + 1) * HEAD_SIZE],
                    (((0,), (0,)), ((), ())),
                    preferred_element_type=jnp.float32,
                )
                for g in range(KEY_VALUE_HEADS)
            ]
        )

    count_lanes = HEAD_SIZE
    spike_block = jnp.concatenate(
        [
            spikes[0].astype(jnp.bfloat16),
            jnp.zeros((token_rows, count_lanes - KEY_VALUE_HEADS), jnp.bfloat16),
        ],
        axis=1,
    )
    packed = jnp.concatenate([k, v, spike_block], axis=1)
    earlier = []
    for distance in range(reach, 0, -1):
        earlier.append(shifted(packed, "ctx", distance))
    near = jnp.zeros((KEY_VALUE_HEADS, HEAD_SIZE, HEAD_SIZE), jnp.float32)
    for piece in earlier:
        piece_counts = jnp.repeat(
            piece[:, 2 * key_value_width : 2 * key_value_width + KEY_VALUE_HEADS].astype(jnp.float32),
            HEAD_SIZE,
            axis=1,
        )
        piece_spiked = (
            piece[:, key_value_width : 2 * key_value_width].astype(jnp.float32) * piece_counts
        ).astype(jnp.bfloat16)
        near = near + state_of(piece[:, :key_value_width], piece_spiked)
    own_and_near = near + state_of(k, spiked)
    prior_half = spread_scan(near, own_and_near, "ctx").astype(jnp.bfloat16)
    window_packed = jnp.concatenate(
        [piece[:, : 2 * key_value_width] for piece in earlier] + [jnp.concatenate([k, v], axis=1)], axis=0
    )
    info = jnp.concatenate(
        [window_lengths.astype(jnp.int32), (lax.axis_index("ctx") * token_rows - padding_rows).reshape(1)]
    ).astype(jnp.int32)
    wout, wdq, dk_win, dv_win = pl.pallas_call(
        window_kernel,
        out_shape=(
            jax.ShapeDtypeStruct((token_rows, width), jnp.float32),
            jax.ShapeDtypeStruct((token_rows, width), jnp.float32),
            jax.ShapeDtypeStruct((window_rows, key_value_width), jnp.float32),
            jax.ShapeDtypeStruct((window_rows, key_value_width), jnp.float32),
        ),
        in_specs=[pl.BlockSpec(memory_space=pltpu.SMEM)] + in_vmem(4),
        out_specs=tuple(in_vmem(4)),
        cost_estimate=pl.CostEstimate(
            flops=12 * QUERY_HEADS * token_rows * window_rows * HEAD_SIZE,
            transcendentals=QUERY_HEADS * token_rows * window_rows,
            bytes_accessed=2 * token_rows * width * (2 + 4) + 2 * window_rows * key_value_width * (2 + 4),
        ),
    )(info, q, c, window_packed[:, :key_value_width], window_packed[:, key_value_width:])
    mixed, d_queries, suffix_local, gain_local, ldk, dsp = pl.pallas_call(
        linear_kernel,
        out_shape=(
            jax.ShapeDtypeStruct((token_rows, width), jnp.bfloat16),
            jax.ShapeDtypeStruct((token_rows, width), jnp.bfloat16),
            jax.ShapeDtypeStruct((KEY_VALUE_HEADS, HEAD_SIZE, HEAD_SIZE), jnp.float32),
            jax.ShapeDtypeStruct((1, width), jnp.float32),
            jax.ShapeDtypeStruct((token_rows, key_value_width), jnp.float32),
            jax.ShapeDtypeStruct((token_rows, key_value_width), jnp.float32),
        ),
        in_specs=in_vmem(8),
        out_specs=tuple(in_vmem(6)),
        cost_estimate=pl.CostEstimate(
            flops=20 * QUERY_HEADS * token_rows * token_rows * HEAD_SIZE,
            transcendentals=QUERY_HEADS * token_rows,
            bytes_accessed=token_rows * width * (2 + 2 + 4 + 4 + 2 + 2) + 6 * token_rows * key_value_width * 4,
        ),
    )(q, c, k, spiked, prior_half, gain.reshape(1, width), wout, wdq)
    total_tokens = queries.shape[0] * lax.axis_size("dp") * token_rows * lax.axis_size("ctx")
    state_rows = KEY_VALUE_HEADS * HEAD_SIZE
    gain_rows = width // HEAD_SIZE
    pad_rows = (-(state_rows + gain_rows)) % 8
    riding = jnp.concatenate(
        [
            suffix_local.reshape(state_rows, HEAD_SIZE),
            gain_local.reshape(gain_rows, HEAD_SIZE),
            jnp.zeros((pad_rows, HEAD_SIZE), jnp.float32),
        ],
        axis=0,
    )
    later_rows, total_rows = butterfly_scan(riding, "ctx", True)
    later_half = later_rows[:state_rows].reshape(suffix_local.shape).astype(jnp.bfloat16)
    gain_ctx = total_rows[state_rows : state_rows + gain_rows].reshape(width)
    d_gain = all_sum(gain_ctx, "dp") * (total_tokens ** (-0.5))
    ldk_parts = []
    dsp_parts = []
    for g in range(KEY_VALUE_HEADS):
        lanes = slice(g * HEAD_SIZE, (g + 1) * HEAD_SIZE)
        ldk_parts.append(
            ldk[:, lanes]
            + lax.dot_general(
                spiked[:, lanes], later_half[g], (((1,), (1,)), ((), ())), preferred_element_type=jnp.float32
            )
        )
        dsp_parts.append(
            dsp[:, lanes] + jnp.dot(k[:, lanes], later_half[g], preferred_element_type=jnp.float32)
        )
    linear_key_gradient = jnp.concatenate(ldk_parts, axis=1)
    linear_value_gradient = jnp.concatenate(dsp_parts, axis=1) * counts
    received = jnp.zeros((token_rows, 2 * key_value_width), jnp.float32)
    for distance in range(1, reach + 1):
        start_row = (reach - distance) * token_rows
        sent = jnp.concatenate(
            [
                dk_win[start_row : start_row + token_rows],
                dv_win[start_row : start_row + token_rows],
            ],
            axis=1,
        )
        received = received + shifted(sent.astype(jnp.bfloat16), "ctx", -distance).astype(jnp.float32)
    keys_gradient = (
        linear_key_gradient + dk_win[padding_rows:] + received[:, :key_value_width]
    ).astype(jnp.bfloat16)
    values_gradient = (
        linear_value_gradient + dv_win[padding_rows:] + received[:, key_value_width:]
    ).astype(jnp.bfloat16)
    return (
        mixed[None],
        d_queries[None],
        keys_gradient[None],
        values_gradient[None],
        d_gain,
    )


def solution(mesh):
    placed = (
        P("dp", "ctx", None),
        P("dp", "ctx", None),
        P("dp", "ctx", None),
        P("dp", "ctx", None),
        P(),
        P(),
        P("dp", "ctx", None),
    )
    return jax.shard_map(
        per_device,
        mesh=mesh,
        in_specs=placed,
        out_specs=(
            P("dp", "ctx", None),
            P("dp", "ctx", None),
            P("dp", "ctx", None),
            P("dp", "ctx", None),
            P(),
        ),
        check_vma=False,
    )
```

```python
import jax
import jax.numpy as jnp
from jax import lax
from jax.experimental import pallas as pl
from jax.experimental.pallas import tpu as pltpu
from jax.sharding import PartitionSpec as P

QUERY_HEADS = 14
KEY_VALUE_HEADS = 2
HEAD_SIZE = 128
WINDOW_REACH = 256


epsilon = 1e-05


def exclusive_scan(part, axis, reverse):
    count = lax.axis_size(axis)
    running = part
    total = None
    distance = 1
    while distance < count:
        if reverse:
            route = [(i + distance, i) for i in range(count - distance)]
        else:
            route = [(i, i + distance) for i in range(count - distance)]
        got = lax.ppermute(running, axis, route)
        total = got if total is None else total + got
        if distance * 2 < count:
            running = running + got
        distance *= 2
    if total is None:
        total = jnp.zeros_like(part)
    return total


def butterfly_scan(part, axis, reverse):
    count = lax.axis_size(axis)
    place = lax.axis_index(axis)
    group = part
    before = jnp.zeros_like(part)
    step = 1
    while step < count:
        mine = group.astype(jnp.bfloat16)
        got = lax.ppermute(mine, axis, [(i, i ^ step) for i in range(count)]).astype(jnp.float32)
        partner = jnp.bitwise_xor(place, step)
        take = partner > place if reverse else partner < place
        before = before + jnp.where(take, got, 0.0)
        group = mine.astype(jnp.float32) + got
        step *= 2
    return before, group


def spread_scan(near, own, axis):
    count = lax.axis_size(axis)
    total = near
    running = own
    stride = 3
    while stride < count:
        parts = []
        for distance in (stride, 2 * stride):
            if distance < count:
                parts.append(shifted(running, axis, distance))
        for got in parts:
            total = total + got
        if 3 * stride < count:
            for got in parts:
                running = running + got
        stride *= 3
    return total


def all_sum(part, axes):
    count = 1
    for axis in axes:
        count *= lax.axis_size(axis)
    step = 1
    while step < count:
        route = [(i, i ^ step) for i in range(count)]
        part = part + lax.ppermute(part, axes, route)
        step *= 2
    return part


def shifted(block, axis, distance):
    devices = range(lax.axis_size(axis))
    route = [(i - distance, i) for i in devices if i - distance in devices]
    return lax.ppermute(block, axis, route)


def stacked_heads(ref, group, group_size):
    return jnp.concatenate(
        [ref[:, (group * group_size + h) * HEAD_SIZE : (group * group_size + h + 1) * HEAD_SIZE] for h in range(group_size)],
        axis=0,
    )


def window_kernel(info_ref, q_ref, c_ref, k_ref, v_ref, wout_ref, wdq_ref, dk_ref, dv_ref):
    group_size = QUERY_HEADS // KEY_VALUE_HEADS
    token_rows = q_ref.shape[0]
    window_rows = k_ref.shape[0]
    padding_rows = window_rows - token_rows
    scale = HEAD_SIZE ** (-0.5)
    stacked_rows = group_size * token_rows
    row = lax.broadcasted_iota(jnp.int32, (stacked_rows, window_rows), 0) % token_rows
    col = lax.broadcasted_iota(jnp.int32, (stacked_rows, window_rows), 1)
    back = row + padding_rows - col
    seen = (back >= 0) & (col + info_ref[2] >= 0)
    for g in range(KEY_VALUE_HEADS):
        visible = seen & (back < info_ref[g])
        lanes = slice(g * HEAD_SIZE, (g + 1) * HEAD_SIZE)
        kg = k_ref[:, lanes]
        vg = v_ref[:, lanes]
        qs = stacked_heads(q_ref, g, group_size)
        cs = stacked_heads(c_ref, g, group_size)
        s = lax.dot_general(qs, kg, (((1,), (1,)), ((), ())), preferred_element_type=jnp.float32) * scale
        s = jnp.where(visible, s, -1e30)
        top = jnp.max(s, axis=-1, keepdims=True)
        e = jnp.exp(s - top)
        p = e * (1.0 / jnp.sum(e, axis=-1, keepdims=True))
        ph = p.astype(jnp.bfloat16)
        wout = jnp.dot(ph, vg, preferred_element_type=jnp.float32)
        gp = lax.dot_general(cs, vg, (((1,), (1,)), ((), ())), preferred_element_type=jnp.float32)
        delta = jnp.sum(cs.astype(jnp.float32) * wout, axis=-1, keepdims=True)
        ds = (p * (gp - delta) * scale).astype(jnp.bfloat16)
        wdq = jnp.dot(ds, kg, preferred_element_type=jnp.float32)
        for h in range(group_size):
            cols = slice((g * group_size + h) * HEAD_SIZE, (g * group_size + h + 1) * HEAD_SIZE)
            rows = slice(h * token_rows, (h + 1) * token_rows)
            wout_ref[:, cols] = wout[rows]
            wdq_ref[:, cols] = wdq[rows]
        dk_ref[:, lanes] = lax.dot_general(ds, qs, (((0,), (0,)), ((), ())), preferred_element_type=jnp.float32)
        dv_ref[:, lanes] = lax.dot_general(ph, cs, (((0,), (0,)), ((), ())), preferred_element_type=jnp.float32)


def linear_kernel(q_ref, c_ref, k_ref, s_ref, prior_ref, gain_ref, wout_ref, wdq_ref,
                  mixed_ref, dq_ref, suffix_ref, gsum_ref, ldk_ref, dsp_ref):
    group_size = QUERY_HEADS // KEY_VALUE_HEADS
    token_rows = q_ref.shape[0]
    stacked_rows = group_size * token_rows
    row = lax.broadcasted_iota(jnp.int32, (stacked_rows, token_rows), 0) % token_rows
    col = lax.broadcasted_iota(jnp.int32, (stacked_rows, token_rows), 1)
    causal = row >= col
    for g in range(KEY_VALUE_HEADS):
        lanes = slice(g * HEAD_SIZE, (g + 1) * HEAD_SIZE)
        kg = k_ref[:, lanes]
        sg = s_ref[:, lanes]
        pg = prior_ref[g]
        qs = stacked_heads(q_ref, g, group_size)
        cs = stacked_heads(c_ref, g, group_size).astype(jnp.float32)
        gs = jnp.concatenate(
            [
                jnp.broadcast_to(
                    gain_ref[:, (g * group_size + h) * HEAD_SIZE : (g * group_size + h + 1) * HEAD_SIZE],
                    (token_rows, HEAD_SIZE),
                )
                for h in range(group_size)
            ],
            axis=0,
        )
        lh = jnp.where(
            causal,
            lax.dot_general(qs, kg, (((1,), (1,)), ((), ())), preferred_element_type=jnp.float32),
            0.0,
        ).astype(jnp.bfloat16)
        lin = jnp.dot(lh, sg, preferred_element_type=jnp.float32) + jnp.dot(
            qs, pg, preferred_element_type=jnp.float32
        )
        inverse_root = 1.0 / jnp.sqrt(jnp.mean(lin * lin, axis=-1, keepdims=True) + epsilon)
        normed = lin * inverse_root
        gn = gs * normed
        weighted = cs * normed
        scaled = cs * gs
        dl = ((scaled - normed * jnp.mean(scaled * normed, axis=-1, keepdims=True)) * inverse_root).astype(
            jnp.bfloat16
        )
        suffix_ref[g] = lax.dot_general(qs, dl, (((0,), (0,)), ((), ())), preferred_element_type=jnp.float32)
        bh = jnp.where(
            causal,
            lax.dot_general(dl, sg, (((1,), (1,)), ((), ())), preferred_element_type=jnp.float32),
            0.0,
        ).astype(jnp.bfloat16)
        ldq = lax.dot_general(dl, pg, (((1,), (1,)), ((), ())), preferred_element_type=jnp.float32)
        ldq = ldq + jnp.dot(bh, kg, preferred_element_type=jnp.float32)
        for h in range(group_size):
            cols = slice((g * group_size + h) * HEAD_SIZE, (g * group_size + h + 1) * HEAD_SIZE)
            rows = slice(h * token_rows, (h + 1) * token_rows)
            mixed_ref[:, cols] = (gn[rows] + wout_ref[:, cols]).astype(mixed_ref.dtype)
            gsum_ref[:, cols] = jnp.sum(weighted[rows], axis=0, keepdims=True)
            dq_ref[:, cols] = (ldq[rows] + wdq_ref[:, cols]).astype(dq_ref.dtype)
        ldk_ref[:, lanes] = lax.dot_general(bh, qs, (((0,), (0,)), ((), ())), preferred_element_type=jnp.float32)
        dsp_ref[:, lanes] = lax.dot_general(lh, dl, (((0,), (0,)), ((), ())), preferred_element_type=jnp.float32)


def in_vmem(count):
    return [pl.BlockSpec(memory_space=pltpu.VMEM)] * count


def per_device(queries, keys, values, spikes, window_lengths, gain, cotangent):
    token_rows = queries.shape[1]
    width = QUERY_HEADS * HEAD_SIZE
    reach = (WINDOW_REACH + token_rows - 2) // token_rows
    padding_rows = reach * token_rows
    window_rows = (reach + 1) * token_rows
    key_value_width = KEY_VALUE_HEADS * HEAD_SIZE
    q = queries[0]
    c = cotangent[0]
    k = keys[0]
    v = values[0]
    counts = jnp.repeat(spikes[0].astype(jnp.float32), HEAD_SIZE, axis=1)
    spiked = (v.astype(jnp.float32) * counts).astype(jnp.bfloat16)
    def state_of(block_keys, block_spiked):
        return jnp.stack(
            [
                lax.dot_general(
                    block_keys[:, g * HEAD_SIZE : (g + 1) * HEAD_SIZE],
                    block_spiked[:, g * HEAD_SIZE : (g + 1) * HEAD_SIZE],
                    (((0,), (0,)), ((), ())),
                    preferred_element_type=jnp.float32,
                )
                for g in range(KEY_VALUE_HEADS)
            ]
        )

    count_lanes = HEAD_SIZE
    spike_block = jnp.concatenate(
        [
            spikes[0].astype(jnp.bfloat16),
            jnp.zeros((token_rows, count_lanes - KEY_VALUE_HEADS), jnp.bfloat16),
        ],
        axis=1,
    )
    packed = jnp.concatenate([k, v, spike_block], axis=1)
    earlier = []
    for distance in range(reach, 0, -1):
        earlier.append(shifted(packed, "ctx", distance))
    near = jnp.zeros((KEY_VALUE_HEADS, HEAD_SIZE, HEAD_SIZE), jnp.float32)
    for piece in earlier:
        piece_counts = jnp.repeat(
            piece[:, 2 * key_value_width : 2 * key_value_width + KEY_VALUE_HEADS].astype(jnp.float32),
            HEAD_SIZE,
            axis=1,
        )
        piece_spiked = (
            piece[:, key_value_width : 2 * key_value_width].astype(jnp.float32) * piece_counts
        ).astype(jnp.bfloat16)
        near = near + state_of(piece[:, :key_value_width], piece_spiked)
    own_and_near = near + state_of(k, spiked)
    prior_half = spread_scan(near, own_and_near, "ctx").astype(jnp.bfloat16)
    window_packed = jnp.concatenate(
        [piece[:, : 2 * key_value_width] for piece in earlier] + [jnp.concatenate([k, v], axis=1)], axis=0
    )
    info = jnp.concatenate(
        [window_lengths.astype(jnp.int32), (lax.axis_index("ctx") * token_rows - padding_rows).reshape(1)]
    ).astype(jnp.int32)
    wout, wdq, dk_win, dv_win = pl.pallas_call(
        window_kernel,
        out_shape=(
            jax.ShapeDtypeStruct((token_rows, width), jnp.float32),
            jax.ShapeDtypeStruct((token_rows, width), jnp.float32),
            jax.ShapeDtypeStruct((window_rows, key_value_width), jnp.float32),
            jax.ShapeDtypeStruct((window_rows, key_value_width), jnp.float32),
        ),
        in_specs=[pl.BlockSpec(memory_space=pltpu.SMEM)] + in_vmem(4),
        out_specs=tuple(in_vmem(4)),
        cost_estimate=pl.CostEstimate(
            flops=12 * QUERY_HEADS * token_rows * window_rows * HEAD_SIZE,
            transcendentals=QUERY_HEADS * token_rows * window_rows,
            bytes_accessed=2 * token_rows * width * (2 + 4) + 2 * window_rows * key_value_width * (2 + 4),
        ),
    )(info, q, c, window_packed[:, :key_value_width], window_packed[:, key_value_width:])
    mixed, d_queries, suffix_local, gain_local, ldk, dsp = pl.pallas_call(
        linear_kernel,
        out_shape=(
            jax.ShapeDtypeStruct((token_rows, width), jnp.bfloat16),
            jax.ShapeDtypeStruct((token_rows, width), jnp.bfloat16),
            jax.ShapeDtypeStruct((KEY_VALUE_HEADS, HEAD_SIZE, HEAD_SIZE), jnp.float32),
            jax.ShapeDtypeStruct((1, width), jnp.float32),
            jax.ShapeDtypeStruct((token_rows, key_value_width), jnp.float32),
            jax.ShapeDtypeStruct((token_rows, key_value_width), jnp.float32),
        ),
        in_specs=in_vmem(8),
        out_specs=tuple(in_vmem(6)),
        cost_estimate=pl.CostEstimate(
            flops=20 * QUERY_HEADS * token_rows * token_rows * HEAD_SIZE,
            transcendentals=QUERY_HEADS * token_rows,
            bytes_accessed=token_rows * width * (2 + 2 + 4 + 4 + 2 + 2) + 6 * token_rows * key_value_width * 4,
        ),
    )(q, c, k, spiked, prior_half, gain.reshape(1, width), wout, wdq)
    total_tokens = queries.shape[0] * lax.axis_size("dp") * token_rows * lax.axis_size("ctx")
    state_rows = KEY_VALUE_HEADS * HEAD_SIZE
    gain_rows = width // HEAD_SIZE
    pad_rows = (-(state_rows + gain_rows)) % 8
    riding = jnp.concatenate(
        [
            suffix_local.reshape(state_rows, HEAD_SIZE),
            gain_local.reshape(gain_rows, HEAD_SIZE),
            jnp.zeros((pad_rows, HEAD_SIZE), jnp.float32),
        ],
        axis=0,
    )
    later_rows, total_rows = butterfly_scan(riding, "ctx", True)
    later_half = later_rows[:state_rows].reshape(suffix_local.shape).astype(jnp.bfloat16)
    gain_ctx = total_rows[state_rows : state_rows + gain_rows].reshape(width)
    d_gain = all_sum(gain_ctx, ("dp",)) * (total_tokens ** (-0.5))
    ldk_parts = []
    dsp_parts = []
    for g in range(KEY_VALUE_HEADS):
        lanes = slice(g * HEAD_SIZE, (g + 1) * HEAD_SIZE)
        ldk_parts.append(
            ldk[:, lanes]
            + lax.dot_general(
                spiked[:, lanes], later_half[g], (((1,), (1,)), ((), ())), preferred_element_type=jnp.float32
            )
        )
        dsp_parts.append(
            dsp[:, lanes] + jnp.dot(k[:, lanes], later_half[g], preferred_element_type=jnp.float32)
        )
    linear_key_gradient = jnp.concatenate(ldk_parts, axis=1)
    linear_value_gradient = jnp.concatenate(dsp_parts, axis=1) * counts
    received = jnp.zeros((token_rows, 2 * key_value_width), jnp.float32)
    for distance in range(1, reach + 1):
        start_row = (reach - distance) * token_rows
        sent = jnp.concatenate(
            [
                dk_win[start_row : start_row + token_rows],
                dv_win[start_row : start_row + token_rows],
            ],
            axis=1,
        )
        received = received + shifted(sent.astype(jnp.bfloat16), "ctx", -distance).astype(jnp.float32)
    keys_gradient = (
        linear_key_gradient + dk_win[padding_rows:] + received[:, :key_value_width]
    ).astype(jnp.bfloat16)
    values_gradient = (
        linear_value_gradient + dv_win[padding_rows:] + received[:, key_value_width:]
    ).astype(jnp.bfloat16)
    return (
        mixed[None],
        d_queries[None],
        keys_gradient[None],
        values_gradient[None],
        d_gain,
    )


def solution(mesh):
    placed = (
        P("dp", "ctx", None),
        P("dp", "ctx", None),
        P("dp", "ctx", None),
        P("dp", "ctx", None),
        P(),
        P(),
        P("dp", "ctx", None),
    )
    return jax.shard_map(
        per_device,
        mesh=mesh,
        in_specs=placed,
        out_specs=(
            P("dp", "ctx", None),
            P("dp", "ctx", None),
            P("dp", "ctx", None),
            P("dp", "ctx", None),
            P(),
        ),
        check_vma=False,
    )
```

```python
import jax
import jax.numpy as jnp
from jax import lax
from jax.experimental import pallas as pl
from jax.experimental.pallas import tpu as pltpu
from jax.sharding import PartitionSpec as P

QUERY_HEADS = 14
KEY_VALUE_HEADS = 2
HEAD_SIZE = 128
WINDOW_REACH = 256


epsilon = 1e-05


def exclusive_scan(part, axis, reverse):
    count = lax.axis_size(axis)
    running = part
    total = None
    distance = 1
    while distance < count:
        if reverse:
            route = [(i + distance, i) for i in range(count - distance)]
        else:
            route = [(i, i + distance) for i in range(count - distance)]
        got = lax.ppermute(running, axis, route)
        total = got if total is None else total + got
        if distance * 2 < count:
            running = running + got
        distance *= 2
    if total is None:
        total = jnp.zeros_like(part)
    return total


def butterfly_scan(part, axis, reverse):
    count = lax.axis_size(axis)
    place = lax.axis_index(axis)
    group = part
    before = jnp.zeros(part.shape, jnp.float32)
    step = 1
    while step < count:
        mine = group.astype(jnp.bfloat16)
        got = lax.ppermute(mine, axis, [(i, i ^ step) for i in range(count)]).astype(jnp.float32)
        partner = jnp.bitwise_xor(place, step)
        take = partner > place if reverse else partner < place
        before = before + jnp.where(take, got, 0.0)
        group = mine.astype(jnp.float32) + got
        step *= 2
    return before, group


def spread_scan(near, own, axis):
    count = lax.axis_size(axis)
    total = near
    running = own
    stride = 3
    while stride < count:
        parts = []
        for distance in (stride, 2 * stride):
            if distance < count:
                parts.append(shifted(running, axis, distance))
        for got in parts:
            total = total + got
        if 3 * stride < count:
            for got in parts:
                running = running + got
        stride *= 3
    return total


def all_sum(part, axes):
    count = 1
    for axis in axes:
        count *= lax.axis_size(axis)
    step = 1
    while step < count:
        route = [(i, i ^ step) for i in range(count)]
        part = part + lax.ppermute(part, axes, route)
        step *= 2
    return part


def shifted(block, axis, distance):
    devices = range(lax.axis_size(axis))
    route = [(i - distance, i) for i in devices if i - distance in devices]
    return lax.ppermute(block, axis, route)


def stacked_heads(ref, group, group_size):
    return jnp.concatenate(
        [ref[:, (group * group_size + h) * HEAD_SIZE : (group * group_size + h + 1) * HEAD_SIZE] for h in range(group_size)],
        axis=0,
    )


def window_kernel(info_ref, q_ref, c_ref, k_ref, v_ref, wout_ref, wdq_ref, halo_ref, own_ref):
    group_size = QUERY_HEADS // KEY_VALUE_HEADS
    token_rows = q_ref.shape[0]
    window_rows = k_ref.shape[0]
    padding_rows = window_rows - token_rows
    scale = HEAD_SIZE ** (-0.5)
    stacked_rows = group_size * token_rows
    row = lax.broadcasted_iota(jnp.int32, (stacked_rows, window_rows), 0) % token_rows
    col = lax.broadcasted_iota(jnp.int32, (stacked_rows, window_rows), 1)
    back = row + padding_rows - col
    seen = (back >= 0) & (col + info_ref[2] >= 0)
    for g in range(KEY_VALUE_HEADS):
        visible = seen & (back < info_ref[g])
        lanes = slice(g * HEAD_SIZE, (g + 1) * HEAD_SIZE)
        kg = k_ref[:, lanes]
        vg = v_ref[:, lanes]
        qs = stacked_heads(q_ref, g, group_size)
        cs = stacked_heads(c_ref, g, group_size)
        s = lax.dot_general(qs, kg, (((1,), (1,)), ((), ())), preferred_element_type=jnp.float32) * scale
        s = jnp.where(visible, s, -1e30)
        top = jnp.max(s, axis=-1, keepdims=True)
        e = jnp.exp(s - top)
        p = e * (1.0 / jnp.sum(e, axis=-1, keepdims=True))
        ph = p.astype(jnp.bfloat16)
        wout = jnp.dot(ph, vg, preferred_element_type=jnp.float32)
        gp = lax.dot_general(cs, vg, (((1,), (1,)), ((), ())), preferred_element_type=jnp.float32)
        delta = jnp.sum(cs.astype(jnp.float32) * wout, axis=-1, keepdims=True)
        ds = (p * (gp - delta) * scale).astype(jnp.bfloat16)
        wdq = jnp.dot(ds, kg, preferred_element_type=jnp.float32)
        for h in range(group_size):
            cols = slice((g * group_size + h) * HEAD_SIZE, (g * group_size + h + 1) * HEAD_SIZE)
            rows = slice(h * token_rows, (h + 1) * token_rows)
            wout_ref[:, cols] = wout[rows]
            wdq_ref[:, cols] = wdq[rows]
        dk = lax.dot_general(ds, qs, (((0,), (0,)), ((), ())), preferred_element_type=jnp.float32)
        dv = lax.dot_general(ph, cs, (((0,), (0,)), ((), ())), preferred_element_type=jnp.float32)
        value_lanes = slice(KEY_VALUE_HEADS * HEAD_SIZE + g * HEAD_SIZE, KEY_VALUE_HEADS * HEAD_SIZE + (g + 1) * HEAD_SIZE)
        reach = padding_rows // token_rows
        for distance in range(1, reach + 1):
            start_row = (reach - distance) * token_rows
            halo_ref[distance - 1, :, lanes] = dk[start_row : start_row + token_rows].astype(halo_ref.dtype)
            halo_ref[distance - 1, :, value_lanes] = dv[start_row : start_row + token_rows].astype(halo_ref.dtype)
        own_ref[:, lanes] = dk[padding_rows:]
        own_ref[:, value_lanes] = dv[padding_rows:]


def linear_kernel(q_ref, c_ref, k_ref, s_ref, prior_ref, gain_ref, wout_ref, wdq_ref,
                  mixed_ref, dq_ref, riding_ref, ldk_ref, dsp_ref):
    group_size = QUERY_HEADS // KEY_VALUE_HEADS
    token_rows = q_ref.shape[0]
    stacked_rows = group_size * token_rows
    row = lax.broadcasted_iota(jnp.int32, (stacked_rows, token_rows), 0) % token_rows
    col = lax.broadcasted_iota(jnp.int32, (stacked_rows, token_rows), 1)
    causal = row >= col
    gain_rows = []
    for g in range(KEY_VALUE_HEADS):
        lanes = slice(g * HEAD_SIZE, (g + 1) * HEAD_SIZE)
        kg = k_ref[:, lanes]
        sg = s_ref[:, lanes]
        pg = prior_ref[g]
        qs = stacked_heads(q_ref, g, group_size)
        cs = stacked_heads(c_ref, g, group_size).astype(jnp.float32)
        gs = jnp.concatenate(
            [
                jnp.broadcast_to(
                    gain_ref[:, (g * group_size + h) * HEAD_SIZE : (g * group_size + h + 1) * HEAD_SIZE],
                    (token_rows, HEAD_SIZE),
                )
                for h in range(group_size)
            ],
            axis=0,
        )
        lh = jnp.where(
            causal,
            lax.dot_general(qs, kg, (((1,), (1,)), ((), ())), preferred_element_type=jnp.float32),
            0.0,
        ).astype(jnp.bfloat16)
        lin = jnp.dot(lh, sg, preferred_element_type=jnp.float32) + jnp.dot(
            qs, pg, preferred_element_type=jnp.float32
        )
        inverse_root = 1.0 / jnp.sqrt(jnp.mean(lin * lin, axis=-1, keepdims=True) + epsilon)
        normed = lin * inverse_root
        gn = gs * normed
        weighted = cs * normed
        scaled = cs * gs
        dl = ((scaled - normed * jnp.mean(scaled * normed, axis=-1, keepdims=True)) * inverse_root).astype(
            jnp.bfloat16
        )
        riding_ref[g * HEAD_SIZE : (g + 1) * HEAD_SIZE, :] = lax.dot_general(
            qs, dl, (((0,), (0,)), ((), ())), preferred_element_type=jnp.float32
        ).astype(riding_ref.dtype)
        bh = jnp.where(
            causal,
            lax.dot_general(dl, sg, (((1,), (1,)), ((), ())), preferred_element_type=jnp.float32),
            0.0,
        ).astype(jnp.bfloat16)
        ldq = lax.dot_general(dl, pg, (((1,), (1,)), ((), ())), preferred_element_type=jnp.float32)
        ldq = ldq + jnp.dot(bh, kg, preferred_element_type=jnp.float32)
        for h in range(group_size):
            cols = slice((g * group_size + h) * HEAD_SIZE, (g * group_size + h + 1) * HEAD_SIZE)
            rows = slice(h * token_rows, (h + 1) * token_rows)
            mixed_ref[:, cols] = (gn[rows] + wout_ref[:, cols]).astype(mixed_ref.dtype)
            gain_rows.append(jnp.sum(weighted[rows], axis=0, keepdims=True))
            dq_ref[:, cols] = (ldq[rows] + wdq_ref[:, cols]).astype(dq_ref.dtype)
        ldk_ref[:, lanes] = lax.dot_general(bh, qs, (((0,), (0,)), ((), ())), preferred_element_type=jnp.float32)
        dsp_ref[:, lanes] = lax.dot_general(lh, dl, (((0,), (0,)), ((), ())), preferred_element_type=jnp.float32)
    state_rows = KEY_VALUE_HEADS * HEAD_SIZE
    spare = riding_ref.shape[0] - state_rows - len(gain_rows)
    riding_ref[state_rows:, :] = jnp.concatenate(
        gain_rows + [jnp.zeros((spare, HEAD_SIZE), jnp.float32)], axis=0
    ).astype(riding_ref.dtype)


def in_vmem(count):
    return [pl.BlockSpec(memory_space=pltpu.VMEM)] * count


def per_device(queries, keys, values, spikes, window_lengths, gain, cotangent):
    token_rows = queries.shape[1]
    width = QUERY_HEADS * HEAD_SIZE
    reach = (WINDOW_REACH + token_rows - 2) // token_rows
    padding_rows = reach * token_rows
    window_rows = (reach + 1) * token_rows
    key_value_width = KEY_VALUE_HEADS * HEAD_SIZE
    q = queries[0]
    c = cotangent[0]
    k = keys[0]
    v = values[0]
    counts = jnp.repeat(spikes[0].astype(jnp.float32), HEAD_SIZE, axis=1)
    spiked = (v.astype(jnp.float32) * counts).astype(jnp.bfloat16)
    def state_of(block_keys, block_spiked):
        return jnp.stack(
            [
                lax.dot_general(
                    block_keys[:, g * HEAD_SIZE : (g + 1) * HEAD_SIZE],
                    block_spiked[:, g * HEAD_SIZE : (g + 1) * HEAD_SIZE],
                    (((0,), (0,)), ((), ())),
                    preferred_element_type=jnp.float32,
                )
                for g in range(KEY_VALUE_HEADS)
            ]
        )

    count_lanes = HEAD_SIZE
    spike_block = jnp.concatenate(
        [
            spikes[0].astype(jnp.bfloat16),
            jnp.zeros((token_rows, count_lanes - KEY_VALUE_HEADS), jnp.bfloat16),
        ],
        axis=1,
    )
    packed = jnp.concatenate([k, v, spike_block], axis=1)
    earlier = []
    for distance in range(reach, 0, -1):
        earlier.append(shifted(packed, "ctx", distance))
    near = jnp.zeros((KEY_VALUE_HEADS, HEAD_SIZE, HEAD_SIZE), jnp.float32)
    for piece in earlier:
        piece_counts = jnp.repeat(
            piece[:, 2 * key_value_width : 2 * key_value_width + KEY_VALUE_HEADS].astype(jnp.float32),
            HEAD_SIZE,
            axis=1,
        )
        piece_spiked = (
            piece[:, key_value_width : 2 * key_value_width].astype(jnp.float32) * piece_counts
        ).astype(jnp.bfloat16)
        near = near + state_of(piece[:, :key_value_width], piece_spiked)
    own_and_near = near + state_of(k, spiked)
    prior_half = spread_scan(near, own_and_near, "ctx").astype(jnp.bfloat16)
    window_packed = jnp.concatenate(
        [piece[:, : 2 * key_value_width] for piece in earlier] + [jnp.concatenate([k, v], axis=1)], axis=0
    )
    info = jnp.concatenate(
        [window_lengths.astype(jnp.int32), (lax.axis_index("ctx") * token_rows - padding_rows).reshape(1)]
    ).astype(jnp.int32)
    wout, wdq, halo_out, own_grad = pl.pallas_call(
        window_kernel,
        out_shape=(
            jax.ShapeDtypeStruct((token_rows, width), jnp.float32),
            jax.ShapeDtypeStruct((token_rows, width), jnp.float32),
            jax.ShapeDtypeStruct((reach, token_rows, 2 * key_value_width), jnp.bfloat16),
            jax.ShapeDtypeStruct((token_rows, 2 * key_value_width), jnp.float32),
        ),
        in_specs=[pl.BlockSpec(memory_space=pltpu.SMEM)] + in_vmem(4),
        out_specs=tuple(in_vmem(4)),
        cost_estimate=pl.CostEstimate(
            flops=12 * QUERY_HEADS * token_rows * window_rows * HEAD_SIZE,
            transcendentals=QUERY_HEADS * token_rows * window_rows,
            bytes_accessed=2 * token_rows * width * (2 + 4) + 2 * window_rows * key_value_width * (2 + 4),
        ),
    )(info, q, c, window_packed[:, :key_value_width], window_packed[:, key_value_width:])
    state_rows = KEY_VALUE_HEADS * HEAD_SIZE
    gain_rows = width // HEAD_SIZE
    riding_rows = state_rows + gain_rows + (-(state_rows + gain_rows)) % 16
    mixed, d_queries, riding, ldk, dsp = pl.pallas_call(
        linear_kernel,
        out_shape=(
            jax.ShapeDtypeStruct((token_rows, width), jnp.bfloat16),
            jax.ShapeDtypeStruct((token_rows, width), jnp.bfloat16),
            jax.ShapeDtypeStruct((riding_rows, HEAD_SIZE), jnp.bfloat16),
            jax.ShapeDtypeStruct((token_rows, key_value_width), jnp.float32),
            jax.ShapeDtypeStruct((token_rows, key_value_width), jnp.float32),
        ),
        in_specs=in_vmem(8),
        out_specs=tuple(in_vmem(5)),
        cost_estimate=pl.CostEstimate(
            flops=20 * QUERY_HEADS * token_rows * token_rows * HEAD_SIZE,
            transcendentals=QUERY_HEADS * token_rows,
            bytes_accessed=token_rows * width * (2 + 2 + 4 + 4 + 2 + 2) + 6 * token_rows * key_value_width * 4,
        ),
    )(q, c, k, spiked, prior_half, gain.reshape(1, width), wout, wdq)
    total_tokens = queries.shape[0] * lax.axis_size("dp") * token_rows * lax.axis_size("ctx")
    later_rows, total_rows = butterfly_scan(riding, "ctx", True)
    later_half = later_rows[:state_rows].reshape(KEY_VALUE_HEADS, HEAD_SIZE, HEAD_SIZE).astype(jnp.bfloat16)
    gain_ctx = total_rows[state_rows : state_rows + gain_rows].reshape(width)
    d_gain = all_sum(gain_ctx, ("dp",)) * (total_tokens ** (-0.5))
    ldk_parts = []
    dsp_parts = []
    for g in range(KEY_VALUE_HEADS):
        lanes = slice(g * HEAD_SIZE, (g + 1) * HEAD_SIZE)
        ldk_parts.append(
            ldk[:, lanes]
            + lax.dot_general(
                spiked[:, lanes], later_half[g], (((1,), (1,)), ((), ())), preferred_element_type=jnp.float32
            )
        )
        dsp_parts.append(
            dsp[:, lanes] + jnp.dot(k[:, lanes], later_half[g], preferred_element_type=jnp.float32)
        )
    linear_key_gradient = jnp.concatenate(ldk_parts, axis=1)
    linear_value_gradient = jnp.concatenate(dsp_parts, axis=1) * counts
    received = own_grad
    for distance in range(1, reach + 1):
        received = received + shifted(halo_out[distance - 1], "ctx", -distance).astype(jnp.float32)
    keys_gradient = (
        linear_key_gradient + received[:, :key_value_width]
    ).astype(jnp.bfloat16)
    values_gradient = (
        linear_value_gradient + received[:, key_value_width:]
    ).astype(jnp.bfloat16)
    return (
        mixed[None],
        d_queries[None],
        keys_gradient[None],
        values_gradient[None],
        d_gain,
    )


def solution(mesh):
    placed = (
        P("dp", "ctx", None),
        P("dp", "ctx", None),
        P("dp", "ctx", None),
        P("dp", "ctx", None),
        P(),
        P(),
        P("dp", "ctx", None),
    )
    return jax.shard_map(
        per_device,
        mesh=mesh,
        in_specs=placed,
        out_specs=(
            P("dp", "ctx", None),
            P("dp", "ctx", None),
            P("dp", "ctx", None),
            P("dp", "ctx", None),
            P(),
        ),
        check_vma=False,
    )
```

```python
import jax
import jax.numpy as jnp
from jax import lax
from jax.experimental import pallas as pl
from jax.experimental.pallas import tpu as pltpu
from jax.sharding import PartitionSpec as P

QUERY_HEADS = 14
KEY_VALUE_HEADS = 2
HEAD_SIZE = 128
WINDOW_REACH = 256


epsilon = 1e-05


def exclusive_scan(part, axis, reverse):
    count = lax.axis_size(axis)
    running = part
    total = None
    distance = 1
    while distance < count:
        if reverse:
            route = [(i + distance, i) for i in range(count - distance)]
        else:
            route = [(i, i + distance) for i in range(count - distance)]
        got = lax.ppermute(running, axis, route)
        total = got if total is None else total + got
        if distance * 2 < count:
            running = running + got
        distance *= 2
    if total is None:
        total = jnp.zeros_like(part)
    return total


def butterfly_scan(part, axis, reverse):
    count = lax.axis_size(axis)
    place = lax.axis_index(axis)
    group = part
    before = jnp.zeros(part.shape, jnp.float32)
    step = 1
    while step < count:
        mine = group.astype(jnp.bfloat16)
        got = lax.ppermute(mine, axis, [(i, i ^ step) for i in range(count)]).astype(jnp.float32)
        partner = jnp.bitwise_xor(place, step)
        take = partner > place if reverse else partner < place
        before = before + jnp.where(take, got, 0.0)
        group = mine.astype(jnp.float32) + got
        step *= 2
    return before, group


def spread_scan(near, own, axis):
    count = lax.axis_size(axis)
    total = near
    running = own
    stride = 3
    while stride < count:
        parts = []
        for distance in (stride, 2 * stride):
            if distance < count:
                parts.append(shifted(running, axis, distance))
        for got in parts:
            total = total + got
        if 3 * stride < count:
            for got in parts:
                running = running + got
        stride *= 3
    return total


def all_sum(part, axes):
    count = 1
    for axis in axes:
        count *= lax.axis_size(axis)
    step = 1
    while step < count:
        route = [(i, i ^ step) for i in range(count)]
        part = part + lax.ppermute(part, axes, route)
        step *= 2
    return part


def shifted(block, axis, distance):
    devices = range(lax.axis_size(axis))
    route = [(i - distance, i) for i in devices if i - distance in devices]
    return lax.ppermute(block, axis, route)


def stacked_heads(ref, group, group_size):
    return jnp.concatenate(
        [ref[:, (group * group_size + h) * HEAD_SIZE : (group * group_size + h + 1) * HEAD_SIZE] for h in range(group_size)],
        axis=0,
    )


def window_kernel(info_ref, q_ref, c_ref, k_ref, v_ref, wout_ref, wdq_ref, halo_ref, own_ref):
    group_size = QUERY_HEADS // KEY_VALUE_HEADS
    token_rows = q_ref.shape[0]
    window_rows = k_ref.shape[0]
    padding_rows = window_rows - token_rows
    scale = HEAD_SIZE ** (-0.5)
    stacked_rows = group_size * token_rows
    row = lax.broadcasted_iota(jnp.int32, (stacked_rows, window_rows), 0) % token_rows
    col = lax.broadcasted_iota(jnp.int32, (stacked_rows, window_rows), 1)
    back = row + padding_rows - col
    base = lax.axis_index("ctx") * token_rows - padding_rows
    seen = (back >= 0) & (col + base >= 0)
    for g in range(KEY_VALUE_HEADS):
        visible = seen & (back < info_ref[g])
        lanes = slice(g * HEAD_SIZE, (g + 1) * HEAD_SIZE)
        kg = k_ref[:, lanes]
        vg = v_ref[:, lanes]
        qs = stacked_heads(q_ref, g, group_size)
        cs = stacked_heads(c_ref, g, group_size)
        s = lax.dot_general(qs, kg, (((1,), (1,)), ((), ())), preferred_element_type=jnp.float32) * scale
        s = jnp.where(visible, s, -1e30)
        top = jnp.max(s, axis=-1, keepdims=True)
        e = jnp.exp(s - top)
        p = e * (1.0 / jnp.sum(e, axis=-1, keepdims=True))
        ph = p.astype(jnp.bfloat16)
        wout = jnp.dot(ph, vg, preferred_element_type=jnp.float32)
        gp = lax.dot_general(cs, vg, (((1,), (1,)), ((), ())), preferred_element_type=jnp.float32)
        delta = jnp.sum(cs.astype(jnp.float32) * wout, axis=-1, keepdims=True)
        ds = (p * (gp - delta) * scale).astype(jnp.bfloat16)
        wdq = jnp.dot(ds, kg, preferred_element_type=jnp.float32)
        for h in range(group_size):
            cols = slice((g * group_size + h) * HEAD_SIZE, (g * group_size + h + 1) * HEAD_SIZE)
            rows = slice(h * token_rows, (h + 1) * token_rows)
            wout_ref[:, cols] = wout[rows]
            wdq_ref[:, cols] = wdq[rows]
        dk = lax.dot_general(ds, qs, (((0,), (0,)), ((), ())), preferred_element_type=jnp.float32)
        dv = lax.dot_general(ph, cs, (((0,), (0,)), ((), ())), preferred_element_type=jnp.float32)
        value_lanes = slice(KEY_VALUE_HEADS * HEAD_SIZE + g * HEAD_SIZE, KEY_VALUE_HEADS * HEAD_SIZE + (g + 1) * HEAD_SIZE)
        reach = padding_rows // token_rows
        for distance in range(1, reach + 1):
            start_row = (reach - distance) * token_rows
            halo_ref[distance - 1, :, lanes] = dk[start_row : start_row + token_rows].astype(halo_ref.dtype)
            halo_ref[distance - 1, :, value_lanes] = dv[start_row : start_row + token_rows].astype(halo_ref.dtype)
        own_ref[:, lanes] = dk[padding_rows:]
        own_ref[:, value_lanes] = dv[padding_rows:]


def linear_kernel(q_ref, c_ref, k_ref, s_ref, prior_ref, gain_ref, wout_ref, wdq_ref,
                  mixed_ref, dq_ref, riding_ref, ldk_ref, dsp_ref):
    group_size = QUERY_HEADS // KEY_VALUE_HEADS
    token_rows = q_ref.shape[0]
    stacked_rows = group_size * token_rows
    row = lax.broadcasted_iota(jnp.int32, (stacked_rows, token_rows), 0) % token_rows
    col = lax.broadcasted_iota(jnp.int32, (stacked_rows, token_rows), 1)
    causal = row >= col
    gain_rows = []
    for g in range(KEY_VALUE_HEADS):
        lanes = slice(g * HEAD_SIZE, (g + 1) * HEAD_SIZE)
        kg = k_ref[:, lanes]
        sg = s_ref[:, lanes]
        pg = prior_ref[g]
        qs = stacked_heads(q_ref, g, group_size)
        cs = stacked_heads(c_ref, g, group_size).astype(jnp.float32)
        gs = jnp.concatenate(
            [
                jnp.broadcast_to(
                    gain_ref[(g * group_size + h) * HEAD_SIZE : (g * group_size + h + 1) * HEAD_SIZE][None, :],
                    (token_rows, HEAD_SIZE),
                )
                for h in range(group_size)
            ],
            axis=0,
        )
        lh = jnp.where(
            causal,
            lax.dot_general(qs, kg, (((1,), (1,)), ((), ())), preferred_element_type=jnp.float32),
            0.0,
        ).astype(jnp.bfloat16)
        lin = jnp.dot(lh, sg, preferred_element_type=jnp.float32) + jnp.dot(
            qs, pg, preferred_element_type=jnp.float32
        )
        inverse_root = 1.0 / jnp.sqrt(jnp.mean(lin * lin, axis=-1, keepdims=True) + epsilon)
        normed = lin * inverse_root
        gn = gs * normed
        weighted = cs * normed
        scaled = cs * gs
        dl = ((scaled - normed * jnp.mean(scaled * normed, axis=-1, keepdims=True)) * inverse_root).astype(
            jnp.bfloat16
        )
        riding_ref[g * HEAD_SIZE : (g + 1) * HEAD_SIZE, :] = lax.dot_general(
            qs, dl, (((0,), (0,)), ((), ())), preferred_element_type=jnp.float32
        ).astype(riding_ref.dtype)
        bh = jnp.where(
            causal,
            lax.dot_general(dl, sg, (((1,), (1,)), ((), ())), preferred_element_type=jnp.float32),
            0.0,
        ).astype(jnp.bfloat16)
        ldq = lax.dot_general(dl, pg, (((1,), (1,)), ((), ())), preferred_element_type=jnp.float32)
        ldq = ldq + jnp.dot(bh, kg, preferred_element_type=jnp.float32)
        for h in range(group_size):
            cols = slice((g * group_size + h) * HEAD_SIZE, (g * group_size + h + 1) * HEAD_SIZE)
            rows = slice(h * token_rows, (h + 1) * token_rows)
            mixed_ref[:, cols] = (gn[rows] + wout_ref[:, cols]).astype(mixed_ref.dtype)
            gain_rows.append(jnp.sum(weighted[rows], axis=0, keepdims=True))
            dq_ref[:, cols] = (ldq[rows] + wdq_ref[:, cols]).astype(dq_ref.dtype)
        ldk_ref[:, lanes] = lax.dot_general(bh, qs, (((0,), (0,)), ((), ())), preferred_element_type=jnp.float32)
        dsp_ref[:, lanes] = lax.dot_general(lh, dl, (((0,), (0,)), ((), ())), preferred_element_type=jnp.float32)
    state_rows = KEY_VALUE_HEADS * HEAD_SIZE
    spare = riding_ref.shape[0] - state_rows - len(gain_rows)
    riding_ref[state_rows:, :] = jnp.concatenate(
        gain_rows + [jnp.zeros((spare, HEAD_SIZE), jnp.float32)], axis=0
    ).astype(riding_ref.dtype)


def in_vmem(count):
    return [pl.BlockSpec(memory_space=pltpu.VMEM)] * count


def per_device(queries, keys, values, spikes, window_lengths, gain, cotangent):
    token_rows = queries.shape[1]
    width = QUERY_HEADS * HEAD_SIZE
    reach = (WINDOW_REACH + token_rows - 2) // token_rows
    padding_rows = reach * token_rows
    window_rows = (reach + 1) * token_rows
    key_value_width = KEY_VALUE_HEADS * HEAD_SIZE
    q = queries[0]
    c = cotangent[0]
    k = keys[0]
    v = values[0]
    counts = jnp.repeat(spikes[0].astype(jnp.float32), HEAD_SIZE, axis=1)
    spiked = (v.astype(jnp.float32) * counts).astype(jnp.bfloat16)
    def state_of(block_keys, block_spiked):
        return jnp.stack(
            [
                lax.dot_general(
                    block_keys[:, g * HEAD_SIZE : (g + 1) * HEAD_SIZE],
                    block_spiked[:, g * HEAD_SIZE : (g + 1) * HEAD_SIZE],
                    (((0,), (0,)), ((), ())),
                    preferred_element_type=jnp.float32,
                )
                for g in range(KEY_VALUE_HEADS)
            ]
        )

    count_lanes = HEAD_SIZE
    spike_block = jnp.concatenate(
        [
            spikes[0].astype(jnp.bfloat16),
            jnp.zeros((token_rows, count_lanes - KEY_VALUE_HEADS), jnp.bfloat16),
        ],
        axis=1,
    )
    packed = jnp.concatenate([k, v, spike_block], axis=1)
    earlier = []
    for distance in range(reach, 0, -1):
        earlier.append(shifted(packed, "ctx", distance))
    near = jnp.zeros((KEY_VALUE_HEADS, HEAD_SIZE, HEAD_SIZE), jnp.float32)
    for piece in earlier:
        piece_counts = jnp.repeat(
            piece[:, 2 * key_value_width : 2 * key_value_width + KEY_VALUE_HEADS].astype(jnp.float32),
            HEAD_SIZE,
            axis=1,
        )
        piece_spiked = (
            piece[:, key_value_width : 2 * key_value_width].astype(jnp.float32) * piece_counts
        ).astype(jnp.bfloat16)
        near = near + state_of(piece[:, :key_value_width], piece_spiked)
    own_and_near = near + state_of(k, spiked)
    prior_half = spread_scan(near, own_and_near, "ctx").astype(jnp.bfloat16)
    window_packed = jnp.concatenate(
        [piece[:, : 2 * key_value_width] for piece in earlier] + [jnp.concatenate([k, v], axis=1)], axis=0
    )
    wout, wdq, halo_out, own_grad = pl.pallas_call(
        window_kernel,
        out_shape=(
            jax.ShapeDtypeStruct((token_rows, width), jnp.float32),
            jax.ShapeDtypeStruct((token_rows, width), jnp.float32),
            jax.ShapeDtypeStruct((reach, token_rows, 2 * key_value_width), jnp.bfloat16),
            jax.ShapeDtypeStruct((token_rows, 2 * key_value_width), jnp.float32),
        ),
        in_specs=[pl.BlockSpec(memory_space=pltpu.SMEM)] + in_vmem(4),
        out_specs=tuple(in_vmem(4)),
        cost_estimate=pl.CostEstimate(
            flops=12 * QUERY_HEADS * token_rows * window_rows * HEAD_SIZE,
            transcendentals=QUERY_HEADS * token_rows * window_rows,
            bytes_accessed=2 * token_rows * width * (2 + 4) + 2 * window_rows * key_value_width * (2 + 4),
        ),
    )(window_lengths, q, c, window_packed[:, :key_value_width], window_packed[:, key_value_width:])
    state_rows = KEY_VALUE_HEADS * HEAD_SIZE
    gain_rows = width // HEAD_SIZE
    riding_rows = state_rows + gain_rows + (-(state_rows + gain_rows)) % 16
    mixed, d_queries, riding, ldk, dsp = pl.pallas_call(
        linear_kernel,
        out_shape=(
            jax.ShapeDtypeStruct((token_rows, width), jnp.bfloat16),
            jax.ShapeDtypeStruct((token_rows, width), jnp.bfloat16),
            jax.ShapeDtypeStruct((riding_rows, HEAD_SIZE), jnp.bfloat16),
            jax.ShapeDtypeStruct((token_rows, key_value_width), jnp.float32),
            jax.ShapeDtypeStruct((token_rows, key_value_width), jnp.float32),
        ),
        in_specs=in_vmem(8),
        out_specs=tuple(in_vmem(5)),
        cost_estimate=pl.CostEstimate(
            flops=20 * QUERY_HEADS * token_rows * token_rows * HEAD_SIZE,
            transcendentals=QUERY_HEADS * token_rows,
            bytes_accessed=token_rows * width * (2 + 2 + 4 + 4 + 2 + 2) + 6 * token_rows * key_value_width * 4,
        ),
    )(q, c, k, spiked, prior_half, gain, wout, wdq)
    total_tokens = queries.shape[0] * lax.axis_size("dp") * token_rows * lax.axis_size("ctx")
    later_rows, total_rows = butterfly_scan(riding, "ctx", True)
    later_half = later_rows[:state_rows].reshape(KEY_VALUE_HEADS, HEAD_SIZE, HEAD_SIZE).astype(jnp.bfloat16)
    gain_ctx = total_rows[state_rows : state_rows + gain_rows].reshape(width)
    d_gain = all_sum(gain_ctx, ("dp",)) * (total_tokens ** (-0.5))
    ldk_parts = []
    dsp_parts = []
    for g in range(KEY_VALUE_HEADS):
        lanes = slice(g * HEAD_SIZE, (g + 1) * HEAD_SIZE)
        ldk_parts.append(
            ldk[:, lanes]
            + lax.dot_general(
                spiked[:, lanes], later_half[g], (((1,), (1,)), ((), ())), preferred_element_type=jnp.float32
            )
        )
        dsp_parts.append(
            dsp[:, lanes] + jnp.dot(k[:, lanes], later_half[g], preferred_element_type=jnp.float32)
        )
    linear_key_gradient = jnp.concatenate(ldk_parts, axis=1)
    linear_value_gradient = jnp.concatenate(dsp_parts, axis=1) * counts
    received = own_grad
    for distance in range(1, reach + 1):
        received = received + shifted(halo_out[distance - 1], "ctx", -distance).astype(jnp.float32)
    keys_gradient = (
        linear_key_gradient + received[:, :key_value_width]
    ).astype(jnp.bfloat16)
    values_gradient = (
        linear_value_gradient + received[:, key_value_width:]
    ).astype(jnp.bfloat16)
    return (
        mixed[None],
        d_queries[None],
        keys_gradient[None],
        values_gradient[None],
        d_gain,
    )


def solution(mesh):
    placed = (
        P("dp", "ctx", None),
        P("dp", "ctx", None),
        P("dp", "ctx", None),
        P("dp", "ctx", None),
        P(),
        P(),
        P("dp", "ctx", None),
    )
    return jax.shard_map(
        per_device,
        mesh=mesh,
        in_specs=placed,
        out_specs=(
            P("dp", "ctx", None),
            P("dp", "ctx", None),
            P("dp", "ctx", None),
            P("dp", "ctx", None),
            P(),
        ),
        check_vma=False,
    )
```

```python
import jax
import jax.numpy as jnp
from jax import lax
from jax.experimental import pallas as pl
from jax.experimental.pallas import tpu as pltpu
from jax.sharding import PartitionSpec as P

QUERY_HEADS = 14
KEY_VALUE_HEADS = 2
HEAD_SIZE = 128
WINDOW_REACH = 256


epsilon = 1e-05


def exclusive_scan(part, axis, reverse):
    count = lax.axis_size(axis)
    running = part
    total = None
    distance = 1
    while distance < count:
        if reverse:
            route = [(i + distance, i) for i in range(count - distance)]
        else:
            route = [(i, i + distance) for i in range(count - distance)]
        got = lax.ppermute(running, axis, route)
        total = got if total is None else total + got
        if distance * 2 < count:
            running = running + got
        distance *= 2
    if total is None:
        total = jnp.zeros_like(part)
    return total


def butterfly_scan(part, axis, reverse):
    count = lax.axis_size(axis)
    place = lax.axis_index(axis)
    group = part
    before = jnp.zeros(part.shape, jnp.float32)
    first = None
    step = 1
    while step < count:
        mine = group.astype(jnp.bfloat16)
        got = lax.ppermute(mine, axis, [(i, i ^ step) for i in range(count)]).astype(jnp.float32)
        if first is None:
            first = got
        partner = jnp.bitwise_xor(place, step)
        take = partner > place if reverse else partner < place
        before = before + jnp.where(take, got, 0.0)
        group = mine.astype(jnp.float32) + got
        step *= 2
    return before, group, first


def spread_scan(near, own, axis):
    count = lax.axis_size(axis)
    total = near
    running = own
    stride = 3
    while stride < count:
        parts = []
        for distance in (stride, 2 * stride):
            if distance < count:
                parts.append(shifted(running, axis, distance))
        for got in parts:
            total = total + got
        if 3 * stride < count:
            for got in parts:
                running = running + got
        stride *= 3
    return total


def all_sum(part, axes):
    count = 1
    for axis in axes:
        count *= lax.axis_size(axis)
    step = 1
    while step < count:
        route = [(i, i ^ step) for i in range(count)]
        part = part + lax.ppermute(part, axes, route)
        step *= 2
    return part


def shifted(block, axis, distance):
    devices = range(lax.axis_size(axis))
    route = [(i - distance, i) for i in devices if i - distance in devices]
    return lax.ppermute(block, axis, route)


def stacked_heads(ref, group, group_size):
    return jnp.concatenate(
        [ref[:, (group * group_size + h) * HEAD_SIZE : (group * group_size + h + 1) * HEAD_SIZE] for h in range(group_size)],
        axis=0,
    )


def window_kernel(info_ref, q_ref, c_ref, k_ref, v_ref, wout_ref, wdq_ref, halo_ref, own_ref):
    group_size = QUERY_HEADS // KEY_VALUE_HEADS
    token_rows = q_ref.shape[0]
    window_rows = k_ref.shape[0]
    padding_rows = window_rows - token_rows
    scale = HEAD_SIZE ** (-0.5)
    stacked_rows = group_size * token_rows
    row = lax.broadcasted_iota(jnp.int32, (stacked_rows, window_rows), 0) % token_rows
    col = lax.broadcasted_iota(jnp.int32, (stacked_rows, window_rows), 1)
    back = row + padding_rows - col
    base = lax.axis_index("ctx") * token_rows - padding_rows
    seen = (back >= 0) & (col + base >= 0)
    for g in range(KEY_VALUE_HEADS):
        visible = seen & (back < info_ref[g])
        lanes = slice(g * HEAD_SIZE, (g + 1) * HEAD_SIZE)
        kg = k_ref[:, lanes]
        vg = v_ref[:, lanes]
        qs = stacked_heads(q_ref, g, group_size)
        cs = stacked_heads(c_ref, g, group_size)
        s = lax.dot_general(qs, kg, (((1,), (1,)), ((), ())), preferred_element_type=jnp.float32) * scale
        s = jnp.where(visible, s, -1e30)
        top = jnp.max(s, axis=-1, keepdims=True)
        e = jnp.exp(s - top)
        p = e * (1.0 / jnp.sum(e, axis=-1, keepdims=True))
        ph = p.astype(jnp.bfloat16)
        wout = jnp.dot(ph, vg, preferred_element_type=jnp.float32)
        gp = lax.dot_general(cs, vg, (((1,), (1,)), ((), ())), preferred_element_type=jnp.float32)
        delta = jnp.sum(cs.astype(jnp.float32) * wout, axis=-1, keepdims=True)
        ds = (p * (gp - delta) * scale).astype(jnp.bfloat16)
        wdq = jnp.dot(ds, kg, preferred_element_type=jnp.float32)
        for h in range(group_size):
            cols = slice((g * group_size + h) * HEAD_SIZE, (g * group_size + h + 1) * HEAD_SIZE)
            rows = slice(h * token_rows, (h + 1) * token_rows)
            wout_ref[:, cols] = wout[rows]
            wdq_ref[:, cols] = wdq[rows]
        dk = lax.dot_general(ds, qs, (((0,), (0,)), ((), ())), preferred_element_type=jnp.float32)
        dv = lax.dot_general(ph, cs, (((0,), (0,)), ((), ())), preferred_element_type=jnp.float32)
        value_lanes = slice(KEY_VALUE_HEADS * HEAD_SIZE + g * HEAD_SIZE, KEY_VALUE_HEADS * HEAD_SIZE + (g + 1) * HEAD_SIZE)
        reach = padding_rows // token_rows
        for distance in range(1, reach + 1):
            start_row = (reach - distance) * token_rows
            halo_ref[distance - 1, :, lanes] = dk[start_row : start_row + token_rows].astype(halo_ref.dtype)
            halo_ref[distance - 1, :, value_lanes] = dv[start_row : start_row + token_rows].astype(halo_ref.dtype)
        own_ref[:, lanes] = dk[padding_rows:]
        own_ref[:, value_lanes] = dv[padding_rows:]


def linear_scores(q_ref, k_ref, group, group_size, causal):
    lanes = slice(group * HEAD_SIZE, (group + 1) * HEAD_SIZE)
    qs = stacked_heads(q_ref, group, group_size)
    kg = k_ref[:, lanes]
    lh = jnp.where(
        causal,
        lax.dot_general(qs, kg, (((1,), (1,)), ((), ())), preferred_element_type=jnp.float32),
        0.0,
    ).astype(jnp.bfloat16)
    return qs, kg, lh


def causal_mask(token_rows, group_size):
    stacked_rows = group_size * token_rows
    row = lax.broadcasted_iota(jnp.int32, (stacked_rows, token_rows), 0) % token_rows
    col = lax.broadcasted_iota(jnp.int32, (stacked_rows, token_rows), 1)
    return row >= col


def linear_forward_kernel(q_ref, c_ref, k_ref, s_ref, prior_ref, gain_ref, wout_ref,
                          mixed_ref, dl_ref, riding_ref):
    group_size = QUERY_HEADS // KEY_VALUE_HEADS
    token_rows = q_ref.shape[0]
    causal = causal_mask(token_rows, group_size)
    gain_rows = []
    for g in range(KEY_VALUE_HEADS):
        lanes = slice(g * HEAD_SIZE, (g + 1) * HEAD_SIZE)
        sg = s_ref[:, lanes]
        pg = prior_ref[g]
        qs, kg, lh = linear_scores(q_ref, k_ref, g, group_size, causal)
        cs = stacked_heads(c_ref, g, group_size).astype(jnp.float32)
        gs = jnp.concatenate(
            [
                jnp.broadcast_to(
                    gain_ref[(g * group_size + h) * HEAD_SIZE : (g * group_size + h + 1) * HEAD_SIZE][None, :],
                    (token_rows, HEAD_SIZE),
                )
                for h in range(group_size)
            ],
            axis=0,
        )
        lin = jnp.dot(lh, sg, preferred_element_type=jnp.float32) + jnp.dot(
            qs, pg, preferred_element_type=jnp.float32
        )
        inverse_root = 1.0 / jnp.sqrt(jnp.mean(lin * lin, axis=-1, keepdims=True) + epsilon)
        normed = lin * inverse_root
        gn = gs * normed
        weighted = cs * normed
        scaled = cs * gs
        dl = ((scaled - normed * jnp.mean(scaled * normed, axis=-1, keepdims=True)) * inverse_root).astype(
            jnp.bfloat16
        )
        dl_ref[g] = dl
        riding_ref[g * HEAD_SIZE : (g + 1) * HEAD_SIZE, :] = lax.dot_general(
            qs, dl, (((0,), (0,)), ((), ())), preferred_element_type=jnp.float32
        ).astype(riding_ref.dtype)
        for h in range(group_size):
            cols = slice((g * group_size + h) * HEAD_SIZE, (g * group_size + h + 1) * HEAD_SIZE)
            rows = slice(h * token_rows, (h + 1) * token_rows)
            mixed_ref[:, cols] = (gn[rows] + wout_ref[:, cols]).astype(mixed_ref.dtype)
            gain_rows.append(jnp.sum(weighted[rows], axis=0, keepdims=True))
    state_rows = KEY_VALUE_HEADS * HEAD_SIZE
    spare = riding_ref.shape[0] - state_rows - len(gain_rows)
    riding_ref[state_rows:, :] = jnp.concatenate(
        gain_rows + [jnp.zeros((spare, HEAD_SIZE), jnp.float32)], axis=0
    ).astype(riding_ref.dtype)


def linear_backward_kernel(q_ref, k_ref, s_ref, prior_ref, dl_ref, wdq_ref, dq_ref, ldk_ref, dsp_ref):
    group_size = QUERY_HEADS // KEY_VALUE_HEADS
    token_rows = q_ref.shape[0]
    causal = causal_mask(token_rows, group_size)
    for g in range(KEY_VALUE_HEADS):
        lanes = slice(g * HEAD_SIZE, (g + 1) * HEAD_SIZE)
        sg = s_ref[:, lanes]
        pg = prior_ref[g]
        qs, kg, lh = linear_scores(q_ref, k_ref, g, group_size, causal)
        dl = dl_ref[g]
        bh = jnp.where(
            causal,
            lax.dot_general(dl, sg, (((1,), (1,)), ((), ())), preferred_element_type=jnp.float32),
            0.0,
        ).astype(jnp.bfloat16)
        ldq = lax.dot_general(dl, pg, (((1,), (1,)), ((), ())), preferred_element_type=jnp.float32)
        ldq = ldq + jnp.dot(bh, kg, preferred_element_type=jnp.float32)
        for h in range(group_size):
            cols = slice((g * group_size + h) * HEAD_SIZE, (g * group_size + h + 1) * HEAD_SIZE)
            rows = slice(h * token_rows, (h + 1) * token_rows)
            dq_ref[:, cols] = (ldq[rows] + wdq_ref[:, cols]).astype(dq_ref.dtype)
        ldk_ref[:, lanes] = lax.dot_general(bh, qs, (((0,), (0,)), ((), ())), preferred_element_type=jnp.float32)
        dsp_ref[:, lanes] = lax.dot_general(lh, dl, (((0,), (0,)), ((), ())), preferred_element_type=jnp.float32)


def in_vmem(count):
    return [pl.BlockSpec(memory_space=pltpu.VMEM)] * count


def per_device(queries, keys, values, spikes, window_lengths, gain, cotangent):
    token_rows = queries.shape[1]
    width = QUERY_HEADS * HEAD_SIZE
    reach = (WINDOW_REACH + token_rows - 2) // token_rows
    padding_rows = reach * token_rows
    window_rows = (reach + 1) * token_rows
    key_value_width = KEY_VALUE_HEADS * HEAD_SIZE
    q = queries[0]
    c = cotangent[0]
    k = keys[0]
    v = values[0]
    counts = jnp.repeat(spikes[0].astype(jnp.float32), HEAD_SIZE, axis=1)
    spiked = (v.astype(jnp.float32) * counts).astype(jnp.bfloat16)
    def state_of(block_keys, block_spiked):
        return jnp.stack(
            [
                lax.dot_general(
                    block_keys[:, g * HEAD_SIZE : (g + 1) * HEAD_SIZE],
                    block_spiked[:, g * HEAD_SIZE : (g + 1) * HEAD_SIZE],
                    (((0,), (0,)), ((), ())),
                    preferred_element_type=jnp.float32,
                )
                for g in range(KEY_VALUE_HEADS)
            ]
        )

    count_lanes = HEAD_SIZE
    spike_block = jnp.concatenate(
        [
            spikes[0].astype(jnp.bfloat16),
            jnp.zeros((token_rows, count_lanes - KEY_VALUE_HEADS), jnp.bfloat16),
        ],
        axis=1,
    )
    packed = jnp.concatenate([k, v, spike_block], axis=1)
    earlier = []
    for distance in range(reach, 0, -1):
        earlier.append(shifted(packed, "ctx", distance))
    near = jnp.zeros((KEY_VALUE_HEADS, HEAD_SIZE, HEAD_SIZE), jnp.float32)
    for piece in earlier:
        piece_counts = jnp.repeat(
            piece[:, 2 * key_value_width : 2 * key_value_width + KEY_VALUE_HEADS].astype(jnp.float32),
            HEAD_SIZE,
            axis=1,
        )
        piece_spiked = (
            piece[:, key_value_width : 2 * key_value_width].astype(jnp.float32) * piece_counts
        ).astype(jnp.bfloat16)
        near = near + state_of(piece[:, :key_value_width], piece_spiked)
    own_and_near = near + state_of(k, spiked)
    prior_half = spread_scan(near, own_and_near, "ctx").astype(jnp.bfloat16)
    window_packed = jnp.concatenate(
        [piece[:, : 2 * key_value_width] for piece in earlier] + [jnp.concatenate([k, v], axis=1)], axis=0
    )
    wout, wdq, halo_out, own_grad = pl.pallas_call(
        window_kernel,
        out_shape=(
            jax.ShapeDtypeStruct((token_rows, width), jnp.float32),
            jax.ShapeDtypeStruct((token_rows, width), jnp.float32),
            jax.ShapeDtypeStruct((reach, token_rows, 2 * key_value_width), jnp.bfloat16),
            jax.ShapeDtypeStruct((token_rows, 2 * key_value_width), jnp.float32),
        ),
        in_specs=[pl.BlockSpec(memory_space=pltpu.SMEM)] + in_vmem(4),
        out_specs=tuple(in_vmem(4)),
        cost_estimate=pl.CostEstimate(
            flops=12 * QUERY_HEADS * token_rows * window_rows * HEAD_SIZE,
            transcendentals=QUERY_HEADS * token_rows * window_rows,
            bytes_accessed=2 * token_rows * width * (2 + 4) + 2 * window_rows * key_value_width * (2 + 4),
        ),
    )(window_lengths, q, c, window_packed[:, :key_value_width], window_packed[:, key_value_width:])
    state_rows = KEY_VALUE_HEADS * HEAD_SIZE
    gain_rows = width // HEAD_SIZE
    riding_rows = state_rows + gain_rows + (-(state_rows + gain_rows)) % 16
    group_size = QUERY_HEADS // KEY_VALUE_HEADS
    mixed, d_linear, riding = pl.pallas_call(
        linear_forward_kernel,
        out_shape=(
            jax.ShapeDtypeStruct((token_rows, width), jnp.bfloat16),
            jax.ShapeDtypeStruct((KEY_VALUE_HEADS, group_size * token_rows, HEAD_SIZE), jnp.bfloat16),
            jax.ShapeDtypeStruct((riding_rows, HEAD_SIZE), jnp.bfloat16),
        ),
        in_specs=in_vmem(7),
        out_specs=tuple(in_vmem(3)),
        cost_estimate=pl.CostEstimate(
            flops=8 * QUERY_HEADS * token_rows * token_rows * HEAD_SIZE,
            transcendentals=QUERY_HEADS * token_rows,
            bytes_accessed=token_rows * width * (2 + 2 + 4 + 2 + 2),
        ),
    )(q, c, k, spiked, prior_half, gain, wout)
    total_tokens = queries.shape[0] * lax.axis_size("dp") * token_rows * lax.axis_size("ctx")
    later_rows, total_rows, first_round = butterfly_scan(riding, "ctx", True)
    late_dl, _ = lax.optimization_barrier((d_linear, first_round))
    d_queries, ldk, dsp = pl.pallas_call(
        linear_backward_kernel,
        out_shape=(
            jax.ShapeDtypeStruct((token_rows, width), jnp.bfloat16),
            jax.ShapeDtypeStruct((token_rows, key_value_width), jnp.float32),
            jax.ShapeDtypeStruct((token_rows, key_value_width), jnp.float32),
        ),
        in_specs=in_vmem(6),
        out_specs=tuple(in_vmem(3)),
        cost_estimate=pl.CostEstimate(
            flops=12 * QUERY_HEADS * token_rows * token_rows * HEAD_SIZE,
            transcendentals=0,
            bytes_accessed=token_rows * width * (2 + 2 + 4 + 2) + 2 * token_rows * key_value_width * 4,
        ),
    )(q, k, spiked, prior_half, late_dl, wdq)
    later_half = later_rows[:state_rows].reshape(KEY_VALUE_HEADS, HEAD_SIZE, HEAD_SIZE).astype(jnp.bfloat16)
    gain_ctx = total_rows[state_rows : state_rows + gain_rows].reshape(width)
    d_gain = all_sum(gain_ctx, ("dp",)) * (total_tokens ** (-0.5))
    ldk_parts = []
    dsp_parts = []
    for g in range(KEY_VALUE_HEADS):
        lanes = slice(g * HEAD_SIZE, (g + 1) * HEAD_SIZE)
        ldk_parts.append(
            ldk[:, lanes]
            + lax.dot_general(
                spiked[:, lanes], later_half[g], (((1,), (1,)), ((), ())), preferred_element_type=jnp.float32
            )
        )
        dsp_parts.append(
            dsp[:, lanes] + jnp.dot(k[:, lanes], later_half[g], preferred_element_type=jnp.float32)
        )
    linear_key_gradient = jnp.concatenate(ldk_parts, axis=1)
    linear_value_gradient = jnp.concatenate(dsp_parts, axis=1) * counts
    received = own_grad
    for distance in range(1, reach + 1):
        received = received + shifted(halo_out[distance - 1], "ctx", -distance).astype(jnp.float32)
    keys_gradient = (
        linear_key_gradient + received[:, :key_value_width]
    ).astype(jnp.bfloat16)
    values_gradient = (
        linear_value_gradient + received[:, key_value_width:]
    ).astype(jnp.bfloat16)
    return (
        mixed[None],
        d_queries[None],
        keys_gradient[None],
        values_gradient[None],
        d_gain,
    )


def solution(mesh):
    placed = (
        P("dp", "ctx", None),
        P("dp", "ctx", None),
        P("dp", "ctx", None),
        P("dp", "ctx", None),
        P(),
        P(),
        P("dp", "ctx", None),
    )
    return jax.shard_map(
        per_device,
        mesh=mesh,
        in_specs=placed,
        out_specs=(
            P("dp", "ctx", None),
            P("dp", "ctx", None),
            P("dp", "ctx", None),
            P("dp", "ctx", None),
            P(),
        ),
        check_vma=False,
    )
```

```python
import jax
import jax.numpy as jnp
from jax import lax
from jax.experimental import pallas as pl
from jax.experimental.pallas import tpu as pltpu
from jax.sharding import PartitionSpec as P

QUERY_HEADS = 14
KEY_VALUE_HEADS = 2
HEAD_SIZE = 128
WINDOW_REACH = 256


epsilon = 1e-05


def exclusive_scan(part, axis, reverse):
    count = lax.axis_size(axis)
    running = part
    total = None
    distance = 1
    while distance < count:
        if reverse:
            route = [(i + distance, i) for i in range(count - distance)]
        else:
            route = [(i, i + distance) for i in range(count - distance)]
        got = lax.ppermute(running, axis, route)
        total = got if total is None else total + got
        if distance * 2 < count:
            running = running + got
        distance *= 2
    if total is None:
        total = jnp.zeros_like(part)
    return total


def butterfly_scan(part, axis, reverse):
    count = lax.axis_size(axis)
    place = lax.axis_index(axis)
    group = part
    before = jnp.zeros(part.shape, jnp.float32)
    step = 1
    while step < count:
        mine = group.astype(jnp.bfloat16)
        got = lax.ppermute(mine, axis, [(i, i ^ step) for i in range(count)]).astype(jnp.float32)
        partner = jnp.bitwise_xor(place, step)
        take = partner > place if reverse else partner < place
        before = before + jnp.where(take, got, 0.0)
        group = mine.astype(jnp.float32) + got
        step *= 2
    return before, group


def spread_scan(near, own, axis):
    count = lax.axis_size(axis)
    total = near
    running = own
    stride = 3
    while stride < count:
        parts = []
        for distance in (stride, 2 * stride):
            if distance < count:
                parts.append(shifted(running.astype(jnp.bfloat16), axis, distance).astype(jnp.float32))
        for got in parts:
            total = total + got
        if 3 * stride < count:
            for got in parts:
                running = running + got
        stride *= 3
    return total


def all_sum(part, axes):
    count = 1
    for axis in axes:
        count *= lax.axis_size(axis)
    step = 1
    while step < count:
        route = [(i, i ^ step) for i in range(count)]
        part = part + lax.ppermute(part, axes, route)
        step *= 2
    return part


def shifted(block, axis, distance):
    devices = range(lax.axis_size(axis))
    route = [(i - distance, i) for i in devices if i - distance in devices]
    return lax.ppermute(block, axis, route)


def stacked_heads(ref, group, group_size):
    return jnp.concatenate(
        [ref[:, (group * group_size + h) * HEAD_SIZE : (group * group_size + h + 1) * HEAD_SIZE] for h in range(group_size)],
        axis=0,
    )


def window_kernel(info_ref, q_ref, c_ref, k_ref, v_ref, wout_ref, wdq_ref, halo_ref, own_ref):
    group_size = QUERY_HEADS // KEY_VALUE_HEADS
    token_rows = q_ref.shape[0]
    window_rows = k_ref.shape[0]
    padding_rows = window_rows - token_rows
    scale = HEAD_SIZE ** (-0.5)
    stacked_rows = group_size * token_rows
    row = lax.broadcasted_iota(jnp.int32, (stacked_rows, window_rows), 0) % token_rows
    col = lax.broadcasted_iota(jnp.int32, (stacked_rows, window_rows), 1)
    back = row + padding_rows - col
    base = lax.axis_index("ctx") * token_rows - padding_rows
    seen = (back >= 0) & (col + base >= 0)
    for g in range(KEY_VALUE_HEADS):
        visible = seen & (back < info_ref[g])
        lanes = slice(g * HEAD_SIZE, (g + 1) * HEAD_SIZE)
        kg = k_ref[:, lanes]
        vg = v_ref[:, lanes]
        qs = stacked_heads(q_ref, g, group_size)
        cs = stacked_heads(c_ref, g, group_size)
        s = lax.dot_general(qs, kg, (((1,), (1,)), ((), ())), preferred_element_type=jnp.float32) * scale
        s = jnp.where(visible, s, -1e30)
        top = jnp.max(s, axis=-1, keepdims=True)
        e = jnp.exp(s - top)
        p = e * (1.0 / jnp.sum(e, axis=-1, keepdims=True))
        ph = p.astype(jnp.bfloat16)
        wout = jnp.dot(ph, vg, preferred_element_type=jnp.float32)
        gp = lax.dot_general(cs, vg, (((1,), (1,)), ((), ())), preferred_element_type=jnp.float32)
        delta = jnp.sum(cs.astype(jnp.float32) * wout, axis=-1, keepdims=True)
        ds = (p * (gp - delta) * scale).astype(jnp.bfloat16)
        wdq = jnp.dot(ds, kg, preferred_element_type=jnp.float32)
        for h in range(group_size):
            cols = slice((g * group_size + h) * HEAD_SIZE, (g * group_size + h + 1) * HEAD_SIZE)
            rows = slice(h * token_rows, (h + 1) * token_rows)
            wout_ref[:, cols] = wout[rows]
            wdq_ref[:, cols] = wdq[rows]
        dk = lax.dot_general(ds, qs, (((0,), (0,)), ((), ())), preferred_element_type=jnp.float32)
        dv = lax.dot_general(ph, cs, (((0,), (0,)), ((), ())), preferred_element_type=jnp.float32)
        value_lanes = slice(KEY_VALUE_HEADS * HEAD_SIZE + g * HEAD_SIZE, KEY_VALUE_HEADS * HEAD_SIZE + (g + 1) * HEAD_SIZE)
        reach = padding_rows // token_rows
        for distance in range(1, reach + 1):
            start_row = (reach - distance) * token_rows
            halo_ref[distance - 1, :, lanes] = dk[start_row : start_row + token_rows].astype(halo_ref.dtype)
            halo_ref[distance - 1, :, value_lanes] = dv[start_row : start_row + token_rows].astype(halo_ref.dtype)
        own_ref[:, lanes] = dk[padding_rows:]
        own_ref[:, value_lanes] = dv[padding_rows:]


def linear_kernel(q_ref, c_ref, k_ref, s_ref, prior_ref, gain_ref, wout_ref, wdq_ref,
                  mixed_ref, dq_ref, riding_ref, ldk_ref, dsp_ref):
    group_size = QUERY_HEADS // KEY_VALUE_HEADS
    token_rows = q_ref.shape[0]
    stacked_rows = group_size * token_rows
    row = lax.broadcasted_iota(jnp.int32, (stacked_rows, token_rows), 0) % token_rows
    col = lax.broadcasted_iota(jnp.int32, (stacked_rows, token_rows), 1)
    causal = row >= col
    gain_rows = []
    for g in range(KEY_VALUE_HEADS):
        lanes = slice(g * HEAD_SIZE, (g + 1) * HEAD_SIZE)
        kg = k_ref[:, lanes]
        sg = s_ref[:, lanes]
        pg = prior_ref[g]
        qs = stacked_heads(q_ref, g, group_size)
        cs = stacked_heads(c_ref, g, group_size).astype(jnp.float32)
        gs = jnp.concatenate(
            [
                jnp.broadcast_to(
                    gain_ref[(g * group_size + h) * HEAD_SIZE : (g * group_size + h + 1) * HEAD_SIZE][None, :],
                    (token_rows, HEAD_SIZE),
                )
                for h in range(group_size)
            ],
            axis=0,
        )
        lh = jnp.where(
            causal,
            lax.dot_general(qs, kg, (((1,), (1,)), ((), ())), preferred_element_type=jnp.float32),
            0.0,
        ).astype(jnp.bfloat16)
        lin = jnp.dot(lh, sg, preferred_element_type=jnp.float32) + jnp.dot(
            qs, pg, preferred_element_type=jnp.float32
        )
        inverse_root = 1.0 / jnp.sqrt(jnp.mean(lin * lin, axis=-1, keepdims=True) + epsilon)
        normed = lin * inverse_root
        gn = gs * normed
        weighted = cs * normed
        scaled = cs * gs
        dl = ((scaled - normed * jnp.mean(scaled * normed, axis=-1, keepdims=True)) * inverse_root).astype(
            jnp.bfloat16
        )
        riding_ref[g * HEAD_SIZE : (g + 1) * HEAD_SIZE, :] = lax.dot_general(
            qs, dl, (((0,), (0,)), ((), ())), preferred_element_type=jnp.float32
        ).astype(riding_ref.dtype)
        bh = jnp.where(
            causal,
            lax.dot_general(dl, sg, (((1,), (1,)), ((), ())), preferred_element_type=jnp.float32),
            0.0,
        ).astype(jnp.bfloat16)
        ldq = lax.dot_general(dl, pg, (((1,), (1,)), ((), ())), preferred_element_type=jnp.float32)
        ldq = ldq + jnp.dot(bh, kg, preferred_element_type=jnp.float32)
        for h in range(group_size):
            cols = slice((g * group_size + h) * HEAD_SIZE, (g * group_size + h + 1) * HEAD_SIZE)
            rows = slice(h * token_rows, (h + 1) * token_rows)
            mixed_ref[:, cols] = (gn[rows] + wout_ref[:, cols]).astype(mixed_ref.dtype)
            gain_rows.append(jnp.sum(weighted[rows], axis=0, keepdims=True))
            dq_ref[:, cols] = (ldq[rows] + wdq_ref[:, cols]).astype(dq_ref.dtype)
        ldk_ref[:, lanes] = lax.dot_general(bh, qs, (((0,), (0,)), ((), ())), preferred_element_type=jnp.float32)
        dsp_ref[:, lanes] = lax.dot_general(lh, dl, (((0,), (0,)), ((), ())), preferred_element_type=jnp.float32)
    state_rows = KEY_VALUE_HEADS * HEAD_SIZE
    spare = riding_ref.shape[0] - state_rows - len(gain_rows)
    riding_ref[state_rows:, :] = jnp.concatenate(
        gain_rows + [jnp.zeros((spare, HEAD_SIZE), jnp.float32)], axis=0
    ).astype(riding_ref.dtype)


def in_vmem(count):
    return [pl.BlockSpec(memory_space=pltpu.VMEM)] * count


def per_device(queries, keys, values, spikes, window_lengths, gain, cotangent):
    token_rows = queries.shape[1]
    width = QUERY_HEADS * HEAD_SIZE
    reach = (WINDOW_REACH + token_rows - 2) // token_rows
    padding_rows = reach * token_rows
    window_rows = (reach + 1) * token_rows
    key_value_width = KEY_VALUE_HEADS * HEAD_SIZE
    q = queries[0]
    c = cotangent[0]
    k = keys[0]
    v = values[0]
    counts = jnp.repeat(spikes[0].astype(jnp.float32), HEAD_SIZE, axis=1)
    spiked = (v.astype(jnp.float32) * counts).astype(jnp.bfloat16)
    def state_of(block_keys, block_spiked):
        return jnp.stack(
            [
                lax.dot_general(
                    block_keys[:, g * HEAD_SIZE : (g + 1) * HEAD_SIZE],
                    block_spiked[:, g * HEAD_SIZE : (g + 1) * HEAD_SIZE],
                    (((0,), (0,)), ((), ())),
                    preferred_element_type=jnp.float32,
                )
                for g in range(KEY_VALUE_HEADS)
            ]
        )

    count_lanes = HEAD_SIZE
    spike_block = jnp.concatenate(
        [
            spikes[0].astype(jnp.bfloat16),
            jnp.zeros((token_rows, count_lanes - KEY_VALUE_HEADS), jnp.bfloat16),
        ],
        axis=1,
    )
    packed = jnp.concatenate([k, v, spike_block], axis=1)
    earlier = []
    for distance in range(reach, 0, -1):
        earlier.append(shifted(packed, "ctx", distance))
    near = jnp.zeros((KEY_VALUE_HEADS, HEAD_SIZE, HEAD_SIZE), jnp.float32)
    for piece in earlier:
        piece_counts = jnp.repeat(
            piece[:, 2 * key_value_width : 2 * key_value_width + KEY_VALUE_HEADS].astype(jnp.float32),
            HEAD_SIZE,
            axis=1,
        )
        piece_spiked = (
            piece[:, key_value_width : 2 * key_value_width].astype(jnp.float32) * piece_counts
        ).astype(jnp.bfloat16)
        near = near + state_of(piece[:, :key_value_width], piece_spiked)
    own_and_near = near + state_of(k, spiked)
    prior_half = spread_scan(near, own_and_near, "ctx").astype(jnp.bfloat16)
    window_packed = jnp.concatenate(
        [piece[:, : 2 * key_value_width] for piece in earlier] + [jnp.concatenate([k, v], axis=1)], axis=0
    )
    wout, wdq, halo_out, own_grad = pl.pallas_call(
        window_kernel,
        out_shape=(
            jax.ShapeDtypeStruct((token_rows, width), jnp.float32),
            jax.ShapeDtypeStruct((token_rows, width), jnp.float32),
            jax.ShapeDtypeStruct((reach, token_rows, 2 * key_value_width), jnp.bfloat16),
            jax.ShapeDtypeStruct((token_rows, 2 * key_value_width), jnp.float32),
        ),
        in_specs=[pl.BlockSpec(memory_space=pltpu.SMEM)] + in_vmem(4),
        out_specs=tuple(in_vmem(4)),
        cost_estimate=pl.CostEstimate(
            flops=12 * QUERY_HEADS * token_rows * window_rows * HEAD_SIZE,
            transcendentals=QUERY_HEADS * token_rows * window_rows,
            bytes_accessed=2 * token_rows * width * (2 + 4) + 2 * window_rows * key_value_width * (2 + 4),
        ),
    )(window_lengths, q, c, window_packed[:, :key_value_width], window_packed[:, key_value_width:])
    state_rows = KEY_VALUE_HEADS * HEAD_SIZE
    gain_rows = width // HEAD_SIZE
    riding_rows = state_rows + gain_rows + (-(state_rows + gain_rows)) % 16
    mixed, d_queries, riding, ldk, dsp = pl.pallas_call(
        linear_kernel,
        out_shape=(
            jax.ShapeDtypeStruct((token_rows, width), jnp.bfloat16),
            jax.ShapeDtypeStruct((token_rows, width), jnp.bfloat16),
            jax.ShapeDtypeStruct((riding_rows, HEAD_SIZE), jnp.bfloat16),
            jax.ShapeDtypeStruct((token_rows, key_value_width), jnp.float32),
            jax.ShapeDtypeStruct((token_rows, key_value_width), jnp.float32),
        ),
        in_specs=in_vmem(8),
        out_specs=tuple(in_vmem(5)),
        cost_estimate=pl.CostEstimate(
            flops=20 * QUERY_HEADS * token_rows * token_rows * HEAD_SIZE,
            transcendentals=QUERY_HEADS * token_rows,
            bytes_accessed=token_rows * width * (2 + 2 + 4 + 4 + 2 + 2) + 6 * token_rows * key_value_width * 4,
        ),
    )(q, c, k, spiked, prior_half, gain, wout, wdq)
    total_tokens = queries.shape[0] * lax.axis_size("dp") * token_rows * lax.axis_size("ctx")
    later_rows, total_rows = butterfly_scan(riding, "ctx", True)
    later_half = later_rows[:state_rows].reshape(KEY_VALUE_HEADS, HEAD_SIZE, HEAD_SIZE).astype(jnp.bfloat16)
    gain_ctx = total_rows[state_rows : state_rows + gain_rows].reshape(width)
    d_gain = all_sum(gain_ctx, ("dp",)) * (total_tokens ** (-0.5))
    ldk_parts = []
    dsp_parts = []
    for g in range(KEY_VALUE_HEADS):
        lanes = slice(g * HEAD_SIZE, (g + 1) * HEAD_SIZE)
        ldk_parts.append(
            ldk[:, lanes]
            + lax.dot_general(
                spiked[:, lanes], later_half[g], (((1,), (1,)), ((), ())), preferred_element_type=jnp.float32
            )
        )
        dsp_parts.append(
            dsp[:, lanes] + jnp.dot(k[:, lanes], later_half[g], preferred_element_type=jnp.float32)
        )
    linear_key_gradient = jnp.concatenate(ldk_parts, axis=1)
    linear_value_gradient = jnp.concatenate(dsp_parts, axis=1) * counts
    received = own_grad
    for distance in range(1, reach + 1):
        received = received + shifted(halo_out[distance - 1], "ctx", -distance).astype(jnp.float32)
    keys_gradient = (
        linear_key_gradient + received[:, :key_value_width]
    ).astype(jnp.bfloat16)
    values_gradient = (
        linear_value_gradient + received[:, key_value_width:]
    ).astype(jnp.bfloat16)
    return (
        mixed[None],
        d_queries[None],
        keys_gradient[None],
        values_gradient[None],
        d_gain,
    )


def solution(mesh):
    placed = (
        P("dp", "ctx", None),
        P("dp", "ctx", None),
        P("dp", "ctx", None),
        P("dp", "ctx", None),
        P(),
        P(),
        P("dp", "ctx", None),
    )
    return jax.shard_map(
        per_device,
        mesh=mesh,
        in_specs=placed,
        out_specs=(
            P("dp", "ctx", None),
            P("dp", "ctx", None),
            P("dp", "ctx", None),
            P("dp", "ctx", None),
            P(),
        ),
        check_vma=False,
    )
```

```python
import jax
import jax.numpy as jnp
from jax import lax
from jax.experimental import pallas as pl
from jax.experimental.pallas import tpu as pltpu
from jax.sharding import PartitionSpec as P

QUERY_HEADS = 14
KEY_VALUE_HEADS = 2
HEAD_SIZE = 128
WINDOW_REACH = 256


epsilon = 1e-05


def exclusive_scan(part, axis, reverse):
    count = lax.axis_size(axis)
    running = part
    total = None
    distance = 1
    while distance < count:
        if reverse:
            route = [(i + distance, i) for i in range(count - distance)]
        else:
            route = [(i, i + distance) for i in range(count - distance)]
        got = lax.ppermute(running, axis, route)
        total = got if total is None else total + got
        if distance * 2 < count:
            running = running + got
        distance *= 2
    if total is None:
        total = jnp.zeros_like(part)
    return total


def butterfly_scan(part, axis, reverse):
    count = lax.axis_size(axis)
    place = lax.axis_index(axis)
    group = part
    before = jnp.zeros(part.shape, jnp.float32)
    step = 1
    while step < count:
        mine = group.astype(jnp.bfloat16)
        got = lax.ppermute(mine, axis, [(i, i ^ step) for i in range(count)]).astype(jnp.float32)
        partner = jnp.bitwise_xor(place, step)
        take = partner > place if reverse else partner < place
        before = before + jnp.where(take, got, 0.0)
        group = mine.astype(jnp.float32) + got
        step *= 2
    return before, group


def spread_scan(near, own, axis):
    count = lax.axis_size(axis)
    total = near
    running = own
    stride = 3
    while stride < count:
        parts = []
        for distance in (stride, 2 * stride):
            if distance < count:
                parts.append(shifted(running, axis, distance))
        for got in parts:
            total = total + got
        if 3 * stride < count:
            for got in parts:
                running = running + got
        stride *= 3
    return total


def all_sum(part, axes):
    count = 1
    for axis in axes:
        count *= lax.axis_size(axis)
    step = 1
    while step < count:
        route = [(i, i ^ step) for i in range(count)]
        part = part + lax.ppermute(part, axes, route)
        step *= 2
    return part


def shifted(block, axis, distance):
    devices = range(lax.axis_size(axis))
    route = [(i - distance, i) for i in devices if i - distance in devices]
    return lax.ppermute(block, axis, route)


def stacked_heads(ref, group, group_size):
    return jnp.concatenate(
        [ref[:, (group * group_size + h) * HEAD_SIZE : (group * group_size + h + 1) * HEAD_SIZE] for h in range(group_size)],
        axis=0,
    )


def window_kernel(info_ref, q_ref, c_ref, k_ref, v_ref, wout_ref, wdq_ref, halo_ref, own_ref):
    group_size = QUERY_HEADS // KEY_VALUE_HEADS
    token_rows = q_ref.shape[0]
    window_rows = k_ref.shape[0]
    padding_rows = window_rows - token_rows
    scale = HEAD_SIZE ** (-0.5)
    stacked_rows = group_size * token_rows
    row = lax.broadcasted_iota(jnp.int32, (stacked_rows, window_rows), 0) % token_rows
    col = lax.broadcasted_iota(jnp.int32, (stacked_rows, window_rows), 1)
    back = row + padding_rows - col
    base = lax.axis_index("ctx") * token_rows - padding_rows
    seen = (back >= 0) & (col + base >= 0)
    for g in range(KEY_VALUE_HEADS):
        visible = seen & (back < info_ref[g])
        lanes = slice(g * HEAD_SIZE, (g + 1) * HEAD_SIZE)
        kg = k_ref[:, lanes]
        vg = v_ref[:, lanes]
        qs = stacked_heads(q_ref, g, group_size)
        cs = stacked_heads(c_ref, g, group_size)
        s = lax.dot_general(qs, kg, (((1,), (1,)), ((), ())), preferred_element_type=jnp.float32) * scale
        s = jnp.where(visible, s, -1e30)
        top = jnp.max(s, axis=-1, keepdims=True)
        e = jnp.exp(s - top)
        p = e * (1.0 / jnp.sum(e, axis=-1, keepdims=True))
        ph = p.astype(jnp.bfloat16)
        wout = jnp.dot(ph, vg, preferred_element_type=jnp.float32)
        gp = lax.dot_general(cs, vg, (((1,), (1,)), ((), ())), preferred_element_type=jnp.float32)
        delta = jnp.sum(cs.astype(jnp.float32) * wout, axis=-1, keepdims=True)
        ds = (p * (gp - delta) * scale).astype(jnp.bfloat16)
        wdq = jnp.dot(ds, kg, preferred_element_type=jnp.float32)
        for h in range(group_size):
            cols = slice((g * group_size + h) * HEAD_SIZE, (g * group_size + h + 1) * HEAD_SIZE)
            rows = slice(h * token_rows, (h + 1) * token_rows)
            wout_ref[:, cols] = wout[rows]
            wdq_ref[:, cols] = wdq[rows]
        dk = lax.dot_general(ds, qs, (((0,), (0,)), ((), ())), preferred_element_type=jnp.float32)
        dv = lax.dot_general(ph, cs, (((0,), (0,)), ((), ())), preferred_element_type=jnp.float32)
        value_lanes = slice(KEY_VALUE_HEADS * HEAD_SIZE + g * HEAD_SIZE, KEY_VALUE_HEADS * HEAD_SIZE + (g + 1) * HEAD_SIZE)
        reach = padding_rows // token_rows
        for distance in range(1, reach + 1):
            start_row = (reach - distance) * token_rows
            halo_ref[distance - 1, :, lanes] = dk[start_row : start_row + token_rows].astype(halo_ref.dtype)
            halo_ref[distance - 1, :, value_lanes] = dv[start_row : start_row + token_rows].astype(halo_ref.dtype)
        own_ref[:, lanes] = dk[padding_rows:]
        own_ref[:, value_lanes] = dv[padding_rows:]


def linear_kernel(q_ref, c_ref, k_ref, s_ref, prior_ref, gain_ref, wout_ref, wdq_ref,
                  mixed_ref, dq_ref, riding_ref, ldk_ref, dsp_ref):
    group_size = QUERY_HEADS // KEY_VALUE_HEADS
    token_rows = q_ref.shape[0]
    stacked_rows = group_size * token_rows
    row = lax.broadcasted_iota(jnp.int32, (stacked_rows, token_rows), 0) % token_rows
    col = lax.broadcasted_iota(jnp.int32, (stacked_rows, token_rows), 1)
    causal = row >= col
    gain_rows = []
    for g in range(KEY_VALUE_HEADS):
        lanes = slice(g * HEAD_SIZE, (g + 1) * HEAD_SIZE)
        kg = k_ref[:, lanes]
        sg = s_ref[:, lanes]
        pg = prior_ref[g]
        qs = stacked_heads(q_ref, g, group_size)
        cs = stacked_heads(c_ref, g, group_size).astype(jnp.float32)
        gs = jnp.concatenate(
            [
                jnp.broadcast_to(
                    gain_ref[(g * group_size + h) * HEAD_SIZE : (g * group_size + h + 1) * HEAD_SIZE][None, :],
                    (token_rows, HEAD_SIZE),
                )
                for h in range(group_size)
            ],
            axis=0,
        )
        lh = jnp.where(
            causal,
            lax.dot_general(qs, kg, (((1,), (1,)), ((), ())), preferred_element_type=jnp.float32),
            0.0,
        ).astype(jnp.bfloat16)
        lin = jnp.dot(lh, sg, preferred_element_type=jnp.float32) + jnp.dot(
            qs, pg, preferred_element_type=jnp.float32
        )
        inverse_root = 1.0 / jnp.sqrt(jnp.mean(lin * lin, axis=-1, keepdims=True) + epsilon)
        normed = lin * inverse_root
        gn = gs * normed
        weighted = cs * normed
        scaled = cs * gs
        dl = ((scaled - normed * jnp.mean(scaled * normed, axis=-1, keepdims=True)) * inverse_root).astype(
            jnp.bfloat16
        )
        riding_ref[g * HEAD_SIZE : (g + 1) * HEAD_SIZE, :] = lax.dot_general(
            qs, dl, (((0,), (0,)), ((), ())), preferred_element_type=jnp.float32
        ).astype(riding_ref.dtype)
        bh = jnp.where(
            causal,
            lax.dot_general(dl, sg, (((1,), (1,)), ((), ())), preferred_element_type=jnp.float32),
            0.0,
        ).astype(jnp.bfloat16)
        ldq = lax.dot_general(dl, pg, (((1,), (1,)), ((), ())), preferred_element_type=jnp.float32)
        ldq = ldq + jnp.dot(bh, kg, preferred_element_type=jnp.float32)
        for h in range(group_size):
            cols = slice((g * group_size + h) * HEAD_SIZE, (g * group_size + h + 1) * HEAD_SIZE)
            rows = slice(h * token_rows, (h + 1) * token_rows)
            mixed_ref[:, cols] = (gn[rows] + wout_ref[:, cols]).astype(mixed_ref.dtype)
            gain_rows.append(jnp.sum(weighted[rows], axis=0, keepdims=True))
            dq_ref[:, cols] = (ldq[rows] + wdq_ref[:, cols]).astype(dq_ref.dtype)
        ldk_ref[:, lanes] = lax.dot_general(bh, qs, (((0,), (0,)), ((), ())), preferred_element_type=jnp.float32)
        dsp_ref[:, lanes] = lax.dot_general(lh, dl, (((0,), (0,)), ((), ())), preferred_element_type=jnp.float32)
    state_rows = KEY_VALUE_HEADS * HEAD_SIZE
    spare = riding_ref.shape[0] - state_rows - len(gain_rows)
    riding_ref[state_rows:, :] = jnp.concatenate(
        gain_rows + [jnp.zeros((spare, HEAD_SIZE), jnp.float32)], axis=0
    ).astype(riding_ref.dtype)


def in_vmem(count):
    return [pl.BlockSpec(memory_space=pltpu.VMEM)] * count


def per_device(queries, keys, values, spikes, window_lengths, gain, cotangent):
    token_rows = queries.shape[1]
    width = QUERY_HEADS * HEAD_SIZE
    reach = (WINDOW_REACH + token_rows - 2) // token_rows
    padding_rows = reach * token_rows
    window_rows = (reach + 1) * token_rows
    key_value_width = KEY_VALUE_HEADS * HEAD_SIZE
    q = queries[0]
    c = cotangent[0]
    k = keys[0]
    v = values[0]
    counts = jnp.repeat(spikes[0].astype(jnp.float32), HEAD_SIZE, axis=1)
    spiked = (v.astype(jnp.float32) * counts).astype(jnp.bfloat16)
    def state_of(block_keys, block_spiked):
        return jnp.stack(
            [
                lax.dot_general(
                    block_keys[:, g * HEAD_SIZE : (g + 1) * HEAD_SIZE],
                    block_spiked[:, g * HEAD_SIZE : (g + 1) * HEAD_SIZE],
                    (((0,), (0,)), ((), ())),
                    preferred_element_type=jnp.float32,
                )
                for g in range(KEY_VALUE_HEADS)
            ]
        )

    count_lanes = HEAD_SIZE
    spike_block = jnp.concatenate(
        [
            spikes[0].astype(jnp.bfloat16),
            jnp.zeros((token_rows, count_lanes - KEY_VALUE_HEADS), jnp.bfloat16),
        ],
        axis=1,
    )
    packed = jnp.concatenate([k, v, spike_block], axis=1)
    earlier = []
    for distance in range(reach, 0, -1):
        earlier.append(shifted(packed, "ctx", distance))
    near = jnp.zeros((KEY_VALUE_HEADS, HEAD_SIZE, HEAD_SIZE), jnp.float32)
    for piece in earlier:
        piece_counts = jnp.repeat(
            piece[:, 2 * key_value_width : 2 * key_value_width + KEY_VALUE_HEADS].astype(jnp.float32),
            HEAD_SIZE,
            axis=1,
        )
        piece_spiked = (
            piece[:, key_value_width : 2 * key_value_width].astype(jnp.float32) * piece_counts
        ).astype(jnp.bfloat16)
        near = near + state_of(piece[:, :key_value_width], piece_spiked)
    own_and_near = near + state_of(k, spiked)
    prior_half = spread_scan(near, own_and_near, "ctx").astype(jnp.bfloat16)
    window_packed = jnp.concatenate(
        [piece[:, : 2 * key_value_width] for piece in earlier] + [jnp.concatenate([k, v], axis=1)], axis=0
    )
    wout, wdq, halo_out, own_grad = pl.pallas_call(
        window_kernel,
        out_shape=(
            jax.ShapeDtypeStruct((token_rows, width), jnp.float32),
            jax.ShapeDtypeStruct((token_rows, width), jnp.float32),
            jax.ShapeDtypeStruct((reach, token_rows, 2 * key_value_width), jnp.bfloat16),
            jax.ShapeDtypeStruct((token_rows, 2 * key_value_width), jnp.float32),
        ),
        in_specs=[pl.BlockSpec(memory_space=pltpu.SMEM)] + in_vmem(4),
        out_specs=tuple(in_vmem(4)),
        cost_estimate=pl.CostEstimate(
            flops=12 * QUERY_HEADS * token_rows * window_rows * HEAD_SIZE,
            transcendentals=QUERY_HEADS * token_rows * window_rows,
            bytes_accessed=2 * token_rows * width * (2 + 4) + 2 * window_rows * key_value_width * (2 + 4),
        ),
    )(window_lengths, q, c, window_packed[:, :key_value_width], window_packed[:, key_value_width:])
    state_rows = KEY_VALUE_HEADS * HEAD_SIZE
    gain_rows = width // HEAD_SIZE
    riding_rows = state_rows + gain_rows + (-(state_rows + gain_rows)) % 16
    mixed, d_queries, riding, ldk, dsp = pl.pallas_call(
        linear_kernel,
        out_shape=(
            jax.ShapeDtypeStruct((token_rows, width), jnp.bfloat16),
            jax.ShapeDtypeStruct((token_rows, width), jnp.bfloat16),
            jax.ShapeDtypeStruct((riding_rows, HEAD_SIZE), jnp.bfloat16),
            jax.ShapeDtypeStruct((token_rows, key_value_width), jnp.float32),
            jax.ShapeDtypeStruct((token_rows, key_value_width), jnp.float32),
        ),
        in_specs=in_vmem(8),
        out_specs=tuple(in_vmem(5)),
        cost_estimate=pl.CostEstimate(
            flops=20 * QUERY_HEADS * token_rows * token_rows * HEAD_SIZE,
            transcendentals=QUERY_HEADS * token_rows,
            bytes_accessed=token_rows * width * (2 + 2 + 4 + 4 + 2 + 2) + 6 * token_rows * key_value_width * 4,
        ),
    )(q, c, k, spiked, prior_half, gain, wout, wdq)
    total_tokens = queries.shape[0] * lax.axis_size("dp") * token_rows * lax.axis_size("ctx")
    received = own_grad
    for distance in range(1, reach + 1):
        received = received + shifted(halo_out[distance - 1], "ctx", -distance).astype(jnp.float32)
    riding, received = lax.optimization_barrier((riding, received))
    later_rows, total_rows = butterfly_scan(riding, "ctx", True)
    later_half = later_rows[:state_rows].reshape(KEY_VALUE_HEADS, HEAD_SIZE, HEAD_SIZE).astype(jnp.bfloat16)
    gain_ctx = total_rows[state_rows : state_rows + gain_rows].reshape(width)
    d_gain = all_sum(gain_ctx, ("dp",)) * (total_tokens ** (-0.5))
    ldk_parts = []
    dsp_parts = []
    for g in range(KEY_VALUE_HEADS):
        lanes = slice(g * HEAD_SIZE, (g + 1) * HEAD_SIZE)
        ldk_parts.append(
            ldk[:, lanes]
            + lax.dot_general(
                spiked[:, lanes], later_half[g], (((1,), (1,)), ((), ())), preferred_element_type=jnp.float32
            )
        )
        dsp_parts.append(
            dsp[:, lanes] + jnp.dot(k[:, lanes], later_half[g], preferred_element_type=jnp.float32)
        )
    linear_key_gradient = jnp.concatenate(ldk_parts, axis=1)
    linear_value_gradient = jnp.concatenate(dsp_parts, axis=1) * counts
    keys_gradient = (
        linear_key_gradient + received[:, :key_value_width]
    ).astype(jnp.bfloat16)
    values_gradient = (
        linear_value_gradient + received[:, key_value_width:]
    ).astype(jnp.bfloat16)
    return (
        mixed[None],
        d_queries[None],
        keys_gradient[None],
        values_gradient[None],
        d_gain,
    )


def solution(mesh):
    placed = (
        P("dp", "ctx", None),
        P("dp", "ctx", None),
        P("dp", "ctx", None),
        P("dp", "ctx", None),
        P(),
        P(),
        P("dp", "ctx", None),
    )
    return jax.shard_map(
        per_device,
        mesh=mesh,
        in_specs=placed,
        out_specs=(
            P("dp", "ctx", None),
            P("dp", "ctx", None),
            P("dp", "ctx", None),
            P("dp", "ctx", None),
            P(),
        ),
        check_vma=False,
    )
```

```python
import functools

import jax
import jax.numpy as jnp
from jax import lax
from jax.experimental import pallas as pl
from jax.experimental.pallas import tpu as pltpu
from jax.sharding import PartitionSpec as P

QUERY_HEADS = 14
KEY_VALUE_HEADS = 2
HEAD_SIZE = 128
WINDOW_REACH = 256


epsilon = 1e-05


def exclusive_scan(part, axis, reverse):
    count = lax.axis_size(axis)
    running = part
    total = None
    distance = 1
    while distance < count:
        if reverse:
            route = [(i + distance, i) for i in range(count - distance)]
        else:
            route = [(i, i + distance) for i in range(count - distance)]
        got = lax.ppermute(running, axis, route)
        total = got if total is None else total + got
        if distance * 2 < count:
            running = running + got
        distance *= 2
    if total is None:
        total = jnp.zeros_like(part)
    return total


def butterfly_scan(part, axis, reverse):
    count = lax.axis_size(axis)
    place = lax.axis_index(axis)
    group = part
    before = jnp.zeros(part.shape, jnp.float32)
    step = 1
    while step < count:
        mine = group.astype(jnp.bfloat16)
        got = lax.ppermute(mine, axis, [(i, i ^ step) for i in range(count)]).astype(jnp.float32)
        partner = jnp.bitwise_xor(place, step)
        take = partner > place if reverse else partner < place
        before = before + jnp.where(take, got, 0.0)
        group = mine.astype(jnp.float32) + got
        step *= 2
    return before, group


def spread_scan(near, own, axis):
    count = lax.axis_size(axis)
    terms = [near]
    running = own
    stride = 3
    while stride < count:
        parts = []
        for distance in (stride, 2 * stride):
            if distance < count:
                parts.append(shifted(running, axis, distance))
        terms.extend(parts)
        if 3 * stride < count:
            for got in parts:
                running = running + got
        stride *= 3
    return terms


def all_sum(part, axes):
    count = 1
    for axis in axes:
        count *= lax.axis_size(axis)
    step = 1
    while step < count:
        route = [(i, i ^ step) for i in range(count)]
        part = part + lax.ppermute(part, axes, route)
        step *= 2
    return part


def shifted(block, axis, distance):
    devices = range(lax.axis_size(axis))
    route = [(i - distance, i) for i in devices if i - distance in devices]
    return lax.ppermute(block, axis, route)


def stacked_heads(ref, group, group_size):
    return jnp.concatenate(
        [ref[:, (group * group_size + h) * HEAD_SIZE : (group * group_size + h + 1) * HEAD_SIZE] for h in range(group_size)],
        axis=0,
    )


def window_kernel(info_ref, q_ref, c_ref, k_ref, v_ref, wout_ref, wdq_ref, halo_ref, own_ref):
    group_size = QUERY_HEADS // KEY_VALUE_HEADS
    token_rows = q_ref.shape[0]
    window_rows = k_ref.shape[0]
    padding_rows = window_rows - token_rows
    scale = HEAD_SIZE ** (-0.5)
    stacked_rows = group_size * token_rows
    row = lax.broadcasted_iota(jnp.int32, (stacked_rows, window_rows), 0) % token_rows
    col = lax.broadcasted_iota(jnp.int32, (stacked_rows, window_rows), 1)
    back = row + padding_rows - col
    base = lax.axis_index("ctx") * token_rows - padding_rows
    seen = (back >= 0) & (col + base >= 0)
    for g in range(KEY_VALUE_HEADS):
        visible = seen & (back < info_ref[g])
        lanes = slice(g * HEAD_SIZE, (g + 1) * HEAD_SIZE)
        kg = k_ref[:, lanes]
        vg = v_ref[:, lanes]
        qs = stacked_heads(q_ref, g, group_size)
        cs = stacked_heads(c_ref, g, group_size)
        s = lax.dot_general(qs, kg, (((1,), (1,)), ((), ())), preferred_element_type=jnp.float32) * scale
        s = jnp.where(visible, s, -1e30)
        top = jnp.max(s, axis=-1, keepdims=True)
        e = jnp.exp(s - top)
        p = e * (1.0 / jnp.sum(e, axis=-1, keepdims=True))
        ph = p.astype(jnp.bfloat16)
        wout = jnp.dot(ph, vg, preferred_element_type=jnp.float32)
        gp = lax.dot_general(cs, vg, (((1,), (1,)), ((), ())), preferred_element_type=jnp.float32)
        delta = jnp.sum(cs.astype(jnp.float32) * wout, axis=-1, keepdims=True)
        ds = (p * (gp - delta) * scale).astype(jnp.bfloat16)
        wdq = jnp.dot(ds, kg, preferred_element_type=jnp.float32)
        for h in range(group_size):
            cols = slice((g * group_size + h) * HEAD_SIZE, (g * group_size + h + 1) * HEAD_SIZE)
            rows = slice(h * token_rows, (h + 1) * token_rows)
            wout_ref[:, cols] = wout[rows]
            wdq_ref[:, cols] = wdq[rows]
        dk = lax.dot_general(ds, qs, (((0,), (0,)), ((), ())), preferred_element_type=jnp.float32)
        dv = lax.dot_general(ph, cs, (((0,), (0,)), ((), ())), preferred_element_type=jnp.float32)
        value_lanes = slice(KEY_VALUE_HEADS * HEAD_SIZE + g * HEAD_SIZE, KEY_VALUE_HEADS * HEAD_SIZE + (g + 1) * HEAD_SIZE)
        reach = padding_rows // token_rows
        for distance in range(1, reach + 1):
            start_row = (reach - distance) * token_rows
            halo_ref[distance - 1, :, lanes] = dk[start_row : start_row + token_rows].astype(halo_ref.dtype)
            halo_ref[distance - 1, :, value_lanes] = dv[start_row : start_row + token_rows].astype(halo_ref.dtype)
        own_ref[:, lanes] = dk[padding_rows:]
        own_ref[:, value_lanes] = dv[padding_rows:]


def linear_kernel(prior_count, q_ref, c_ref, k_ref, s_ref, *refs):
    prior_refs = refs[:prior_count]
    gain_ref, wout_ref, wdq_ref, mixed_ref, dq_ref, riding_ref, ldk_ref, dsp_ref = refs[prior_count:]
    group_size = QUERY_HEADS // KEY_VALUE_HEADS
    token_rows = q_ref.shape[0]
    stacked_rows = group_size * token_rows
    row = lax.broadcasted_iota(jnp.int32, (stacked_rows, token_rows), 0) % token_rows
    col = lax.broadcasted_iota(jnp.int32, (stacked_rows, token_rows), 1)
    causal = row >= col
    gain_rows = []
    for g in range(KEY_VALUE_HEADS):
        lanes = slice(g * HEAD_SIZE, (g + 1) * HEAD_SIZE)
        kg = k_ref[:, lanes]
        sg = s_ref[:, lanes]
        pg = prior_refs[0][g]
        for extra in prior_refs[1:]:
            pg = pg + extra[g]
        pg = pg.astype(jnp.bfloat16)
        qs = stacked_heads(q_ref, g, group_size)
        cs = stacked_heads(c_ref, g, group_size).astype(jnp.float32)
        gs = jnp.concatenate(
            [
                jnp.broadcast_to(
                    gain_ref[(g * group_size + h) * HEAD_SIZE : (g * group_size + h + 1) * HEAD_SIZE][None, :],
                    (token_rows, HEAD_SIZE),
                )
                for h in range(group_size)
            ],
            axis=0,
        )
        lh = jnp.where(
            causal,
            lax.dot_general(qs, kg, (((1,), (1,)), ((), ())), preferred_element_type=jnp.float32),
            0.0,
        ).astype(jnp.bfloat16)
        lin = jnp.dot(lh, sg, preferred_element_type=jnp.float32) + jnp.dot(
            qs, pg, preferred_element_type=jnp.float32
        )
        inverse_root = 1.0 / jnp.sqrt(jnp.mean(lin * lin, axis=-1, keepdims=True) + epsilon)
        normed = lin * inverse_root
        gn = gs * normed
        weighted = cs * normed
        scaled = cs * gs
        dl = ((scaled - normed * jnp.mean(scaled * normed, axis=-1, keepdims=True)) * inverse_root).astype(
            jnp.bfloat16
        )
        riding_ref[g * HEAD_SIZE : (g + 1) * HEAD_SIZE, :] = lax.dot_general(
            qs, dl, (((0,), (0,)), ((), ())), preferred_element_type=jnp.float32
        ).astype(riding_ref.dtype)
        bh = jnp.where(
            causal,
            lax.dot_general(dl, sg, (((1,), (1,)), ((), ())), preferred_element_type=jnp.float32),
            0.0,
        ).astype(jnp.bfloat16)
        ldq = lax.dot_general(dl, pg, (((1,), (1,)), ((), ())), preferred_element_type=jnp.float32)
        ldq = ldq + jnp.dot(bh, kg, preferred_element_type=jnp.float32)
        for h in range(group_size):
            cols = slice((g * group_size + h) * HEAD_SIZE, (g * group_size + h + 1) * HEAD_SIZE)
            rows = slice(h * token_rows, (h + 1) * token_rows)
            mixed_ref[:, cols] = (gn[rows] + wout_ref[:, cols]).astype(mixed_ref.dtype)
            gain_rows.append(jnp.sum(weighted[rows], axis=0, keepdims=True))
            dq_ref[:, cols] = (ldq[rows] + wdq_ref[:, cols]).astype(dq_ref.dtype)
        ldk_ref[:, lanes] = lax.dot_general(bh, qs, (((0,), (0,)), ((), ())), preferred_element_type=jnp.float32)
        dsp_ref[:, lanes] = lax.dot_general(lh, dl, (((0,), (0,)), ((), ())), preferred_element_type=jnp.float32)
    state_rows = KEY_VALUE_HEADS * HEAD_SIZE
    spare = riding_ref.shape[0] - state_rows - len(gain_rows)
    riding_ref[state_rows:, :] = jnp.concatenate(
        gain_rows + [jnp.zeros((spare, HEAD_SIZE), jnp.float32)], axis=0
    ).astype(riding_ref.dtype)


def in_vmem(count):
    return [pl.BlockSpec(memory_space=pltpu.VMEM)] * count


def per_device(queries, keys, values, spikes, window_lengths, gain, cotangent):
    token_rows = queries.shape[1]
    width = QUERY_HEADS * HEAD_SIZE
    reach = (WINDOW_REACH + token_rows - 2) // token_rows
    padding_rows = reach * token_rows
    window_rows = (reach + 1) * token_rows
    key_value_width = KEY_VALUE_HEADS * HEAD_SIZE
    q = queries[0]
    c = cotangent[0]
    k = keys[0]
    v = values[0]
    counts = jnp.repeat(spikes[0].astype(jnp.float32), HEAD_SIZE, axis=1)
    spiked = (v.astype(jnp.float32) * counts).astype(jnp.bfloat16)
    def state_of(block_keys, block_spiked):
        return jnp.stack(
            [
                lax.dot_general(
                    block_keys[:, g * HEAD_SIZE : (g + 1) * HEAD_SIZE],
                    block_spiked[:, g * HEAD_SIZE : (g + 1) * HEAD_SIZE],
                    (((0,), (0,)), ((), ())),
                    preferred_element_type=jnp.float32,
                )
                for g in range(KEY_VALUE_HEADS)
            ]
        )

    count_lanes = HEAD_SIZE
    spike_block = jnp.concatenate(
        [
            spikes[0].astype(jnp.bfloat16),
            jnp.zeros((token_rows, count_lanes - KEY_VALUE_HEADS), jnp.bfloat16),
        ],
        axis=1,
    )
    packed = jnp.concatenate([k, v, spike_block], axis=1)
    earlier = []
    for distance in range(reach, 0, -1):
        earlier.append(shifted(packed, "ctx", distance))
    near = jnp.zeros((KEY_VALUE_HEADS, HEAD_SIZE, HEAD_SIZE), jnp.float32)
    for piece in earlier:
        piece_counts = jnp.repeat(
            piece[:, 2 * key_value_width : 2 * key_value_width + KEY_VALUE_HEADS].astype(jnp.float32),
            HEAD_SIZE,
            axis=1,
        )
        piece_spiked = (
            piece[:, key_value_width : 2 * key_value_width].astype(jnp.float32) * piece_counts
        ).astype(jnp.bfloat16)
        near = near + state_of(piece[:, :key_value_width], piece_spiked)
    own_and_near = near + state_of(k, spiked)
    prior_terms = spread_scan(near, own_and_near, "ctx")
    window_packed = jnp.concatenate(
        [piece[:, : 2 * key_value_width] for piece in earlier] + [jnp.concatenate([k, v], axis=1)], axis=0
    )
    wout, wdq, halo_out, own_grad = pl.pallas_call(
        window_kernel,
        out_shape=(
            jax.ShapeDtypeStruct((token_rows, width), jnp.float32),
            jax.ShapeDtypeStruct((token_rows, width), jnp.float32),
            jax.ShapeDtypeStruct((reach, token_rows, 2 * key_value_width), jnp.bfloat16),
            jax.ShapeDtypeStruct((token_rows, 2 * key_value_width), jnp.float32),
        ),
        in_specs=[pl.BlockSpec(memory_space=pltpu.SMEM)] + in_vmem(4),
        out_specs=tuple(in_vmem(4)),
        cost_estimate=pl.CostEstimate(
            flops=12 * QUERY_HEADS * token_rows * window_rows * HEAD_SIZE,
            transcendentals=QUERY_HEADS * token_rows * window_rows,
            bytes_accessed=2 * token_rows * width * (2 + 4) + 2 * window_rows * key_value_width * (2 + 4),
        ),
    )(window_lengths, q, c, window_packed[:, :key_value_width], window_packed[:, key_value_width:])
    state_rows = KEY_VALUE_HEADS * HEAD_SIZE
    gain_rows = width // HEAD_SIZE
    riding_rows = state_rows + gain_rows + (-(state_rows + gain_rows)) % 16
    mixed, d_queries, riding, ldk, dsp = pl.pallas_call(
        functools.partial(linear_kernel, len(prior_terms)),
        out_shape=(
            jax.ShapeDtypeStruct((token_rows, width), jnp.bfloat16),
            jax.ShapeDtypeStruct((token_rows, width), jnp.bfloat16),
            jax.ShapeDtypeStruct((riding_rows, HEAD_SIZE), jnp.bfloat16),
            jax.ShapeDtypeStruct((token_rows, key_value_width), jnp.float32),
            jax.ShapeDtypeStruct((token_rows, key_value_width), jnp.float32),
        ),
        in_specs=in_vmem(7 + len(prior_terms)),
        out_specs=tuple(in_vmem(5)),
        cost_estimate=pl.CostEstimate(
            flops=20 * QUERY_HEADS * token_rows * token_rows * HEAD_SIZE,
            transcendentals=QUERY_HEADS * token_rows,
            bytes_accessed=token_rows * width * (2 + 2 + 4 + 4 + 2 + 2) + 6 * token_rows * key_value_width * 4,
        ),
    )(q, c, k, spiked, *prior_terms, gain, wout, wdq)
    total_tokens = queries.shape[0] * lax.axis_size("dp") * token_rows * lax.axis_size("ctx")
    later_rows, total_rows = butterfly_scan(riding, "ctx", True)
    later_half = later_rows[:state_rows].reshape(KEY_VALUE_HEADS, HEAD_SIZE, HEAD_SIZE).astype(jnp.bfloat16)
    gain_ctx = total_rows[state_rows : state_rows + gain_rows].reshape(width)
    d_gain = all_sum(gain_ctx, ("dp",)) * (total_tokens ** (-0.5))
    ldk_parts = []
    dsp_parts = []
    for g in range(KEY_VALUE_HEADS):
        lanes = slice(g * HEAD_SIZE, (g + 1) * HEAD_SIZE)
        ldk_parts.append(
            ldk[:, lanes]
            + lax.dot_general(
                spiked[:, lanes], later_half[g], (((1,), (1,)), ((), ())), preferred_element_type=jnp.float32
            )
        )
        dsp_parts.append(
            dsp[:, lanes] + jnp.dot(k[:, lanes], later_half[g], preferred_element_type=jnp.float32)
        )
    linear_key_gradient = jnp.concatenate(ldk_parts, axis=1)
    linear_value_gradient = jnp.concatenate(dsp_parts, axis=1) * counts
    received = own_grad
    for distance in range(1, reach + 1):
        received = received + shifted(halo_out[distance - 1], "ctx", -distance).astype(jnp.float32)
    keys_gradient = (
        linear_key_gradient + received[:, :key_value_width]
    ).astype(jnp.bfloat16)
    values_gradient = (
        linear_value_gradient + received[:, key_value_width:]
    ).astype(jnp.bfloat16)
    return (
        mixed[None],
        d_queries[None],
        keys_gradient[None],
        values_gradient[None],
        d_gain,
    )


def solution(mesh):
    placed = (
        P("dp", "ctx", None),
        P("dp", "ctx", None),
        P("dp", "ctx", None),
        P("dp", "ctx", None),
        P(),
        P(),
        P("dp", "ctx", None),
    )
    return jax.shard_map(
        per_device,
        mesh=mesh,
        in_specs=placed,
        out_specs=(
            P("dp", "ctx", None),
            P("dp", "ctx", None),
            P("dp", "ctx", None),
            P("dp", "ctx", None),
            P(),
        ),
        check_vma=False,
    )
```

```python
import jax
import jax.numpy as jnp
from jax import lax
from jax.experimental import pallas as pl
from jax.experimental.pallas import tpu as pltpu
from jax.sharding import PartitionSpec as P

QUERY_HEADS = 14
KEY_VALUE_HEADS = 2
HEAD_SIZE = 128
WINDOW_REACH = 256


epsilon = 1e-05


def exclusive_scan(part, axis, reverse):
    count = lax.axis_size(axis)
    running = part
    total = None
    distance = 1
    while distance < count:
        if reverse:
            route = [(i + distance, i) for i in range(count - distance)]
        else:
            route = [(i, i + distance) for i in range(count - distance)]
        got = lax.ppermute(running, axis, route)
        total = got if total is None else total + got
        if distance * 2 < count:
            running = running + got
        distance *= 2
    if total is None:
        total = jnp.zeros_like(part)
    return total


def butterfly_scan(part, axis, reverse):
    count = lax.axis_size(axis)
    place = lax.axis_index(axis)
    group = part
    before = jnp.zeros(part.shape, jnp.float32)
    step = 1
    while step < count:
        mine = group.astype(jnp.bfloat16)
        got = lax.ppermute(mine, axis, [(i, i ^ step) for i in range(count)]).astype(jnp.float32)
        partner = jnp.bitwise_xor(place, step)
        take = partner > place if reverse else partner < place
        before = before + jnp.where(take, got, 0.0)
        group = mine.astype(jnp.float32) + got
        step *= 2
    return before, group


def spread_scan(near, own, axis):
    count = lax.axis_size(axis)
    total = near
    running = own
    stride = 3
    while stride < count:
        parts = []
        for distance in (stride, 2 * stride):
            if distance < count:
                parts.append(shifted(running, axis, distance))
        for got in parts:
            total = total + got
        if 3 * stride < count:
            for got in parts:
                running = running + got
        stride *= 3
    return total


def all_sum(part, axes):
    count = 1
    for axis in axes:
        count *= lax.axis_size(axis)
    step = 1
    while step < count:
        route = [(i, i ^ step) for i in range(count)]
        part = part + lax.ppermute(part, axes, route)
        step *= 2
    return part


def shifted(block, axis, distance):
    devices = range(lax.axis_size(axis))
    route = [(i - distance, i) for i in devices if i - distance in devices]
    return lax.ppermute(block, axis, route)


def stacked_heads(ref, group, group_size):
    return jnp.concatenate(
        [ref[:, (group * group_size + h) * HEAD_SIZE : (group * group_size + h + 1) * HEAD_SIZE] for h in range(group_size)],
        axis=0,
    )


def window_kernel(info_ref, q_ref, c_ref, k_ref, v_ref, wout_ref, wdq_ref, halo_ref, own_ref):
    group_size = QUERY_HEADS // KEY_VALUE_HEADS
    token_rows = q_ref.shape[0]
    window_rows = k_ref.shape[0]
    padding_rows = window_rows - token_rows
    scale = HEAD_SIZE ** (-0.5)
    stacked_rows = group_size * token_rows
    row = lax.broadcasted_iota(jnp.int32, (stacked_rows, window_rows), 0) % token_rows
    col = lax.broadcasted_iota(jnp.int32, (stacked_rows, window_rows), 1)
    back = row + padding_rows - col
    base = lax.axis_index("ctx") * token_rows - padding_rows
    seen = (back >= 0) & (col + base >= 0)
    for g in range(KEY_VALUE_HEADS):
        visible = seen & (back < info_ref[g])
        lanes = slice(g * HEAD_SIZE, (g + 1) * HEAD_SIZE)
        kg = k_ref[:, lanes]
        vg = v_ref[:, lanes]
        qs = stacked_heads(q_ref, g, group_size)
        cs = stacked_heads(c_ref, g, group_size)
        s = lax.dot_general(qs, kg, (((1,), (1,)), ((), ())), preferred_element_type=jnp.float32) * scale
        s = jnp.where(visible, s, -1e30)
        top = jnp.max(s, axis=-1, keepdims=True)
        e = jnp.exp(s - top)
        p = e * (1.0 / jnp.sum(e, axis=-1, keepdims=True))
        ph = p.astype(jnp.bfloat16)
        wout = jnp.dot(ph, vg, preferred_element_type=jnp.float32)
        gp = lax.dot_general(cs, vg, (((1,), (1,)), ((), ())), preferred_element_type=jnp.float32)
        delta = jnp.sum(cs.astype(jnp.float32) * wout, axis=-1, keepdims=True)
        ds = (p * (gp - delta) * scale).astype(jnp.bfloat16)
        wdq = jnp.dot(ds, kg, preferred_element_type=jnp.float32)
        for h in range(group_size):
            cols = slice((g * group_size + h) * HEAD_SIZE, (g * group_size + h + 1) * HEAD_SIZE)
            rows = slice(h * token_rows, (h + 1) * token_rows)
            wout_ref[:, cols] = wout[rows]
            wdq_ref[:, cols] = wdq[rows]
        dk = lax.dot_general(ds, qs, (((0,), (0,)), ((), ())), preferred_element_type=jnp.float32)
        dv = lax.dot_general(ph, cs, (((0,), (0,)), ((), ())), preferred_element_type=jnp.float32)
        value_lanes = slice(KEY_VALUE_HEADS * HEAD_SIZE + g * HEAD_SIZE, KEY_VALUE_HEADS * HEAD_SIZE + (g + 1) * HEAD_SIZE)
        reach = padding_rows // token_rows
        for distance in range(1, reach + 1):
            start_row = (reach - distance) * token_rows
            halo_ref[distance - 1, :, lanes] = dk[start_row : start_row + token_rows].astype(halo_ref.dtype)
            halo_ref[distance - 1, :, value_lanes] = dv[start_row : start_row + token_rows].astype(halo_ref.dtype)
        own_ref[:, lanes] = dk[padding_rows:]
        own_ref[:, value_lanes] = dv[padding_rows:]


def linear_kernel(q_ref, c_ref, k_ref, s_ref, prior_ref, gain_ref, wout_ref, wdq_ref,
                  mixed_ref, dq_ref, riding_ref, ldk_ref, dsp_ref):
    group_size = QUERY_HEADS // KEY_VALUE_HEADS
    token_rows = q_ref.shape[0]
    stacked_rows = group_size * token_rows
    row = lax.broadcasted_iota(jnp.int32, (stacked_rows, token_rows), 0) % token_rows
    col = lax.broadcasted_iota(jnp.int32, (stacked_rows, token_rows), 1)
    causal = row >= col
    gain_rows = []
    for g in range(KEY_VALUE_HEADS):
        lanes = slice(g * HEAD_SIZE, (g + 1) * HEAD_SIZE)
        kg = k_ref[:, lanes]
        sg = s_ref[:, lanes]
        pg = prior_ref[g]
        qs = stacked_heads(q_ref, g, group_size)
        cs = stacked_heads(c_ref, g, group_size).astype(jnp.float32)
        gs = jnp.concatenate(
            [
                jnp.broadcast_to(
                    gain_ref[(g * group_size + h) * HEAD_SIZE : (g * group_size + h + 1) * HEAD_SIZE][None, :],
                    (token_rows, HEAD_SIZE),
                )
                for h in range(group_size)
            ],
            axis=0,
        )
        lh = jnp.where(
            causal,
            lax.dot_general(qs, kg, (((1,), (1,)), ((), ())), preferred_element_type=jnp.float32),
            0.0,
        ).astype(jnp.bfloat16)
        lin = jnp.dot(lh, sg, preferred_element_type=jnp.float32) + jnp.dot(
            qs, pg, preferred_element_type=jnp.float32
        )
        inverse_root = 1.0 / jnp.sqrt(jnp.mean(lin * lin, axis=-1, keepdims=True) + epsilon)
        normed = lin * inverse_root
        gn = gs * normed
        weighted = cs * normed
        scaled = cs * gs
        dl = ((scaled - normed * jnp.mean(scaled * normed, axis=-1, keepdims=True)) * inverse_root).astype(
            jnp.bfloat16
        )
        riding_ref[g * HEAD_SIZE : (g + 1) * HEAD_SIZE, :] = lax.dot_general(
            qs, dl, (((0,), (0,)), ((), ())), preferred_element_type=jnp.float32
        ).astype(riding_ref.dtype)
        bh = jnp.where(
            causal,
            lax.dot_general(dl, sg, (((1,), (1,)), ((), ())), preferred_element_type=jnp.float32),
            0.0,
        ).astype(jnp.bfloat16)
        ldq = lax.dot_general(dl, pg, (((1,), (1,)), ((), ())), preferred_element_type=jnp.float32)
        ldq = ldq + jnp.dot(bh, kg, preferred_element_type=jnp.float32)
        for h in range(group_size):
            cols = slice((g * group_size + h) * HEAD_SIZE, (g * group_size + h + 1) * HEAD_SIZE)
            rows = slice(h * token_rows, (h + 1) * token_rows)
            mixed_ref[:, cols] = (gn[rows] + wout_ref[:, cols]).astype(mixed_ref.dtype)
            gain_rows.append(jnp.sum(weighted[rows], axis=0, keepdims=True))
            dq_ref[:, cols] = (ldq[rows] + wdq_ref[:, cols]).astype(dq_ref.dtype)
        ldk_ref[:, lanes] = lax.dot_general(bh, qs, (((0,), (0,)), ((), ())), preferred_element_type=jnp.float32)
        dsp_ref[:, lanes] = lax.dot_general(lh, dl, (((0,), (0,)), ((), ())), preferred_element_type=jnp.float32)
    state_rows = KEY_VALUE_HEADS * HEAD_SIZE
    spare = riding_ref.shape[0] - state_rows - len(gain_rows)
    riding_ref[state_rows:, :] = jnp.concatenate(
        gain_rows + [jnp.zeros((spare, HEAD_SIZE), jnp.float32)], axis=0
    ).astype(riding_ref.dtype)


def in_vmem(count):
    return [pl.BlockSpec(memory_space=pltpu.VMEM)] * count


def per_device(queries, keys, values, spikes, window_lengths, gain, cotangent):
    token_rows = queries.shape[1]
    width = QUERY_HEADS * HEAD_SIZE
    reach = (WINDOW_REACH + token_rows - 2) // token_rows
    padding_rows = reach * token_rows
    window_rows = (reach + 1) * token_rows
    key_value_width = KEY_VALUE_HEADS * HEAD_SIZE
    q = queries[0]
    c = cotangent[0]
    k = keys[0]
    v = values[0]
    counts = jnp.repeat(spikes[0].astype(jnp.float32), HEAD_SIZE, axis=1)
    spiked = (v.astype(jnp.float32) * counts).astype(jnp.bfloat16)
    def state_of(block_keys, block_spiked):
        return jnp.stack(
            [
                lax.dot_general(
                    block_keys[:, g * HEAD_SIZE : (g + 1) * HEAD_SIZE],
                    block_spiked[:, g * HEAD_SIZE : (g + 1) * HEAD_SIZE],
                    (((0,), (0,)), ((), ())),
                    preferred_element_type=jnp.float32,
                )
                for g in range(KEY_VALUE_HEADS)
            ]
        )

    count_lanes = HEAD_SIZE
    spike_block = jnp.concatenate(
        [
            spikes[0].astype(jnp.bfloat16),
            jnp.zeros((token_rows, count_lanes - KEY_VALUE_HEADS), jnp.bfloat16),
        ],
        axis=1,
    )
    packed = jnp.concatenate([k, v, spike_block], axis=1)
    earlier = []
    for distance in range(reach, 0, -1):
        earlier.append(shifted(packed, "ctx", distance))
    near = jnp.zeros((KEY_VALUE_HEADS, HEAD_SIZE, HEAD_SIZE), jnp.float32)
    for piece in earlier:
        piece_counts = jnp.repeat(
            piece[:, 2 * key_value_width : 2 * key_value_width + KEY_VALUE_HEADS].astype(jnp.float32),
            HEAD_SIZE,
            axis=1,
        )
        piece_spiked = (
            piece[:, key_value_width : 2 * key_value_width].astype(jnp.float32) * piece_counts
        ).astype(jnp.bfloat16)
        near = near + state_of(piece[:, :key_value_width], piece_spiked)
    own_and_near = near + state_of(k, spiked)
    window_packed = jnp.concatenate(
        [piece[:, : 2 * key_value_width] for piece in earlier] + [jnp.concatenate([k, v], axis=1)], axis=0
    )
    wout, wdq, halo_out, own_grad = pl.pallas_call(
        window_kernel,
        out_shape=(
            jax.ShapeDtypeStruct((token_rows, width), jnp.float32),
            jax.ShapeDtypeStruct((token_rows, width), jnp.float32),
            jax.ShapeDtypeStruct((reach, token_rows, 2 * key_value_width), jnp.bfloat16),
            jax.ShapeDtypeStruct((token_rows, 2 * key_value_width), jnp.float32),
        ),
        in_specs=[pl.BlockSpec(memory_space=pltpu.SMEM)] + in_vmem(4),
        out_specs=tuple(in_vmem(4)),
        cost_estimate=pl.CostEstimate(
            flops=12 * QUERY_HEADS * token_rows * window_rows * HEAD_SIZE,
            transcendentals=QUERY_HEADS * token_rows * window_rows,
            bytes_accessed=2 * token_rows * width * (2 + 4) + 2 * window_rows * key_value_width * (2 + 4),
        ),
    )(window_lengths, q, c, window_packed[:, :key_value_width], window_packed[:, key_value_width:])
    near, own_and_near, _ = lax.optimization_barrier((near, own_and_near, wdq))
    prior_half = spread_scan(near, own_and_near, "ctx").astype(jnp.bfloat16)
    state_rows = KEY_VALUE_HEADS * HEAD_SIZE
    gain_rows = width // HEAD_SIZE
    riding_rows = state_rows + gain_rows + (-(state_rows + gain_rows)) % 16
    mixed, d_queries, riding, ldk, dsp = pl.pallas_call(
        linear_kernel,
        out_shape=(
            jax.ShapeDtypeStruct((token_rows, width), jnp.bfloat16),
            jax.ShapeDtypeStruct((token_rows, width), jnp.bfloat16),
            jax.ShapeDtypeStruct((riding_rows, HEAD_SIZE), jnp.bfloat16),
            jax.ShapeDtypeStruct((token_rows, key_value_width), jnp.float32),
            jax.ShapeDtypeStruct((token_rows, key_value_width), jnp.float32),
        ),
        in_specs=in_vmem(8),
        out_specs=tuple(in_vmem(5)),
        cost_estimate=pl.CostEstimate(
            flops=20 * QUERY_HEADS * token_rows * token_rows * HEAD_SIZE,
            transcendentals=QUERY_HEADS * token_rows,
            bytes_accessed=token_rows * width * (2 + 2 + 4 + 4 + 2 + 2) + 6 * token_rows * key_value_width * 4,
        ),
    )(q, c, k, spiked, prior_half, gain, wout, wdq)
    total_tokens = queries.shape[0] * lax.axis_size("dp") * token_rows * lax.axis_size("ctx")
    later_rows, total_rows = butterfly_scan(riding, "ctx", True)
    later_half = later_rows[:state_rows].reshape(KEY_VALUE_HEADS, HEAD_SIZE, HEAD_SIZE).astype(jnp.bfloat16)
    gain_ctx = total_rows[state_rows : state_rows + gain_rows].reshape(width)
    d_gain = all_sum(gain_ctx, ("dp",)) * (total_tokens ** (-0.5))
    ldk_parts = []
    dsp_parts = []
    for g in range(KEY_VALUE_HEADS):
        lanes = slice(g * HEAD_SIZE, (g + 1) * HEAD_SIZE)
        ldk_parts.append(
            ldk[:, lanes]
            + lax.dot_general(
                spiked[:, lanes], later_half[g], (((1,), (1,)), ((), ())), preferred_element_type=jnp.float32
            )
        )
        dsp_parts.append(
            dsp[:, lanes] + jnp.dot(k[:, lanes], later_half[g], preferred_element_type=jnp.float32)
        )
    linear_key_gradient = jnp.concatenate(ldk_parts, axis=1)
    linear_value_gradient = jnp.concatenate(dsp_parts, axis=1) * counts
    received = own_grad
    for distance in range(1, reach + 1):
        received = received + shifted(halo_out[distance - 1], "ctx", -distance).astype(jnp.float32)
    keys_gradient = (
        linear_key_gradient + received[:, :key_value_width]
    ).astype(jnp.bfloat16)
    values_gradient = (
        linear_value_gradient + received[:, key_value_width:]
    ).astype(jnp.bfloat16)
    return (
        mixed[None],
        d_queries[None],
        keys_gradient[None],
        values_gradient[None],
        d_gain,
    )


def solution(mesh):
    placed = (
        P("dp", "ctx", None),
        P("dp", "ctx", None),
        P("dp", "ctx", None),
        P("dp", "ctx", None),
        P(),
        P(),
        P("dp", "ctx", None),
    )
    return jax.shard_map(
        per_device,
        mesh=mesh,
        in_specs=placed,
        out_specs=(
            P("dp", "ctx", None),
            P("dp", "ctx", None),
            P("dp", "ctx", None),
            P("dp", "ctx", None),
            P(),
        ),
        check_vma=False,
    )
```
